32 devices in a mesh: ctx: 16 (over z, y, core), head: 2 (over x).
Axes of the slice: x: 2, y: 2, z: 4, core: 2. Of those that a mesh axis runs over, the one named last changes fastest.
Arguments:
- queries: bfloat16 [8192, 32, 128], P('ctx', 'head'), may hold values from -6 to 6
- keys: bfloat16 [8192, 32, 128], P('ctx', 'head'), may hold values from -6 to 6
- values: bfloat16 [8192, 32, 128], P('ctx', 'head'), may hold values from -6 to 6
- far_blocks: int32 [128, 5], replicated, may hold values from 0 to 127, as said below
- out_weight: bfloat16 [4096, 4096], P('head'), may hold values from -0.125 to 0.125
Outputs:
- mixed: bfloat16 [8192, 4096], P('ctx', 'head')
The draws below stay inside these ranges and needn't reach their ends.
Inputs may be any that keep to these rules, and one draw needn't show every extreme that they name: `far_blocks`: entry j (from 0) of query block q either equals q, or names a block of the group of 8 consecutive blocks that lies 2**j groups before the group of q (groups begin at multiples of 8); it names such a block only when q % 8 is a multiple of 2**j.
All inputs are finite; a program needn't handle non-finite values.
Results may differ from the reference program's by a relative error of at most 0.006.
Values may be sent and summed in bfloat16 or wider, within the bound.
No kernel may reach another device: no remote copies, remote signals or barrier semaphores. Data moves between devices by JAX's collectives and lax.ppermute only.
A program may use at most 192 MiB of HBM per device.

```python
import math
import jax
import jax.numpy as jnp
from jax import lax

D = 4096
HEADS = 32
HD = 128
BLOCK = 64
WINDOW = 512
NOFF = 5
SEQ = 8192
BPD = 8
QBLOCKS = 128
WB = 8
N_HEAD = 2


def joint_fields(key):
    key_q = jax.random.fold_in(key, 101)
    key_k = jax.random.fold_in(key, 202)
    shape = (SEQ, HEADS, HD)
    queries = 1.5 * jax.random.truncated_normal(key_q, -4.0, 4.0, shape, jnp.float32)
    keys = 1.5 * jax.random.truncated_normal(key_k, -4.0, 4.0, shape, jnp.float32)
    return (queries, keys)


def draw_queries(key, part):
    return joint_fields(key)[0].astype(jnp.bfloat16)


def draw_keys(key, part):
    return joint_fields(key)[1].astype(jnp.bfloat16)


def draw_far_blocks(key, part):
    qblock = jnp.arange(QBLOCKS, dtype=jnp.int32)
    group = qblock // BPD
    inner = qblock % BPD
    offsets = 2 ** jnp.arange(NOFF, dtype=jnp.int32)
    source = group[:, None] - offsets[None, :]
    named = (inner[:, None] % offsets[None, :] == 0) & (source >= 0)
    picks = jax.random.randint(key, (QBLOCKS, NOFF), 0, BPD, dtype=jnp.int32)
    return jnp.where(named, source * BPD + picks, qblock[:, None]).astype(jnp.int32)


def spiked(values, rng, source, target, parts, factor):
    owner, partner = [(jnp.arange(values.shape[dim]) // (values.shape[dim] // parts)).reshape([-1 if axis == dim else 1 for axis in range(values.ndim)]) for dim in (source, target)]
    chosen = jax.random.permutation(rng, parts)[partner]
    strong = (owner == chosen) | (owner == (partner + parts // 2) % parts)
    return jnp.where(strong, factor * values, values)


def block_scale(stream_key, shape, pieces, smallest, high):
    gain, own = 1.0, jax.random.fold_in(stream_key, 6)
    for dim, blocks in pieces:
        steps = jnp.exp(jax.random.uniform(jax.random.fold_in(own, dim), (blocks,), jnp.float32, smallest / len(pieces), high / len(pieces)))
        gain = gain * jnp.repeat(steps, shape[dim] // blocks).reshape([-1 if axis == dim else 1 for axis in range(len(shape))])
    return gain


def normal_values(own_key, extent, scale, bound, split=(), kind=jnp.bfloat16):
    values = jax.random.normal(own_key, extent, jnp.float32) * scale
    if len(split) > 0:
        values = block_scale(own_key, extent, split, -0.22, 0.18) * values
    return jnp.clip(values, min=-bound, max=bound).astype(kind)


def gaussian_with(rng, shape, scale, reach, cuts, heavy, held_as=jnp.bfloat16):
    values = scale * jax.random.normal(rng, shape, jnp.float32)
    if cuts:
        values = values * block_scale(rng, shape, cuts, -0.22, 0.18)
    return jnp.clip(spiked(values, jax.random.fold_in(rng, 3), *heavy), -reach, reach).astype(held_as)


def setup_inputs(seed: int = 0) -> dict:
    seeds = jax.random.split(jax.random.key(seed), 6)
    return {
        "queries": draw_queries(jax.random.fold_in(seeds[5], 71), 0),
        "keys": draw_keys(jax.random.fold_in(seeds[5], 71), 0),
        "values": normal_values(seeds[2], (SEQ, HEADS, HD), 1.0, 6.0, ((0, 16), (1, 2))),
        "far_blocks": draw_far_blocks(jax.random.fold_in(seeds[5], 71), 0),
        "out_weight": gaussian_with(seeds[4], (HEADS * HD, D), (HEADS * HD) ** -0.5, 0.125, ((0, 2),), (0, 1, 2, 2.0)),
    }


def reference(queries, keys, values, far_blocks, out_weight):
    scale = 1.0 / math.sqrt(HD)
    pad_k = jnp.pad(keys, ((WINDOW, 0), (0, 0), (0, 0)))
    pad_v = jnp.pad(values, ((WINDOW, 0), (0, 0), (0, 0)))
    key_blocks = keys.reshape(QBLOCKS, BLOCK, HEADS, HD)
    value_blocks = values.reshape(QBLOCKS, BLOCK, HEADS, HD)

    def one_block(qblock):
        base = (qblock * BLOCK).astype(jnp.int32)
        q_rows = lax.dynamic_slice_in_dim(queries, base, BLOCK, 0).astype(jnp.float32)
        k_win = lax.dynamic_slice_in_dim(pad_k, base, WINDOW + BLOCK, 0).astype(jnp.float32)
        v_win = lax.dynamic_slice_in_dim(pad_v, base, WINDOW + BLOCK, 0).astype(jnp.float32)
        pos_q = base + jnp.arange(BLOCK, dtype=jnp.int32)
        pos_k = base - WINDOW + jnp.arange(WINDOW + BLOCK, dtype=jnp.int32)
        win_ok = (pos_k[None, :] <= pos_q[:, None]) & (pos_k[None, :] > pos_q[:, None] - WINDOW) & (pos_k[None, :] >= 0)
        entries = lax.dynamic_index_in_dim(far_blocks, qblock, 0, keepdims=False)
        used = entries <= qblock - WB - 1
        k_far = key_blocks[entries].reshape(NOFF * BLOCK, HEADS, HD).astype(jnp.float32)
        v_far = value_blocks[entries].reshape(NOFF * BLOCK, HEADS, HD).astype(jnp.float32)
        far_ok = jnp.repeat(used, BLOCK)
        s_win = jnp.einsum('thd,uhd->htu', q_rows, k_win) * scale
        s_win = jnp.where(win_ok[None], s_win, -jnp.inf)
        s_far = jnp.einsum('thd,uhd->htu', q_rows, k_far) * scale
        s_far = jnp.where(far_ok[None, None, :], s_far, -jnp.inf)
        top = jnp.maximum(lax.optimization_barrier(jnp.max(s_win, axis=-1)), lax.optimization_barrier(jnp.max(s_far, axis=-1)))
        p_win = jnp.exp(s_win - top[..., None])
        p_far = jnp.exp(s_far - top[..., None])
        total = lax.optimization_barrier(jnp.sum(p_win, axis=-1)) + lax.optimization_barrier(jnp.sum(p_far, axis=-1))
        r_win = lax.optimization_barrier(p_win.astype(jnp.bfloat16)).astype(jnp.float32)
        r_far = lax.optimization_barrier(p_far.astype(jnp.bfloat16)).astype(jnp.float32)
        summed = jnp.einsum('htu,uhd->thd', r_win, v_win) + jnp.einsum('htu,uhd->thd', r_far, v_far)
        return (summed / jnp.transpose(total)[:, :, None]).astype(jnp.bfloat16)
    attended = lax.map(one_block, jnp.arange(QBLOCKS, dtype=jnp.int32))
    attended = attended.reshape(SEQ, HEADS * HD)
    group = HEADS // N_HEAD * HD
    mixed = jnp.zeros((SEQ, D), jnp.float32)
    for index in range(N_HEAD):
        partial_value = jnp.dot(attended[:, index * group:(index + 1) * group], out_weight[index * group:(index + 1) * group], preferred_element_type=jnp.float32)
        partial_value = lax.optimization_barrier(partial_value.astype(jnp.bfloat16))
        mixed = mixed + partial_value.astype(jnp.float32)
    return mixed.astype(jnp.bfloat16)
```

```python
import functools
import math

import jax
import jax.numpy as jnp
from jax import lax
from jax.experimental import pallas as pl
from jax.experimental.pallas import tpu as pltpu
from jax.sharding import PartitionSpec as P

BLOCK = 64
WINDOW = 512
NOFF = 5
HEADS_PER_STEP = 2


def from_behind(value, axis, steps):
    count = lax.axis_size(axis)
    initial, last = (max(0, -steps), min(count, count - steps))
    return lax.ppermute(value, axis, [(source, source + steps) for source in range(initial, last)])


def attention_kernel(levels, per_dev, width, scale, meta_ref, used_ref, q_ref, kp_ref, vp_ref,
                     ko_ref, vo_ref, *rest):
    far_refs = rest[:-1]
    o_ref = rest[-1]
    prev_ok = meta_ref[0] > 0
    neg = jnp.float32(-jnp.inf)
    for hh in range(HEADS_PER_STEP):
        cols = pl.ds(hh * width, width)
        for i in range(per_dev):
            lo = i * BLOCK
            q = q_ref[lo:lo + BLOCK, cols]
            pieces = []

            def score(keys):
                return lax.dot_general(
                    q, keys, (((1,), (1,)), ((), ())), preferred_element_type=jnp.float32
                ) * scale

            n_prev = per_dev * BLOCK - lo
            s_p = score(kp_ref[lo:, cols])
            r_ids = lax.broadcasted_iota(jnp.int32, (BLOCK, n_prev), 0)
            c_ids = lax.broadcasted_iota(jnp.int32, (BLOCK, n_prev), 1)
            s_p = jnp.where((c_ids > r_ids) & prev_ok, s_p, neg)
            pieces.append((s_p, vp_ref[lo:, cols]))
            n_own = lo + BLOCK
            s_o = score(ko_ref[:n_own, cols])
            r_ids = lax.broadcasted_iota(jnp.int32, (BLOCK, n_own), 0)
            c_ids = lax.broadcasted_iota(jnp.int32, (BLOCK, n_own), 1)
            s_o = jnp.where(c_ids <= r_ids + lo, s_o, neg)
            pieces.append((s_o, vo_ref[:n_own, cols]))
            start = pl.multiple_of(meta_ref[1 + i] * BLOCK, BLOCK)
            s_f = score(kp_ref[pl.ds(start, BLOCK), cols])
            s_f = jnp.where(used_ref[i * NOFF] > 0, s_f, neg)
            pieces.append((s_f, vp_ref[pl.ds(start, BLOCK), cols]))
            for level, (k_ref, v_ref) in zip(levels, zip(far_refs[0::2], far_refs[1::2])):
                offset = 2**level
                if i % offset:
                    continue
                flo = (i // offset) * BLOCK
                s_f = score(k_ref[flo:flo + BLOCK, cols])
                s_f = jnp.where(used_ref[i * NOFF + level] > 0, s_f, neg)
                pieces.append((s_f, v_ref[flo:flo + BLOCK, cols]))
            top = pieces[0][0].max(axis=1, keepdims=True)
            for s, _ in pieces[1:]:
                top = jnp.maximum(top, s.max(axis=1, keepdims=True))
            total = None
            summed = None
            for s, v in pieces:
                p = jnp.exp(s - top)
                part_total = p.sum(axis=1, keepdims=True)
                part = jnp.dot(p.astype(jnp.bfloat16), v, preferred_element_type=jnp.float32)
                total = part_total if total is None else total + part_total
                summed = part if summed is None else summed + part
            o_ref[lo:lo + BLOCK, cols] = (summed / total).astype(o_ref.dtype)


def per_device(queries, keys, values, far_blocks, out_weight):
    rows, heads, width = queries.shape
    per_dev = rows // BLOCK
    device = lax.axis_index("ctx")
    cycle_size = lax.axis_size("ctx")
    scale = 1.0 / math.sqrt(width)
    prev_k, prev_v = from_behind((keys, values), "ctx", 1)
    key_blocks = keys.reshape(per_dev, BLOCK, heads, width)
    value_blocks = values.reshape(per_dev, BLOCK, heads, width)
    levels = []
    far_arrays = []
    for level in range(1, NOFF):
        offset = 2**level
        if offset >= cycle_size:
            continue
        target = lax.dynamic_slice_in_dim(far_blocks, (device + offset) * per_dev, per_dev, 0)[
            ::offset, level
        ]
        local = jnp.clip(target - device * per_dev, 0, per_dev - 1)
        sent_k, sent_v = from_behind((key_blocks[local], value_blocks[local]), "ctx", offset)
        levels.append(level)
        far_arrays.append(sent_k.reshape(-1, heads * width))
        far_arrays.append(sent_v.reshape(-1, heads * width))

    own = lax.dynamic_slice_in_dim(far_blocks, device * per_dev, per_dev, 0)
    query_index = device * per_dev + jnp.arange(per_dev, dtype=jnp.int32)
    used = (own <= (query_index - WINDOW // BLOCK - 1)[:, None]).astype(jnp.int32).reshape(-1)
    pick = jnp.clip(own[:, 0] - (device - 1) * per_dev, 0, per_dev - 1)
    meta = jnp.concatenate([(device > 0).astype(jnp.int32)[None], pick.astype(jnp.int32)])

    flat = lambda a: a.reshape(rows, heads * width)
    cw = HEADS_PER_STEP * width
    row_spec = pl.BlockSpec((rows, cw), lambda h, *_: (0, h))
    far_specs = [pl.BlockSpec((a.shape[0], cw), lambda h, *_: (0, h)) for a in far_arrays]
    n_keys = WINDOW + BLOCK + NOFF * BLOCK
    cost = pl.CostEstimate(
        flops=4 * rows * heads * width * n_keys,
        transcendentals=rows * heads * n_keys,
        bytes_accessed=2 * heads * width * (6 * rows + sum(a.shape[0] for a in far_arrays)),
    )
    attended = pl.pallas_call(
        functools.partial(attention_kernel, levels, per_dev, width, scale),
        out_shape=jax.ShapeDtypeStruct((rows, heads * width), queries.dtype),
        grid_spec=pltpu.PrefetchScalarGridSpec(
            num_scalar_prefetch=2,
            grid=(heads // HEADS_PER_STEP,),
            in_specs=[row_spec] * 5 + far_specs,
            out_specs=row_spec,
        ),
        compiler_params=pltpu.CompilerParams(dimension_semantics=("arbitrary",)),
        cost_estimate=cost,
    )(meta, used, flat(queries), flat(prev_k), flat(prev_v), flat(keys), flat(values), *far_arrays)

    n_head = lax.axis_size("head")
    if n_head != 2:
        partial_value = jnp.dot(attended, out_weight, preferred_element_type=jnp.float32)
        return lax.psum_scatter(
            partial_value.astype(jnp.bfloat16), "head", scatter_dimension=1, tiled=True
        )
    hidx = lax.axis_index("head")
    split_w = out_weight.reshape(out_weight.shape[0], 2, -1)
    w_other = lax.dynamic_index_in_dim(split_w, 1 - hidx, axis=1, keepdims=False)
    w_own = lax.dynamic_index_in_dim(split_w, hidx, axis=1, keepdims=False)
    p_other = jnp.dot(attended, w_other, preferred_element_type=jnp.float32).astype(jnp.bfloat16)
    received = lax.ppermute(p_other, "head", [(0, 1), (1, 0)])
    p_own = jnp.dot(attended, w_own, preferred_element_type=jnp.float32).astype(jnp.bfloat16)
    return (p_own.astype(jnp.float32) + received.astype(jnp.float32)).astype(jnp.bfloat16)


def solution(mesh):
    placed = (
        P("ctx", "head", None),
        P("ctx", "head", None),
        P("ctx", "head", None),
        P(),
        P("head", None),
    )
    return jax.shard_map(
        per_device, mesh=mesh, in_specs=placed, out_specs=P("ctx", "head"), check_vma=False
    )
```

```python
import functools
import math

import jax
import jax.numpy as jnp
from jax import lax
from jax.experimental import pallas as pl
from jax.experimental.pallas import tpu as pltpu
from jax.sharding import PartitionSpec as P

BLOCK = 64
WINDOW = 512
NOFF = 5
HEADS_PER_STEP = 1


def from_behind(value, axis, steps):
    count = lax.axis_size(axis)
    initial, last = (max(0, -steps), min(count, count - steps))
    return lax.ppermute(value, axis, [(source, source + steps) for source in range(initial, last)])


def attention_kernel(levels, per_dev, width, scale, meta_ref, used_ref, q_ref, kp_ref, vp_ref,
                     ko_ref, vo_ref, *rest):
    far_refs = rest[:-1]
    o_ref = rest[-1]
    prev_ok = meta_ref[0] > 0
    neg = jnp.float32(-jnp.inf)
    if True:
        cols = slice(None)
        for i in range(per_dev):
            lo = i * BLOCK
            q = q_ref[lo:lo + BLOCK, cols]
            pieces = []

            def score(keys):
                return lax.dot_general(
                    q, keys, (((1,), (1,)), ((), ())), preferred_element_type=jnp.float32
                ) * scale

            n_prev = per_dev * BLOCK - lo
            s_p = score(kp_ref[lo:, cols])
            r_ids = lax.broadcasted_iota(jnp.int32, (BLOCK, n_prev), 0)
            c_ids = lax.broadcasted_iota(jnp.int32, (BLOCK, n_prev), 1)
            s_p = jnp.where((c_ids > r_ids) & prev_ok, s_p, neg)
            pieces.append((s_p, vp_ref[lo:, cols]))
            n_own = lo + BLOCK
            s_o = score(ko_ref[:n_own, cols])
            r_ids = lax.broadcasted_iota(jnp.int32, (BLOCK, n_own), 0)
            c_ids = lax.broadcasted_iota(jnp.int32, (BLOCK, n_own), 1)
            s_o = jnp.where(c_ids <= r_ids + lo, s_o, neg)
            pieces.append((s_o, vo_ref[:n_own, cols]))
            start = pl.multiple_of(meta_ref[1 + i] * BLOCK, BLOCK)
            s_f = score(kp_ref[pl.ds(start, BLOCK), cols])
            s_f = jnp.where(used_ref[i * NOFF] > 0, s_f, neg)
            pieces.append((s_f, vp_ref[pl.ds(start, BLOCK), cols]))
            for level, (k_ref, v_ref) in zip(levels, zip(far_refs[0::2], far_refs[1::2])):
                offset = 2**level
                if i % offset:
                    continue
                flo = (i // offset) * BLOCK
                s_f = score(k_ref[flo:flo + BLOCK, cols])
                s_f = jnp.where(used_ref[i * NOFF + level] > 0, s_f, neg)
                pieces.append((s_f, v_ref[flo:flo + BLOCK, cols]))
            top = pieces[0][0].max(axis=1, keepdims=True)
            for s, _ in pieces[1:]:
                top = jnp.maximum(top, s.max(axis=1, keepdims=True))
            total = None
            summed = None
            for s, v in pieces:
                p = jnp.exp(s - top)
                part_total = p.sum(axis=1, keepdims=True)
                part = jnp.dot(p.astype(jnp.bfloat16), v, preferred_element_type=jnp.float32)
                total = part_total if total is None else total + part_total
                summed = part if summed is None else summed + part
            o_ref[lo:lo + BLOCK, cols] = (summed / total).astype(o_ref.dtype)


def matmul_kernel(sel_ref, a_ref, w_ref, o_ref):
    o_ref[...] = jnp.dot(a_ref[...], w_ref[...], preferred_element_type=jnp.float32).astype(
        o_ref.dtype
    )


def project_half(attended, weight, half, tn=512):
    rows, depth = attended.shape
    cw = weight.shape[1] // 2
    steps = cw // tn
    return pl.pallas_call(
        matmul_kernel,
        out_shape=jax.ShapeDtypeStruct((rows, cw), jnp.bfloat16),
        grid_spec=pltpu.PrefetchScalarGridSpec(
            num_scalar_prefetch=1,
            grid=(steps,),
            in_specs=[
                pl.BlockSpec((rows, depth), lambda j, sel: (0, 0)),
                pl.BlockSpec((depth, tn), lambda j, sel: (0, sel[0] * steps + j)),
            ],
            out_specs=pl.BlockSpec((rows, tn), lambda j, sel: (0, j)),
        ),
        compiler_params=pltpu.CompilerParams(dimension_semantics=("arbitrary",)),
        cost_estimate=pl.CostEstimate(
            flops=2 * rows * depth * cw,
            transcendentals=0,
            bytes_accessed=2 * (rows * depth + depth * cw + rows * cw),
        ),
    )(jnp.reshape(half, (1,)).astype(jnp.int32), attended, weight)


def per_device(queries, keys, values, far_blocks, out_weight):
    rows, heads, width = queries.shape
    per_dev = rows // BLOCK
    device = lax.axis_index("ctx")
    cycle_size = lax.axis_size("ctx")
    scale = 1.0 / math.sqrt(width)
    q_t, k_t, v_t = (jnp.transpose(a, (1, 0, 2)) for a in (queries, keys, values))
    prev_k, prev_v = from_behind((k_t, v_t), "ctx", 1)
    levels = []
    far_arrays = []
    for level in range(1, NOFF):
        offset = 2**level
        if offset >= cycle_size:
            continue
        target = lax.dynamic_slice_in_dim(far_blocks, (device + offset) * per_dev, per_dev, 0)[
            ::offset, level
        ]
        local = jnp.clip(target - device * per_dev, 0, per_dev - 1)
        picked = [
            jnp.concatenate(
                [lax.dynamic_slice_in_dim(a, local[b] * BLOCK, BLOCK, axis=1) for b in range(local.shape[0])],
                axis=1,
            )
            for a in (k_t, v_t)
        ]
        sent_k, sent_v = from_behind(tuple(picked), "ctx", offset)
        levels.append(level)
        far_arrays.append(sent_k)
        far_arrays.append(sent_v)

    own = lax.dynamic_slice_in_dim(far_blocks, device * per_dev, per_dev, 0)
    query_index = device * per_dev + jnp.arange(per_dev, dtype=jnp.int32)
    used = (own <= (query_index - WINDOW // BLOCK - 1)[:, None]).astype(jnp.int32).reshape(-1)
    pick = jnp.clip(own[:, 0] - (device - 1) * per_dev, 0, per_dev - 1)
    meta = jnp.concatenate([(device > 0).astype(jnp.int32)[None], pick.astype(jnp.int32)])

    row_spec = pl.BlockSpec((None, rows, width), lambda h, *_: (h, 0, 0))
    out_spec = pl.BlockSpec((rows, width), lambda h, *_: (0, h))
    far_specs = [pl.BlockSpec((None, a.shape[1], width), lambda h, *_: (h, 0, 0)) for a in far_arrays]
    n_keys = WINDOW + BLOCK + NOFF * BLOCK
    cost = pl.CostEstimate(
        flops=4 * rows * heads * width * n_keys,
        transcendentals=rows * heads * n_keys,
        bytes_accessed=2 * heads * width * (6 * rows + sum(a.shape[1] for a in far_arrays)),
    )
    attended = pl.pallas_call(
        functools.partial(attention_kernel, levels, per_dev, width, scale),
        out_shape=jax.ShapeDtypeStruct((rows, heads * width), queries.dtype),
        grid_spec=pltpu.PrefetchScalarGridSpec(
            num_scalar_prefetch=2,
            grid=(heads // HEADS_PER_STEP,),
            in_specs=[row_spec] * 5 + far_specs,
            out_specs=out_spec,
        ),
        compiler_params=pltpu.CompilerParams(dimension_semantics=("arbitrary",)),
        cost_estimate=cost,
    )(meta, used, q_t, prev_k, prev_v, k_t, v_t, *far_arrays)

    n_head = lax.axis_size("head")
    if n_head != 2:
        partial_value = jnp.dot(attended, out_weight, preferred_element_type=jnp.float32)
        return lax.psum_scatter(
            partial_value.astype(jnp.bfloat16), "head", scatter_dimension=1, tiled=True
        )
    hidx = lax.axis_index("head")
    p_other = project_half(attended, out_weight, 1 - hidx)
    received = lax.ppermute(p_other, "head", [(0, 1), (1, 0)])
    p_own = project_half(attended, out_weight, hidx)
    return (p_own.astype(jnp.float32) + received.astype(jnp.float32)).astype(jnp.bfloat16)


def solution(mesh):
    placed = (
        P("ctx", "head", None),
        P("ctx", "head", None),
        P("ctx", "head", None),
        P(),
        P("head", None),
    )
    return jax.shard_map(
        per_device, mesh=mesh, in_specs=placed, out_specs=P("ctx", "head"), check_vma=False
    )
```

```python
import functools
import math

import jax
import jax.numpy as jnp
from jax import lax
from jax.experimental import pallas as pl
from jax.experimental.pallas import tpu as pltpu
from jax.sharding import PartitionSpec as P

BLOCK = 64
WINDOW = 512
NOFF = 5
HEADS_PER_STEP = 1


def from_behind(value, axis, steps):
    count = lax.axis_size(axis)
    initial, last = (max(0, -steps), min(count, count - steps))
    return lax.ppermute(value, axis, [(source, source + steps) for source in range(initial, last)])


def attention_kernel(levels, per_dev, width, scale, meta_ref, used_ref, q_ref, kp_ref, vp_ref,
                     ko_ref, vo_ref, *rest):
    far_refs = rest[:-1]
    o_ref = rest[-1]
    prev_ok = meta_ref[0] > 0
    neg = jnp.float32(-jnp.inf)
    if True:
        cols = slice(None)
        for i in range(per_dev):
            lo = i * BLOCK
            q = q_ref[lo:lo + BLOCK, cols]
            pieces = []

            def score(keys):
                return lax.dot_general(
                    q, keys, (((1,), (1,)), ((), ())), preferred_element_type=jnp.float32
                ) * scale

            n_prev = per_dev * BLOCK - lo
            s_p = score(kp_ref[lo:, cols])
            r_ids = lax.broadcasted_iota(jnp.int32, (BLOCK, n_prev), 0)
            c_ids = lax.broadcasted_iota(jnp.int32, (BLOCK, n_prev), 1)
            s_p = jnp.where((c_ids > r_ids) & prev_ok, s_p, neg)
            pieces.append((s_p, vp_ref[lo:, cols]))
            n_own = lo + BLOCK
            s_o = score(ko_ref[:n_own, cols])
            r_ids = lax.broadcasted_iota(jnp.int32, (BLOCK, n_own), 0)
            c_ids = lax.broadcasted_iota(jnp.int32, (BLOCK, n_own), 1)
            s_o = jnp.where(c_ids <= r_ids + lo, s_o, neg)
            pieces.append((s_o, vo_ref[:n_own, cols]))
            start = pl.multiple_of(meta_ref[1 + i] * BLOCK, BLOCK)
            s_f = score(kp_ref[pl.ds(start, BLOCK), cols])
            s_f = jnp.where(used_ref[i * NOFF] > 0, s_f, neg)
            pieces.append((s_f, vp_ref[pl.ds(start, BLOCK), cols]))
            pos = 0
            for level in levels:
                offset = 2**level
                n_src = 2 if level == 1 else 1
                refs = far_refs[pos:pos + 2 * n_src]
                pos += 2 * n_src
                if i % offset:
                    continue
                flo = (i // offset) * BLOCK
                k_blk = refs[0][flo:flo + BLOCK, cols]
                v_blk = refs[1][flo:flo + BLOCK, cols]
                if n_src == 2:
                    odd = meta_ref[1 + per_dev] > 0
                    k_blk = jnp.where(odd, refs[2][flo:flo + BLOCK, cols], k_blk)
                    v_blk = jnp.where(odd, refs[3][flo:flo + BLOCK, cols], v_blk)
                s_f = score(k_blk)
                s_f = jnp.where(used_ref[i * NOFF + level] > 0, s_f, neg)
                pieces.append((s_f, v_blk))
            top = pieces[0][0].max(axis=1, keepdims=True)
            for s, _ in pieces[1:]:
                top = jnp.maximum(top, s.max(axis=1, keepdims=True))
            total = None
            summed = None
            for s, v in pieces:
                p = jnp.exp(s - top)
                part_total = p.sum(axis=1, keepdims=True)
                part = jnp.dot(p.astype(jnp.bfloat16), v, preferred_element_type=jnp.float32)
                total = part_total if total is None else total + part_total
                summed = part if summed is None else summed + part
            o_ref[lo:lo + BLOCK, cols] = (summed / total).astype(o_ref.dtype)


def matmul_kernel(sel_ref, a_ref, w_ref, o_ref):
    o_ref[...] = jnp.dot(a_ref[...], w_ref[...], preferred_element_type=jnp.float32).astype(
        o_ref.dtype
    )


def project_half(attended, weight, half, tn=512):
    rows, depth = attended.shape
    cw = weight.shape[1] // 2
    steps = cw // tn
    return pl.pallas_call(
        matmul_kernel,
        out_shape=jax.ShapeDtypeStruct((rows, cw), jnp.bfloat16),
        grid_spec=pltpu.PrefetchScalarGridSpec(
            num_scalar_prefetch=1,
            grid=(steps,),
            in_specs=[
                pl.BlockSpec((rows, depth), lambda j, sel: (0, 0)),
                pl.BlockSpec((depth, tn), lambda j, sel: (0, sel[0] * steps + j)),
            ],
            out_specs=pl.BlockSpec((rows, tn), lambda j, sel: (0, j)),
        ),
        compiler_params=pltpu.CompilerParams(dimension_semantics=("arbitrary",)),
        cost_estimate=pl.CostEstimate(
            flops=2 * rows * depth * cw,
            transcendentals=0,
            bytes_accessed=2 * (rows * depth + depth * cw + rows * cw),
        ),
    )(jnp.reshape(half, (1,)).astype(jnp.int32), attended, weight)


def pick_blocks(kv, local):
    return jnp.concatenate(
        [lax.dynamic_slice_in_dim(kv, local[b] * BLOCK, BLOCK, axis=2) for b in range(local.shape[0])],
        axis=2,
    )


def per_device(queries, keys, values, far_blocks, out_weight):
    rows, heads, width = queries.shape
    per_dev = rows // BLOCK
    device = lax.axis_index("ctx")
    cycle_size = lax.axis_size("ctx")
    scale = 1.0 / math.sqrt(width)
    q_t = jnp.transpose(queries, (1, 0, 2))
    kv_t = jnp.stack([jnp.transpose(keys, (1, 0, 2)), jnp.transpose(values, (1, 0, 2))])
    prev_kv = from_behind(kv_t, "ctx", 1)
    levels = []
    far_arrays = []
    for level in range(1, NOFF):
        offset = 2**level
        if offset >= cycle_size:
            continue
        target = lax.dynamic_slice_in_dim(far_blocks, (device + offset) * per_dev, per_dev, 0)[
            ::offset, level
        ]
        local = jnp.clip(target - device * per_dev, 0, per_dev - 1)
        if level == 1:
            direct = lax.ppermute(
                pick_blocks(kv_t, local), "ctx",
                [(s, s + 2) for s in range(0, cycle_size - 2, 2)],
            )
            nxt = lax.dynamic_slice_in_dim(far_blocks, (device + 1) * per_dev, per_dev, 0)[::2, 1]
            fwd_local = jnp.clip(nxt - (device - 1) * per_dev, 0, per_dev - 1)
            forwarded = lax.ppermute(
                pick_blocks(prev_kv, fwd_local), "ctx",
                [(s, s + 1) for s in range(0, cycle_size - 1, 2)],
            )
            far_arrays.append((direct, forwarded))
        else:
            far_arrays.append((from_behind(pick_blocks(kv_t, local), "ctx", offset),))
        levels.append(level)

    own = lax.dynamic_slice_in_dim(far_blocks, device * per_dev, per_dev, 0)
    query_index = device * per_dev + jnp.arange(per_dev, dtype=jnp.int32)
    used = (own <= (query_index - WINDOW // BLOCK - 1)[:, None]).astype(jnp.int32).reshape(-1)
    pick = jnp.clip(own[:, 0] - (device - 1) * per_dev, 0, per_dev - 1)
    meta = jnp.concatenate(
        [(device > 0).astype(jnp.int32)[None], pick.astype(jnp.int32), (device % 2)[None]]
    )

    row_spec = pl.BlockSpec((None, rows, width), lambda h, *_: (h, 0, 0))
    out_spec = pl.BlockSpec((rows, width), lambda h, *_: (0, h))
    k_spec = lambda n: pl.BlockSpec((None, None, n, width), lambda h, *_: (0, h, 0, 0))
    v_spec = lambda n: pl.BlockSpec((None, None, n, width), lambda h, *_: (1, h, 0, 0))
    far_specs, far_operands = [], []
    for group in far_arrays:
        for a in group:
            far_specs += [k_spec(a.shape[2]), v_spec(a.shape[2])]
            far_operands += [a, a]
    n_keys = WINDOW + BLOCK + NOFF * BLOCK
    cost = pl.CostEstimate(
        flops=4 * rows * heads * width * n_keys,
        transcendentals=rows * heads * n_keys,
        bytes_accessed=2 * heads * width * (6 * rows + sum(a.shape[2] for a in far_operands)),
    )
    attended = pl.pallas_call(
        functools.partial(attention_kernel, levels, per_dev, width, scale),
        out_shape=jax.ShapeDtypeStruct((rows, heads * width), queries.dtype),
        grid_spec=pltpu.PrefetchScalarGridSpec(
            num_scalar_prefetch=2,
            grid=(heads // HEADS_PER_STEP,),
            in_specs=[row_spec, k_spec(rows), v_spec(rows), k_spec(rows), v_spec(rows)] + far_specs,
            out_specs=out_spec,
        ),
        compiler_params=pltpu.CompilerParams(dimension_semantics=("arbitrary",)),
        cost_estimate=cost,
    )(meta, used, q_t, prev_kv, prev_kv, kv_t, kv_t, *far_operands)

    n_head = lax.axis_size("head")
    if n_head != 2:
        partial_value = jnp.dot(attended, out_weight, preferred_element_type=jnp.float32)
        return lax.psum_scatter(
            partial_value.astype(jnp.bfloat16), "head", scatter_dimension=1, tiled=True
        )
    hidx = lax.axis_index("head")
    p_other = project_half(attended, out_weight, 1 - hidx)
    received = lax.ppermute(p_other, "head", [(0, 1), (1, 0)])
    p_own = project_half(attended, out_weight, hidx)
    return (p_own.astype(jnp.float32) + received.astype(jnp.float32)).astype(jnp.bfloat16)


def solution(mesh):
    placed = (
        P("ctx", "head", None),
        P("ctx", "head", None),
        P("ctx", "head", None),
        P(),
        P("head", None),
    )
    return jax.shard_map(
        per_device, mesh=mesh, in_specs=placed, out_specs=P("ctx", "head"), check_vma=False
    )
```

```python
import functools
import math

import jax
import jax.numpy as jnp
from jax import lax
from jax.experimental import pallas as pl
from jax.experimental.pallas import tpu as pltpu
from jax.sharding import PartitionSpec as P

BLOCK = 64
WINDOW = 512
NOFF = 5
HEADS_PER_STEP = 1


def from_behind(value, axis, steps):
    count = lax.axis_size(axis)
    initial, last = (max(0, -steps), min(count, count - steps))
    return lax.ppermute(value, axis, [(source, source + steps) for source in range(initial, last)])


def block_scores(q, keys, scale):
    return lax.dot_general(
        q, keys, (((1,), (1,)), ((), ())), preferred_element_type=jnp.float32
    ) * scale


def merge(pieces, m_old, l_old, acc_old):
    top = m_old
    for s, _ in pieces:
        row_max = s.max(axis=1, keepdims=True)
        top = row_max if top is None else jnp.maximum(top, row_max)
    total = None
    summed = None
    for s, v in pieces:
        p = jnp.exp(s - top)
        part_total = p.sum(axis=1, keepdims=True)
        part = jnp.dot(p.astype(jnp.bfloat16), v, preferred_element_type=jnp.float32)
        total = part_total if total is None else total + part_total
        summed = part if summed is None else summed + part
    if m_old is not None:
        alpha = jnp.exp(m_old - top)
        total = total + l_old * alpha
        summed = summed + acc_old * alpha
    return top, total, summed


def pack_stats(m, l, width):
    lane = lax.broadcasted_iota(jnp.int32, (m.shape[0], width), 1)
    return jnp.where(lane == 0, m, jnp.where(lane == 1, l, 0.0))


def own_kernel(per_dev, width, scale, q_ref, k_ref, v_ref, acc_ref, st_ref):
    neg = jnp.float32(-jnp.inf)
    for i in range(per_dev):
        lo = i * BLOCK
        q = q_ref[lo:lo + BLOCK, :]
        n_own = lo + BLOCK
        s_o = block_scores(q, k_ref[:n_own, :], scale)
        r_ids = lax.broadcasted_iota(jnp.int32, (BLOCK, n_own), 0)
        c_ids = lax.broadcasted_iota(jnp.int32, (BLOCK, n_own), 1)
        s_o = jnp.where(c_ids <= r_ids + lo, s_o, neg)
        m, l, acc = merge([(s_o, v_ref[:n_own, :])], None, None, None)
        acc_ref[lo:lo + BLOCK, :] = acc
        st_ref[lo:lo + BLOCK, :] = pack_stats(m, l, width)


def prev_kernel(per_dev, width, scale, meta_ref, used_ref, q_ref, kp_ref, vp_ref, acc_ref, st_ref,
                odd_ref, acc_out, st_out):
    prev_ok = meta_ref[0] > 0
    neg = jnp.float32(-jnp.inf)
    for i in range(per_dev):
        lo = i * BLOCK
        q = q_ref[lo:lo + BLOCK, :]
        n_prev = per_dev * BLOCK - lo
        s_p = block_scores(q, kp_ref[lo:, :], scale)
        r_ids = lax.broadcasted_iota(jnp.int32, (BLOCK, n_prev), 0)
        c_ids = lax.broadcasted_iota(jnp.int32, (BLOCK, n_prev), 1)
        s_p = jnp.where((c_ids > r_ids) & prev_ok, s_p, neg)
        start = pl.multiple_of(meta_ref[1 + i] * BLOCK, BLOCK)
        s_f = block_scores(q, kp_ref[pl.ds(start, BLOCK), :], scale)
        s_f = jnp.where(used_ref[i * NOFF] > 0, s_f, neg)
        st = st_ref[lo:lo + BLOCK, :]
        m, l, acc = merge(
            [(s_p, vp_ref[lo:, :]), (s_f, vp_ref[pl.ds(start, BLOCK), :])],
            st[:, 0:1], st[:, 1:2], acc_ref[lo:lo + BLOCK, :],
        )
        half = (i // 2) * BLOCK
        if i % 2:
            odd_ref[half:half + BLOCK, :] = (acc / l).astype(odd_ref.dtype)
        else:
            acc_out[half:half + BLOCK, :] = acc
            st_out[half:half + BLOCK, :] = pack_stats(m, l, width)


def far_kernel(levels, per_dev, width, scale, meta_ref, used_ref, q_ref, acc_ref, st_ref, *rest):
    far_refs = rest[:-1]
    even_ref = rest[-1]
    neg = jnp.float32(-jnp.inf)
    for i in range(0, per_dev, 2):
        lo = i * BLOCK
        half = (i // 2) * BLOCK
        q = q_ref[lo:lo + BLOCK, :]
        pieces = []
        pos = 0
        for level in levels:
            offset = 2**level
            n_src = 2 if level == 1 else 1
            refs = far_refs[pos:pos + 2 * n_src]
            pos += 2 * n_src
            if i % offset:
                continue
            flo = (i // offset) * BLOCK
            k_blk = refs[0][flo:flo + BLOCK, :]
            v_blk = refs[1][flo:flo + BLOCK, :]
            if n_src == 2:
                odd = meta_ref[1 + per_dev] > 0
                k_blk = jnp.where(odd, refs[2][flo:flo + BLOCK, :], k_blk)
                v_blk = jnp.where(odd, refs[3][flo:flo + BLOCK, :], v_blk)
            s_f = block_scores(q, k_blk, scale)
            s_f = jnp.where(used_ref[i * NOFF + level] > 0, s_f, neg)
            pieces.append((s_f, v_blk))
        st = st_ref[half:half + BLOCK, :]
        m, l, acc = merge(pieces, st[:, 0:1], st[:, 1:2], acc_ref[half:half + BLOCK, :])
        even_ref[half:half + BLOCK, :] = (acc / l).astype(even_ref.dtype)


def matmul_kernel(sel_ref, a_ref, w_ref, o_ref):
    o_ref[...] = jnp.dot(a_ref[...], w_ref[...], preferred_element_type=jnp.float32).astype(
        o_ref.dtype
    )


def project_half(attended, weight, half, tn=512):
    rows, depth = attended.shape
    cw = weight.shape[1] // 2
    steps = cw // tn
    return pl.pallas_call(
        matmul_kernel,
        out_shape=jax.ShapeDtypeStruct((rows, cw), jnp.bfloat16),
        grid_spec=pltpu.PrefetchScalarGridSpec(
            num_scalar_prefetch=1,
            grid=(steps,),
            in_specs=[
                pl.BlockSpec((rows, depth), lambda j, sel: (0, 0)),
                pl.BlockSpec((depth, tn), lambda j, sel: (0, sel[0] * steps + j)),
            ],
            out_specs=pl.BlockSpec((rows, tn), lambda j, sel: (0, j)),
        ),
        compiler_params=pltpu.CompilerParams(dimension_semantics=("arbitrary",)),
        cost_estimate=pl.CostEstimate(
            flops=2 * rows * depth * cw,
            transcendentals=0,
            bytes_accessed=2 * (rows * depth + depth * cw + rows * cw),
        ),
    )(jnp.reshape(half, (1,)).astype(jnp.int32), attended, weight)


def pick_blocks(kv, local):
    return jnp.concatenate(
        [lax.dynamic_slice_in_dim(kv, local[b] * BLOCK, BLOCK, axis=2) for b in range(local.shape[0])],
        axis=2,
    )


def per_device(queries, keys, values, far_blocks, out_weight):
    rows, heads, width = queries.shape
    per_dev = rows // BLOCK
    device = lax.axis_index("ctx")
    cycle_size = lax.axis_size("ctx")
    scale = 1.0 / math.sqrt(width)
    q_t = jnp.transpose(queries, (1, 0, 2))
    kv_t = jnp.stack([jnp.transpose(keys, (1, 0, 2)), jnp.transpose(values, (1, 0, 2))])
    prev_kv = from_behind(kv_t, "ctx", 1)
    levels = []
    far_arrays = []
    for level in range(1, NOFF):
        offset = 2**level
        if offset >= cycle_size:
            continue
        target = lax.dynamic_slice_in_dim(far_blocks, (device + offset) * per_dev, per_dev, 0)[
            ::offset, level
        ]
        local = jnp.clip(target - device * per_dev, 0, per_dev - 1)
        if level == 1:
            direct = lax.ppermute(
                pick_blocks(kv_t, local), "ctx",
                [(s, s + 2) for s in range(0, cycle_size - 2, 2)],
            )
            nxt = lax.dynamic_slice_in_dim(far_blocks, (device + 1) * per_dev, per_dev, 0)[::2, 1]
            fwd_local = jnp.clip(nxt - (device - 1) * per_dev, 0, per_dev - 1)
            far_arrays.append((direct, None))
        else:
            far_arrays.append((from_behind(pick_blocks(kv_t, local), "ctx", offset),))
        levels.append(level)

    own = lax.dynamic_slice_in_dim(far_blocks, device * per_dev, per_dev, 0)
    query_index = device * per_dev + jnp.arange(per_dev, dtype=jnp.int32)
    used = (own <= (query_index - WINDOW // BLOCK - 1)[:, None]).astype(jnp.int32).reshape(-1)
    pick = jnp.clip(own[:, 0] - (device - 1) * per_dev, 0, per_dev - 1)
    meta = jnp.concatenate(
        [(device > 0).astype(jnp.int32)[None], pick.astype(jnp.int32), (device % 2)[None]]
    )

    row_spec = lambda n: pl.BlockSpec((None, n, width), lambda h, *_: (h, 0, 0))
    out_spec = lambda n: pl.BlockSpec((n, width), lambda h, *_: (0, h))
    k_spec = lambda n: pl.BlockSpec((None, None, n, width), lambda h, *_: (0, h, 0, 0))
    v_spec = lambda n: pl.BlockSpec((None, None, n, width), lambda h, *_: (1, h, 0, 0))
    half_rows = rows // 2
    f32 = jnp.float32
    params = pltpu.CompilerParams(dimension_semantics=("arbitrary",))
    state = lambda n: jax.ShapeDtypeStruct((heads, n, width), f32)

    def cost(keys_per_row, n_rows, extra_bytes):
        return pl.CostEstimate(
            flops=4 * n_rows * heads * width * keys_per_row,
            transcendentals=n_rows * heads * keys_per_row,
            bytes_accessed=extra_bytes,
        )

    acc0, st0 = pl.pallas_call(
        functools.partial(own_kernel, per_dev, width, scale),
        out_shape=(state(rows), state(rows)),
        grid=(heads,),
        in_specs=[row_spec(rows), k_spec(rows), v_spec(rows)],
        out_specs=(row_spec(rows), row_spec(rows)),
        compiler_params=params,
        cost_estimate=cost(WINDOW // 2, rows, 2 * heads * rows * width * (3 * 2 + 2 * 4)),
    )(q_t, kv_t, kv_t)

    prev_kv, acc0, st0 = lax.optimization_barrier((prev_kv, acc0, st0))
    if far_arrays and far_arrays[0][1] is None:
        forwarded = lax.ppermute(
            pick_blocks(prev_kv, fwd_local), "ctx",
            [(s, s + 1) for s in range(0, cycle_size - 1, 2)],
        )
        far_arrays[0] = (far_arrays[0][0], forwarded)
    far_specs, far_operands = [], []
    for group in far_arrays:
        for a in group:
            far_specs += [k_spec(a.shape[2]), v_spec(a.shape[2])]
            far_operands += [a, a]
    att_odd, acc1, st1 = pl.pallas_call(
        functools.partial(prev_kernel, per_dev, width, scale),
        out_shape=(
            jax.ShapeDtypeStruct((half_rows, heads * width), queries.dtype),
            state(half_rows),
            state(half_rows),
        ),
        grid_spec=pltpu.PrefetchScalarGridSpec(
            num_scalar_prefetch=2,
            grid=(heads,),
            in_specs=[row_spec(rows), k_spec(rows), v_spec(rows), row_spec(rows), row_spec(rows)],
            out_specs=(out_spec(half_rows), row_spec(half_rows), row_spec(half_rows)),
        ),
        compiler_params=params,
        cost_estimate=cost(WINDOW // 2 + BLOCK, rows, heads * rows * width * (3 * 2 + 2 * 4 + 8)),
    )(meta, used, q_t, prev_kv, prev_kv, acc0, st0)

    att_even = pl.pallas_call(
        functools.partial(far_kernel, levels, per_dev, width, scale),
        out_shape=jax.ShapeDtypeStruct((half_rows, heads * width), queries.dtype),
        grid_spec=pltpu.PrefetchScalarGridSpec(
            num_scalar_prefetch=2,
            grid=(heads,),
            in_specs=[row_spec(rows), row_spec(half_rows), row_spec(half_rows)] + far_specs,
            out_specs=out_spec(half_rows),
        ),
        compiler_params=params,
        cost_estimate=cost(2 * BLOCK, half_rows, heads * width * (2 * rows + 8 * half_rows + 2 * sum(a.shape[2] for a in far_operands))),
    )(meta, used, q_t, acc1, st1, *far_operands)

    n_head = lax.axis_size("head")
    if n_head != 2:
        parts = []
        for att in (att_even, att_odd):
            partial_value = jnp.dot(att, out_weight, preferred_element_type=jnp.float32)
            parts.append(lax.psum_scatter(
                partial_value.astype(jnp.bfloat16), "head", scatter_dimension=1, tiled=True
            ))
    else:
        hidx = lax.axis_index("head")
        parts = []
        for att in (att_odd, att_even):
            p_other = project_half(att, out_weight, 1 - hidx)
            received = lax.ppermute(p_other, "head", [(0, 1), (1, 0)])
            p_own = project_half(att, out_weight, hidx)
            parts.append(
                (p_own.astype(jnp.float32) + received.astype(jnp.float32)).astype(jnp.bfloat16)
            )
        parts = parts[::-1]
    even, odd = (p.reshape(per_dev // 2, BLOCK, -1) for p in parts)
    return jnp.stack([even, odd], axis=1).reshape(rows, -1)


def solution(mesh):
    placed = (
        P("ctx", "head", None),
        P("ctx", "head", None),
        P("ctx", "head", None),
        P(),
        P("head", None),
    )
    return jax.shard_map(
        per_device, mesh=mesh, in_specs=placed, out_specs=P("ctx", "head"), check_vma=False
    )
```

```python
import functools
import math

import jax
import jax.numpy as jnp
from jax import lax
from jax.experimental import pallas as pl
from jax.experimental.pallas import tpu as pltpu
from jax.sharding import PartitionSpec as P

BLOCK = 64
WINDOW = 512
NOFF = 5
HEADS_PER_STEP = 1


def from_behind(value, axis, steps):
    count = lax.axis_size(axis)
    initial, last = (max(0, -steps), min(count, count - steps))
    return lax.ppermute(value, axis, [(source, source + steps) for source in range(initial, last)])


def block_scores(q, keys, scale):
    return lax.dot_general(
        q, keys, (((1,), (1,)), ((), ())), preferred_element_type=jnp.float32
    ) * scale


def merge(pieces, m_old, l_old, acc_old):
    top = m_old
    for s, _ in pieces:
        row_max = s.max(axis=1, keepdims=True)
        top = row_max if top is None else jnp.maximum(top, row_max)
    total = None
    summed = None
    for s, v in pieces:
        p = jnp.exp(s - top)
        part_total = p.sum(axis=1, keepdims=True)
        part = jnp.dot(p.astype(jnp.bfloat16), v, preferred_element_type=jnp.float32)
        total = part_total if total is None else total + part_total
        summed = part if summed is None else summed + part
    if m_old is not None:
        alpha = jnp.exp(m_old - top)
        total = total + l_old * alpha
        summed = summed + acc_old * alpha
    return top, total, summed


def pack_stats(m, l, width):
    lane = lax.broadcasted_iota(jnp.int32, (m.shape[0], width), 1)
    return jnp.where(lane == 0, m, jnp.where(lane == 1, l, 0.0))


TILE = 256


def own_kernel(per_dev, width, scale, q_ref, k_ref, v_ref, acc_ref, st_ref):
    neg = jnp.float32(-jnp.inf)
    rows = per_dev * BLOCK
    for lo in range(0, rows, TILE):
        q = q_ref[lo:lo + TILE, :]
        n_own = lo + TILE
        s_o = block_scores(q, k_ref[:n_own, :], scale)
        r_ids = lax.broadcasted_iota(jnp.int32, (TILE, n_own), 0)
        c_ids = lax.broadcasted_iota(jnp.int32, (TILE, n_own), 1)
        s_o = jnp.where(c_ids <= r_ids + lo, s_o, neg)
        m, l, acc = merge([(s_o, v_ref[:n_own, :])], None, None, None)
        acc_ref[lo:lo + TILE, :] = acc
        st_ref[lo:lo + TILE, :] = pack_stats(m, l, width)


def column_map(n_cols, values):
    seg = lax.broadcasted_iota(jnp.int32, (1, n_cols), 1) // BLOCK
    out = jnp.zeros((1, n_cols), jnp.int32)
    for j, value in enumerate(values):
        out = jnp.where(seg == j, value, out)
    return out


def prev_kernel(per_dev, width, scale, meta_ref, used_ref, q_ref, kp_ref, vp_ref, acc_ref, st_ref,
                odd_ref, acc_out, st_out):
    prev_ok = meta_ref[0] > 0
    neg = jnp.float32(-jnp.inf)
    rows = per_dev * BLOCK
    per_tile = TILE // BLOCK
    for lo in range(0, rows, TILE):
        q = q_ref[lo:lo + TILE, :]
        n_prev = rows - lo
        s_p = block_scores(q, kp_ref[lo:, :], scale)
        r_ids = lax.broadcasted_iota(jnp.int32, (TILE, n_prev), 0)
        c_ids = lax.broadcasted_iota(jnp.int32, (TILE, n_prev), 1)
        s_p = jnp.where((c_ids > r_ids) & prev_ok, s_p, neg)
        blocks = range(lo // BLOCK, lo // BLOCK + per_tile)
        starts = [pl.multiple_of(meta_ref[1 + i] * BLOCK, BLOCK) for i in blocks]
        k0 = jnp.concatenate([kp_ref[pl.ds(st, BLOCK), :] for st in starts], axis=0)
        v0 = jnp.concatenate([vp_ref[pl.ds(st, BLOCK), :] for st in starts], axis=0)
        s_f = block_scores(q, k0, scale)
        flags = column_map(TILE, [used_ref[i * NOFF] for i in blocks])
        r_blk = lax.broadcasted_iota(jnp.int32, (TILE, TILE), 0) // BLOCK
        c_blk = lax.broadcasted_iota(jnp.int32, (TILE, TILE), 1) // BLOCK
        s_f = jnp.where((r_blk == c_blk) & (flags > 0), s_f, neg)
        st = st_ref[lo:lo + TILE, :]
        m, l, acc = merge(
            [(s_p, vp_ref[lo:, :]), (s_f, v0)], st[:, 0:1], st[:, 1:2], acc_ref[lo:lo + TILE, :]
        )
        for b, i in enumerate(blocks):
            sl = slice(b * BLOCK, (b + 1) * BLOCK)
            half = (i // 2) * BLOCK
            if i % 2:
                odd_ref[half:half + BLOCK, :] = (acc[sl] / l[sl]).astype(odd_ref.dtype)
            else:
                acc_out[half:half + BLOCK, :] = acc[sl]
                st_out[half:half + BLOCK, :] = pack_stats(m[sl], l[sl], width)


def far_kernel(levels, per_dev, width, scale, meta_ref, used_ref, q_ref, acc_ref, st_ref, *rest):
    far_refs = rest[:-1]
    even_ref = rest[-1]
    neg = jnp.float32(-jnp.inf)
    n_even = per_dev // 2
    q = jnp.concatenate([q_ref[2 * e * BLOCK:(2 * e + 1) * BLOCK, :] for e in range(n_even)], axis=0)
    keys, vals, targets, flags = [], [], [], []
    pos = 0
    for level in levels:
        offset = 2**level
        n_src = 2 if level == 1 else 1
        refs = far_refs[pos:pos + 2 * n_src]
        pos += 2 * n_src
        k_lvl = refs[0][...]
        v_lvl = refs[1][...]
        if n_src == 2:
            odd = meta_ref[1 + per_dev] > 0
            k_lvl = jnp.where(odd, refs[2][...], k_lvl)
            v_lvl = jnp.where(odd, refs[3][...], v_lvl)
        keys.append(k_lvl)
        vals.append(v_lvl)
        for k in range(k_lvl.shape[0] // BLOCK):
            qblock = k * offset
            targets.append(qblock // 2)
            flags.append(used_ref[qblock * NOFF + level])
    k_far = jnp.concatenate(keys, axis=0)
    v_far = jnp.concatenate(vals, axis=0)
    n_keys = k_far.shape[0]
    s_f = block_scores(q, k_far, scale)
    col_target = column_map(n_keys, targets)
    col_flag = column_map(n_keys, flags)
    r_blk = lax.broadcasted_iota(jnp.int32, (n_even * BLOCK, n_keys), 0) // BLOCK
    s_f = jnp.where((r_blk == col_target) & (col_flag > 0), s_f, neg)
    st = st_ref[...]
    m, l, acc = merge([(s_f, v_far)], st[:, 0:1], st[:, 1:2], acc_ref[...])
    even_ref[...] = (acc / l).astype(even_ref.dtype)


def matmul_kernel(sel_ref, a_ref, w_ref, o_ref):
    o_ref[...] = jnp.dot(a_ref[...], w_ref[...], preferred_element_type=jnp.float32).astype(
        o_ref.dtype
    )


def project_half(attended, weight, half, tn=512):
    rows, depth = attended.shape
    cw = weight.shape[1] // 2
    steps = cw // tn
    return pl.pallas_call(
        matmul_kernel,
        out_shape=jax.ShapeDtypeStruct((rows, cw), jnp.bfloat16),
        grid_spec=pltpu.PrefetchScalarGridSpec(
            num_scalar_prefetch=1,
            grid=(steps,),
            in_specs=[
                pl.BlockSpec((rows, depth), lambda j, sel: (0, 0)),
                pl.BlockSpec((depth, tn), lambda j, sel: (0, sel[0] * steps + j)),
            ],
            out_specs=pl.BlockSpec((rows, tn), lambda j, sel: (0, j)),
        ),
        compiler_params=pltpu.CompilerParams(dimension_semantics=("arbitrary",)),
        cost_estimate=pl.CostEstimate(
            flops=2 * rows * depth * cw,
            transcendentals=0,
            bytes_accessed=2 * (rows * depth + depth * cw + rows * cw),
        ),
    )(jnp.reshape(half, (1,)).astype(jnp.int32), attended, weight)


def pick_blocks(kv, local):
    return jnp.concatenate(
        [lax.dynamic_slice_in_dim(kv, local[b] * BLOCK, BLOCK, axis=2) for b in range(local.shape[0])],
        axis=2,
    )


def per_device(queries, keys, values, far_blocks, out_weight):
    rows, heads, width = queries.shape
    per_dev = rows // BLOCK
    device = lax.axis_index("ctx")
    cycle_size = lax.axis_size("ctx")
    scale = 1.0 / math.sqrt(width)
    q_t = jnp.transpose(queries, (1, 0, 2))
    kv_t = jnp.stack([jnp.transpose(keys, (1, 0, 2)), jnp.transpose(values, (1, 0, 2))])
    prev_kv = from_behind(kv_t, "ctx", 1)
    levels = []
    far_arrays = []
    for level in range(1, NOFF):
        offset = 2**level
        if offset >= cycle_size:
            continue
        target = lax.dynamic_slice_in_dim(far_blocks, (device + offset) * per_dev, per_dev, 0)[
            ::offset, level
        ]
        local = jnp.clip(target - device * per_dev, 0, per_dev - 1)
        if level == 1:
            direct = lax.ppermute(
                pick_blocks(kv_t, local), "ctx",
                [(s, s + 2) for s in range(0, cycle_size - 2, 2)],
            )
            nxt = lax.dynamic_slice_in_dim(far_blocks, (device + 1) * per_dev, per_dev, 0)[::2, 1]
            fwd_local = jnp.clip(nxt - (device - 1) * per_dev, 0, per_dev - 1)
            far_arrays.append((direct, None))
        else:
            far_arrays.append((from_behind(pick_blocks(kv_t, local), "ctx", offset),))
        levels.append(level)

    own = lax.dynamic_slice_in_dim(far_blocks, device * per_dev, per_dev, 0)
    query_index = device * per_dev + jnp.arange(per_dev, dtype=jnp.int32)
    used = (own <= (query_index - WINDOW // BLOCK - 1)[:, None]).astype(jnp.int32).reshape(-1)
    pick = jnp.clip(own[:, 0] - (device - 1) * per_dev, 0, per_dev - 1)
    meta = jnp.concatenate(
        [(device > 0).astype(jnp.int32)[None], pick.astype(jnp.int32), (device % 2)[None]]
    )

    row_spec = lambda n: pl.BlockSpec((None, n, width), lambda h, *_: (h, 0, 0))
    out_spec = lambda n: pl.BlockSpec((n, width), lambda h, *_: (0, h))
    k_spec = lambda n: pl.BlockSpec((None, None, n, width), lambda h, *_: (0, h, 0, 0))
    v_spec = lambda n: pl.BlockSpec((None, None, n, width), lambda h, *_: (1, h, 0, 0))
    half_rows = rows // 2
    f32 = jnp.float32
    params = pltpu.CompilerParams(dimension_semantics=("arbitrary",))
    state = lambda n: jax.ShapeDtypeStruct((heads, n, width), f32)

    def cost(keys_per_row, n_rows, extra_bytes):
        return pl.CostEstimate(
            flops=4 * n_rows * heads * width * keys_per_row,
            transcendentals=n_rows * heads * keys_per_row,
            bytes_accessed=extra_bytes,
        )

    acc0, st0 = pl.pallas_call(
        functools.partial(own_kernel, per_dev, width, scale),
        out_shape=(state(rows), state(rows)),
        grid=(heads,),
        in_specs=[row_spec(rows), k_spec(rows), v_spec(rows)],
        out_specs=(row_spec(rows), row_spec(rows)),
        compiler_params=params,
        cost_estimate=cost(WINDOW // 2, rows, 2 * heads * rows * width * (3 * 2 + 2 * 4)),
    )(q_t, kv_t, kv_t)

    prev_kv, acc0, st0 = lax.optimization_barrier((prev_kv, acc0, st0))
    if far_arrays and far_arrays[0][1] is None:
        forwarded = lax.ppermute(
            pick_blocks(prev_kv, fwd_local), "ctx",
            [(s, s + 1) for s in range(0, cycle_size - 1, 2)],
        )
        far_arrays[0] = (far_arrays[0][0], forwarded)
    far_specs, far_operands = [], []
    for group in far_arrays:
        for a in group:
            far_specs += [k_spec(a.shape[2]), v_spec(a.shape[2])]
            far_operands += [a, a]
    att_odd, acc1, st1 = pl.pallas_call(
        functools.partial(prev_kernel, per_dev, width, scale),
        out_shape=(
            jax.ShapeDtypeStruct((half_rows, heads * width), queries.dtype),
            state(half_rows),
            state(half_rows),
        ),
        grid_spec=pltpu.PrefetchScalarGridSpec(
            num_scalar_prefetch=2,
            grid=(heads,),
            in_specs=[row_spec(rows), k_spec(rows), v_spec(rows), row_spec(rows), row_spec(rows)],
            out_specs=(out_spec(half_rows), row_spec(half_rows), row_spec(half_rows)),
        ),
        compiler_params=params,
        cost_estimate=cost(WINDOW // 2 + BLOCK, rows, heads * rows * width * (3 * 2 + 2 * 4 + 8)),
    )(meta, used, q_t, prev_kv, prev_kv, acc0, st0)

    att_even = pl.pallas_call(
        functools.partial(far_kernel, levels, per_dev, width, scale),
        out_shape=jax.ShapeDtypeStruct((half_rows, heads * width), queries.dtype),
        grid_spec=pltpu.PrefetchScalarGridSpec(
            num_scalar_prefetch=2,
            grid=(heads,),
            in_specs=[row_spec(rows), row_spec(half_rows), row_spec(half_rows)] + far_specs,
            out_specs=out_spec(half_rows),
        ),
        compiler_params=params,
        cost_estimate=cost(2 * BLOCK, half_rows, heads * width * (2 * rows + 8 * half_rows + 2 * sum(a.shape[2] for a in far_operands))),
    )(meta, used, q_t, acc1, st1, *far_operands)

    n_head = lax.axis_size("head")
    if n_head != 2:
        parts = []
        for att in (att_even, att_odd):
            partial_value = jnp.dot(att, out_weight, preferred_element_type=jnp.float32)
            parts.append(lax.psum_scatter(
                partial_value.astype(jnp.bfloat16), "head", scatter_dimension=1, tiled=True
            ))
    else:
        hidx = lax.axis_index("head")
        parts = []
        for att in (att_odd, att_even):
            p_other = project_half(att, out_weight, 1 - hidx)
            received = lax.ppermute(p_other, "head", [(0, 1), (1, 0)])
            p_own = project_half(att, out_weight, hidx)
            parts.append(
                (p_own.astype(jnp.float32) + received.astype(jnp.float32)).astype(jnp.bfloat16)
            )
        parts = parts[::-1]
    even, odd = (p.reshape(per_dev // 2, BLOCK, -1) for p in parts)
    return jnp.stack([even, odd], axis=1).reshape(rows, -1)


def solution(mesh):
    placed = (
        P("ctx", "head", None),
        P("ctx", "head", None),
        P("ctx", "head", None),
        P(),
        P("head", None),
    )
    return jax.shard_map(
        per_device, mesh=mesh, in_specs=placed, out_specs=P("ctx", "head"), check_vma=False
    )
```

```python
import functools
import math

import jax
import jax.numpy as jnp
from jax import lax
from jax.experimental import pallas as pl
from jax.experimental.pallas import tpu as pltpu
from jax.sharding import PartitionSpec as P

BLOCK = 64
WINDOW = 512
NOFF = 5
HEADS_PER_STEP = 1


def from_behind(value, axis, steps):
    count = lax.axis_size(axis)
    initial, last = (max(0, -steps), min(count, count - steps))
    return lax.ppermute(value, axis, [(source, source + steps) for source in range(initial, last)])


def block_scores(q, keys, scale):
    return lax.dot_general(
        q, keys, (((1,), (1,)), ((), ())), preferred_element_type=jnp.float32
    ) * scale


def merge(pieces, m_old, l_old, acc_old):
    top = m_old
    for s, _ in pieces:
        row_max = s.max(axis=1, keepdims=True)
        top = row_max if top is None else jnp.maximum(top, row_max)
    total = None
    summed = None
    for s, v in pieces:
        p = jnp.exp(s - top)
        part_total = p.sum(axis=1, keepdims=True)
        part = jnp.dot(p.astype(jnp.bfloat16), v, preferred_element_type=jnp.float32)
        total = part_total if total is None else total + part_total
        summed = part if summed is None else summed + part
    if m_old is not None:
        alpha = jnp.exp(m_old - top)
        total = total + l_old * alpha
        summed = summed + acc_old * alpha
    return top, total, summed


def pack_stats(m, l, width):
    lane = lax.broadcasted_iota(jnp.int32, (m.shape[0], width), 1)
    return jnp.where(lane == 0, m, jnp.where(lane == 1, l, 0.0))


TILE = 256


def own_kernel(per_dev, width, scale, q_ref, k_ref, v_ref, acc_ref, st_ref):
    neg = jnp.float32(-jnp.inf)
    rows = per_dev * BLOCK
    for lo in range(0, rows, TILE):
        q = q_ref[lo:lo + TILE, :]
        n_own = lo + TILE
        s_o = block_scores(q, k_ref[:n_own, :], scale)
        r_ids = lax.broadcasted_iota(jnp.int32, (TILE, n_own), 0)
        c_ids = lax.broadcasted_iota(jnp.int32, (TILE, n_own), 1)
        s_o = jnp.where(c_ids <= r_ids + lo, s_o, neg)
        m, l, acc = merge([(s_o, v_ref[:n_own, :])], None, None, None)
        acc_ref[lo:lo + TILE, :] = acc
        st_ref[lo:lo + TILE, :] = pack_stats(m, l, width)


def column_map(n_cols, values):
    seg = lax.broadcasted_iota(jnp.int32, (1, n_cols), 1) // BLOCK
    out = jnp.zeros((1, n_cols), jnp.int32)
    for j, value in enumerate(values):
        out = jnp.where(seg == j, value, out)
    return out


def prev_kernel(per_dev, width, scale, meta_ref, used_ref, q_ref, kp_ref, vp_ref, acc_ref, st_ref,
                odd_ref, acc_out, st_out):
    prev_ok = meta_ref[0] > 0
    neg = jnp.float32(-jnp.inf)
    rows = per_dev * BLOCK
    per_tile = TILE // BLOCK
    for lo in range(0, rows, TILE):
        q = q_ref[lo:lo + TILE, :]
        n_prev = rows - lo
        s_p = block_scores(q, kp_ref[lo:, :], scale)
        r_ids = lax.broadcasted_iota(jnp.int32, (TILE, n_prev), 0)
        c_ids = lax.broadcasted_iota(jnp.int32, (TILE, n_prev), 1)
        s_p = jnp.where((c_ids > r_ids) & prev_ok, s_p, neg)
        blocks = range(lo // BLOCK, lo // BLOCK + per_tile)
        starts = [pl.multiple_of(meta_ref[1 + i] * BLOCK, BLOCK) for i in blocks]
        k0 = jnp.concatenate([kp_ref[pl.ds(st, BLOCK), :] for st in starts], axis=0)
        v0 = jnp.concatenate([vp_ref[pl.ds(st, BLOCK), :] for st in starts], axis=0)
        s_f = block_scores(q, k0, scale)
        flags = column_map(TILE, [used_ref[i * NOFF] for i in blocks])
        r_blk = lax.broadcasted_iota(jnp.int32, (TILE, TILE), 0) // BLOCK
        c_blk = lax.broadcasted_iota(jnp.int32, (TILE, TILE), 1) // BLOCK
        s_f = jnp.where((r_blk == c_blk) & (flags > 0), s_f, neg)
        st = st_ref[lo:lo + TILE, :]
        m, l, acc = merge(
            [(s_p, vp_ref[lo:, :]), (s_f, v0)], st[:, 0:1], st[:, 1:2], acc_ref[lo:lo + TILE, :]
        )
        for b, i in enumerate(blocks):
            sl = slice(b * BLOCK, (b + 1) * BLOCK)
            half = (i // 2) * BLOCK
            if i % 2:
                odd_ref[half:half + BLOCK, :] = (acc[sl] / l[sl]).astype(odd_ref.dtype)
            else:
                acc_out[half:half + BLOCK, :] = acc[sl]
                st_out[half:half + BLOCK, :] = pack_stats(m[sl], l[sl], width)


def far_kernel(levels, per_dev, width, scale, meta_ref, used_ref, q_ref, acc_ref, st_ref, *rest):
    far_refs = rest[:-1]
    even_ref = rest[-1]
    neg = jnp.float32(-jnp.inf)
    n_even = per_dev // 2
    q = jnp.concatenate([q_ref[2 * e * BLOCK:(2 * e + 1) * BLOCK, :] for e in range(n_even)], axis=0)
    keys, vals, targets, flags = [], [], [], []
    pos = 0
    for level in levels:
        offset = 2**level
        n_src = 2 if level == 1 else 1
        refs = far_refs[pos:pos + 2 * n_src]
        pos += 2 * n_src
        k_lvl = refs[0][...]
        v_lvl = refs[1][...]
        if n_src == 2:
            odd = meta_ref[1 + per_dev] > 0
            k_lvl = jnp.where(odd, refs[2][...], k_lvl)
            v_lvl = jnp.where(odd, refs[3][...], v_lvl)
        keys.append(k_lvl)
        vals.append(v_lvl)
        for k in range(k_lvl.shape[0] // BLOCK):
            qblock = k * offset
            targets.append(qblock // 2)
            flags.append(used_ref[qblock * NOFF + level])
    k_far = jnp.concatenate(keys, axis=0)
    v_far = jnp.concatenate(vals, axis=0)
    n_keys = k_far.shape[0]
    s_f = block_scores(q, k_far, scale)
    col_target = column_map(n_keys, targets)
    col_flag = column_map(n_keys, flags)
    r_blk = lax.broadcasted_iota(jnp.int32, (n_even * BLOCK, n_keys), 0) // BLOCK
    s_f = jnp.where((r_blk == col_target) & (col_flag > 0), s_f, neg)
    st = st_ref[...]
    m, l, acc = merge([(s_f, v_far)], st[:, 0:1], st[:, 1:2], acc_ref[...])
    even_ref[...] = (acc / l).astype(even_ref.dtype)


def matmul_kernel(sel_ref, a_ref, w_ref, o_ref):
    o_ref[...] = jnp.dot(a_ref[...], w_ref[...], preferred_element_type=jnp.float32).astype(
        o_ref.dtype
    )


def project_half(attended, weight, half, tn=512):
    rows, depth = attended.shape
    cw = weight.shape[1] // 2
    steps = cw // tn
    return pl.pallas_call(
        matmul_kernel,
        out_shape=jax.ShapeDtypeStruct((rows, cw), jnp.bfloat16),
        grid_spec=pltpu.PrefetchScalarGridSpec(
            num_scalar_prefetch=1,
            grid=(steps,),
            in_specs=[
                pl.BlockSpec((rows, depth), lambda j, sel: (0, 0)),
                pl.BlockSpec((depth, tn), lambda j, sel: (0, sel[0] * steps + j)),
            ],
            out_specs=pl.BlockSpec((rows, tn), lambda j, sel: (0, j)),
        ),
        compiler_params=pltpu.CompilerParams(dimension_semantics=("arbitrary",)),
        cost_estimate=pl.CostEstimate(
            flops=2 * rows * depth * cw,
            transcendentals=0,
            bytes_accessed=2 * (rows * depth + depth * cw + rows * cw),
        ),
    )(jnp.reshape(half, (1,)).astype(jnp.int32), attended, weight)


def pick_blocks(kv, local):
    return jnp.concatenate(
        [lax.dynamic_slice_in_dim(kv, local[b] * BLOCK, BLOCK, axis=2) for b in range(local.shape[0])],
        axis=2,
    )


def per_device(queries, keys, values, far_blocks, out_weight):
    rows, heads, width = queries.shape
    per_dev = rows // BLOCK
    device = lax.axis_index("ctx")
    cycle_size = lax.axis_size("ctx")
    scale = 1.0 / math.sqrt(width)
    q_t = jnp.transpose(queries, (1, 0, 2))
    kv_t = jnp.stack([jnp.transpose(keys, (1, 0, 2)), jnp.transpose(values, (1, 0, 2))])
    prev_kv = from_behind(kv_t, "ctx", 1)
    levels = []
    sends = []
    for level in range(1, NOFF):
        offset = 2**level
        if offset >= cycle_size:
            continue
        target = lax.dynamic_slice_in_dim(far_blocks, (device + offset) * per_dev, per_dev, 0)[
            ::offset, level
        ]
        local = jnp.clip(target - device * per_dev, 0, per_dev - 1)
        if level == 1:
            pairs = [(s, s + 2) for s in range(0, cycle_size - 2, 2)]
            nxt = lax.dynamic_slice_in_dim(far_blocks, (device + 1) * per_dev, per_dev, 0)[::2, 1]
            fwd_local = jnp.clip(nxt - (device - 1) * per_dev, 0, per_dev - 1)
        else:
            pairs = [(s, s + offset) for s in range(0, cycle_size - offset)]
        sends.append((pick_blocks(kv_t, local), pairs))
        levels.append(level)
    q_t, kv_t, *operands = lax.optimization_barrier((q_t, kv_t, *[op for op, _ in sends]))
    far_arrays = []
    for (_, pairs), op, level in zip(sends, operands, levels):
        received = lax.ppermute(op, "ctx", pairs)
        far_arrays.append((received, None) if level == 1 else (received,))

    own = lax.dynamic_slice_in_dim(far_blocks, device * per_dev, per_dev, 0)
    query_index = device * per_dev + jnp.arange(per_dev, dtype=jnp.int32)
    used = (own <= (query_index - WINDOW // BLOCK - 1)[:, None]).astype(jnp.int32).reshape(-1)
    pick = jnp.clip(own[:, 0] - (device - 1) * per_dev, 0, per_dev - 1)
    meta = jnp.concatenate(
        [(device > 0).astype(jnp.int32)[None], pick.astype(jnp.int32), (device % 2)[None]]
    )

    row_spec = lambda n: pl.BlockSpec((None, n, width), lambda h, *_: (h, 0, 0))
    out_spec = lambda n: pl.BlockSpec((n, width), lambda h, *_: (0, h))
    k_spec = lambda n: pl.BlockSpec((None, None, n, width), lambda h, *_: (0, h, 0, 0))
    v_spec = lambda n: pl.BlockSpec((None, None, n, width), lambda h, *_: (1, h, 0, 0))
    half_rows = rows // 2
    f32 = jnp.float32
    params = pltpu.CompilerParams(dimension_semantics=("arbitrary",))
    state = lambda n: jax.ShapeDtypeStruct((heads, n, width), f32)

    def cost(keys_per_row, n_rows, extra_bytes):
        return pl.CostEstimate(
            flops=4 * n_rows * heads * width * keys_per_row,
            transcendentals=n_rows * heads * keys_per_row,
            bytes_accessed=extra_bytes,
        )

    acc0, st0 = pl.pallas_call(
        functools.partial(own_kernel, per_dev, width, scale),
        out_shape=(state(rows), state(rows)),
        grid=(heads,),
        in_specs=[row_spec(rows), k_spec(rows), v_spec(rows)],
        out_specs=(row_spec(rows), row_spec(rows)),
        compiler_params=params,
        cost_estimate=cost(WINDOW // 2, rows, 2 * heads * rows * width * (3 * 2 + 2 * 4)),
    )(q_t, kv_t, kv_t)

    prev_kv, acc0, st0 = lax.optimization_barrier((prev_kv, acc0, st0))
    if far_arrays and far_arrays[0][1] is None:
        forwarded = lax.ppermute(
            pick_blocks(prev_kv, fwd_local), "ctx",
            [(s, s + 1) for s in range(0, cycle_size - 1, 2)],
        )
        far_arrays[0] = (far_arrays[0][0], forwarded)
    far_specs, far_operands = [], []
    for group in far_arrays:
        for a in group:
            far_specs += [k_spec(a.shape[2]), v_spec(a.shape[2])]
            far_operands += [a, a]
    att_odd, acc1, st1 = pl.pallas_call(
        functools.partial(prev_kernel, per_dev, width, scale),
        out_shape=(
            jax.ShapeDtypeStruct((half_rows, heads * width), queries.dtype),
            state(half_rows),
            state(half_rows),
        ),
        grid_spec=pltpu.PrefetchScalarGridSpec(
            num_scalar_prefetch=2,
            grid=(heads,),
            in_specs=[row_spec(rows), k_spec(rows), v_spec(rows), row_spec(rows), row_spec(rows)],
            out_specs=(out_spec(half_rows), row_spec(half_rows), row_spec(half_rows)),
        ),
        compiler_params=params,
        cost_estimate=cost(WINDOW // 2 + BLOCK, rows, heads * rows * width * (3 * 2 + 2 * 4 + 8)),
    )(meta, used, q_t, prev_kv, prev_kv, acc0, st0)

    n_head = lax.axis_size("head")
    if n_head != 2:
        att_even = pl.pallas_call(
            functools.partial(far_kernel, levels, per_dev, width, scale),
            out_shape=jax.ShapeDtypeStruct((half_rows, heads * width), queries.dtype),
            grid_spec=pltpu.PrefetchScalarGridSpec(
                num_scalar_prefetch=2,
                grid=(heads,),
                in_specs=[row_spec(rows), row_spec(half_rows), row_spec(half_rows)] + far_specs,
                out_specs=out_spec(half_rows),
            ),
            compiler_params=params,
            cost_estimate=cost(2 * BLOCK, half_rows, heads * width * (2 * rows + 8 * half_rows + 2 * sum(a.shape[2] for a in far_operands))),
        )(meta, used, q_t, acc1, st1, *far_operands)

        parts = []
        for att in (att_even, att_odd):
            partial_value = jnp.dot(att, out_weight, preferred_element_type=jnp.float32)
            parts.append(lax.psum_scatter(
                partial_value.astype(jnp.bfloat16), "head", scatter_dimension=1, tiled=True
            ))
    else:
        hidx = lax.axis_index("head")
        swap = [(0, 1), (1, 0)]
        received_odd = lax.ppermute(project_half(att_odd, out_weight, 1 - hidx), "head", swap)
        own_odd = project_half(att_odd, out_weight, hidx)
        acc1, st1, own_odd = lax.optimization_barrier((acc1, st1, own_odd))
        att_even = pl.pallas_call(
            functools.partial(far_kernel, levels, per_dev, width, scale),
            out_shape=jax.ShapeDtypeStruct((half_rows, heads * width), queries.dtype),
            grid_spec=pltpu.PrefetchScalarGridSpec(
                num_scalar_prefetch=2,
                grid=(heads,),
                in_specs=[row_spec(rows), row_spec(half_rows), row_spec(half_rows)] + far_specs,
                out_specs=out_spec(half_rows),
            ),
            compiler_params=params,
            cost_estimate=cost(2 * BLOCK, half_rows, heads * width * (2 * rows + 8 * half_rows + 2 * sum(a.shape[2] for a in far_operands))),
        )(meta, used, q_t, acc1, st1, *far_operands)

        received_even = lax.ppermute(project_half(att_even, out_weight, 1 - hidx), "head", swap)
        own_even = project_half(att_even, out_weight, hidx)
        parts = [
            (own.astype(jnp.float32) + got.astype(jnp.float32)).astype(jnp.bfloat16)
            for own, got in ((own_even, received_even), (own_odd, received_odd))
        ]
    even, odd = (p.reshape(per_dev // 2, BLOCK, -1) for p in parts)
    return jnp.stack([even, odd], axis=1).reshape(rows, -1)


def solution(mesh):
    placed = (
        P("ctx", "head", None),
        P("ctx", "head", None),
        P("ctx", "head", None),
        P(),
        P("head", None),
    )
    return jax.shard_map(
        per_device, mesh=mesh, in_specs=placed, out_specs=P("ctx", "head"), check_vma=False
    )
```

```python
import functools
import math

import jax
import jax.numpy as jnp
from jax import lax
from jax.experimental import pallas as pl
from jax.experimental.pallas import tpu as pltpu
from jax.sharding import PartitionSpec as P

BLOCK = 64
WINDOW = 512
NOFF = 5
HEADS_PER_STEP = 4


def from_behind(value, axis, steps):
    count = lax.axis_size(axis)
    initial, last = (max(0, -steps), min(count, count - steps))
    return lax.ppermute(value, axis, [(source, source + steps) for source in range(initial, last)])


def block_scores(q, keys, scale):
    return lax.dot_general(
        q, keys, (((1,), (1,)), ((), ())), preferred_element_type=jnp.float32
    ) * scale


def merge(pieces, m_old, l_old, acc_old):
    top = m_old
    for s, _ in pieces:
        row_max = s.max(axis=1, keepdims=True)
        top = row_max if top is None else jnp.maximum(top, row_max)
    total = None
    summed = None
    for s, v in pieces:
        p = jnp.exp(s - top)
        part_total = p.sum(axis=1, keepdims=True)
        part = jnp.dot(p.astype(jnp.bfloat16), v, preferred_element_type=jnp.float32)
        total = part_total if total is None else total + part_total
        summed = part if summed is None else summed + part
    if m_old is not None:
        alpha = jnp.exp(m_old - top)
        total = total + l_old * alpha
        summed = summed + acc_old * alpha
    return top, total, summed


def pack_stats(m, l, width):
    lane = lax.broadcasted_iota(jnp.int32, (m.shape[0], width), 1)
    return jnp.where(lane == 0, m, jnp.where(lane == 1, l, 0.0))


TILE = 256


class HeadView:
    def __init__(self, ref, head, width=None):
        self.ref, self.head, self.width = ref, head, width

    def _index(self, idx):
        if idx is Ellipsis:
            idx = (slice(None), slice(None))
        if self.width is None:
            return (self.head,) + tuple(idx)
        return (idx[0], pl.ds(self.head * self.width, self.width))

    @property
    def dtype(self):
        return self.ref.dtype

    def __getitem__(self, idx):
        return self.ref[self._index(idx)]

    def __setitem__(self, idx, value):
        self.ref[self._index(idx)] = value


def per_head(body, n_prefetch, n_head_major, n_rows_out, width, heads_per_step):
    def kernel(*refs):
        pre = refs[:n_prefetch]
        rest = refs[n_prefetch:]
        n_major = len(rest) - n_rows_out
        for hh in range(heads_per_step):
            views = [HeadView(r, hh) for r in rest[:n_major]]
            outs = [HeadView(r, hh, width) for r in rest[n_major:]]
            body(*pre, *views, *outs)

    return kernel


def own_kernel(per_dev, width, scale, q_ref, k_ref, v_ref, acc_ref, st_ref):
    neg = jnp.float32(-jnp.inf)
    rows = per_dev * BLOCK
    for lo in range(0, rows, TILE):
        q = q_ref[lo:lo + TILE, :]
        n_own = lo + TILE
        s_o = block_scores(q, k_ref[:n_own, :], scale)
        r_ids = lax.broadcasted_iota(jnp.int32, (TILE, n_own), 0)
        c_ids = lax.broadcasted_iota(jnp.int32, (TILE, n_own), 1)
        s_o = jnp.where(c_ids <= r_ids + lo, s_o, neg)
        m, l, acc = merge([(s_o, v_ref[:n_own, :])], None, None, None)
        acc_ref[lo:lo + TILE, :] = acc
        st_ref[lo:lo + TILE, :] = pack_stats(m, l, width)


def column_map(n_cols, values):
    seg = lax.broadcasted_iota(jnp.int32, (1, n_cols), 1) // BLOCK
    out = jnp.zeros((1, n_cols), jnp.int32)
    for j, value in enumerate(values):
        out = jnp.where(seg == j, value, out)
    return out


def prev_kernel(per_dev, width, scale, meta_ref, used_ref, q_ref, kp_ref, vp_ref, acc_ref, st_ref,
                acc_out, st_out, odd_ref):
    prev_ok = meta_ref[0] > 0
    neg = jnp.float32(-jnp.inf)
    rows = per_dev * BLOCK
    per_tile = TILE // BLOCK
    for lo in range(0, rows, TILE):
        q = q_ref[lo:lo + TILE, :]
        n_prev = rows - lo
        s_p = block_scores(q, kp_ref[lo:, :], scale)
        r_ids = lax.broadcasted_iota(jnp.int32, (TILE, n_prev), 0)
        c_ids = lax.broadcasted_iota(jnp.int32, (TILE, n_prev), 1)
        s_p = jnp.where((c_ids > r_ids) & prev_ok, s_p, neg)
        blocks = range(lo // BLOCK, lo // BLOCK + per_tile)
        starts = [pl.multiple_of(meta_ref[1 + i] * BLOCK, BLOCK) for i in blocks]
        k0 = jnp.concatenate([kp_ref[pl.ds(st, BLOCK), :] for st in starts], axis=0)
        v0 = jnp.concatenate([vp_ref[pl.ds(st, BLOCK), :] for st in starts], axis=0)
        s_f = block_scores(q, k0, scale)
        flags = column_map(TILE, [used_ref[i * NOFF] for i in blocks])
        r_blk = lax.broadcasted_iota(jnp.int32, (TILE, TILE), 0) // BLOCK
        c_blk = lax.broadcasted_iota(jnp.int32, (TILE, TILE), 1) // BLOCK
        s_f = jnp.where((r_blk == c_blk) & (flags > 0), s_f, neg)
        st = st_ref[lo:lo + TILE, :]
        m, l, acc = merge(
            [(s_p, vp_ref[lo:, :]), (s_f, v0)], st[:, 0:1], st[:, 1:2], acc_ref[lo:lo + TILE, :]
        )
        for b, i in enumerate(blocks):
            sl = slice(b * BLOCK, (b + 1) * BLOCK)
            half = (i // 2) * BLOCK
            if i % 2:
                odd_ref[half:half + BLOCK, :] = (acc[sl] / l[sl]).astype(odd_ref.dtype)
            else:
                acc_out[half:half + BLOCK, :] = acc[sl]
                st_out[half:half + BLOCK, :] = pack_stats(m[sl], l[sl], width)


def far_kernel(levels, per_dev, width, scale, meta_ref, used_ref, q_ref, acc_ref, st_ref, *rest):
    far_refs = rest[:-1]
    even_ref = rest[-1]
    neg = jnp.float32(-jnp.inf)
    n_even = per_dev // 2
    q = jnp.concatenate([q_ref[2 * e * BLOCK:(2 * e + 1) * BLOCK, :] for e in range(n_even)], axis=0)
    keys, vals, targets, flags = [], [], [], []
    pos = 0
    for level in levels:
        offset = 2**level
        n_src = 2 if level == 1 else 1
        refs = far_refs[pos:pos + 2 * n_src]
        pos += 2 * n_src
        k_lvl = refs[0][...]
        v_lvl = refs[1][...]
        if n_src == 2:
            odd = meta_ref[1 + per_dev] > 0
            k_lvl = jnp.where(odd, refs[2][...], k_lvl)
            v_lvl = jnp.where(odd, refs[3][...], v_lvl)
        keys.append(k_lvl)
        vals.append(v_lvl)
        for k in range(k_lvl.shape[0] // BLOCK):
            qblock = k * offset
            targets.append(qblock // 2)
            flags.append(used_ref[qblock * NOFF + level])
    k_far = jnp.concatenate(keys, axis=0)
    v_far = jnp.concatenate(vals, axis=0)
    n_keys = k_far.shape[0]
    s_f = block_scores(q, k_far, scale)
    col_target = column_map(n_keys, targets)
    col_flag = column_map(n_keys, flags)
    r_blk = lax.broadcasted_iota(jnp.int32, (n_even * BLOCK, n_keys), 0) // BLOCK
    s_f = jnp.where((r_blk == col_target) & (col_flag > 0), s_f, neg)
    st = st_ref[...]
    m, l, acc = merge([(s_f, v_far)], st[:, 0:1], st[:, 1:2], acc_ref[...])
    even_ref[...] = (acc / l).astype(even_ref.dtype)


def matmul_kernel(sel_ref, a_ref, w_ref, o_ref):
    o_ref[...] = jnp.dot(a_ref[...], w_ref[...], preferred_element_type=jnp.float32).astype(
        o_ref.dtype
    )


def project_half(attended, weight, half, tn=512):
    rows, depth = attended.shape
    cw = weight.shape[1] // 2
    steps = cw // tn
    return pl.pallas_call(
        matmul_kernel,
        out_shape=jax.ShapeDtypeStruct((rows, cw), jnp.bfloat16),
        grid_spec=pltpu.PrefetchScalarGridSpec(
            num_scalar_prefetch=1,
            grid=(steps,),
            in_specs=[
                pl.BlockSpec((rows, depth), lambda j, sel: (0, 0)),
                pl.BlockSpec((depth, tn), lambda j, sel: (0, sel[0] * steps + j)),
            ],
            out_specs=pl.BlockSpec((rows, tn), lambda j, sel: (0, j)),
        ),
        compiler_params=pltpu.CompilerParams(dimension_semantics=("arbitrary",)),
        cost_estimate=pl.CostEstimate(
            flops=2 * rows * depth * cw,
            transcendentals=0,
            bytes_accessed=2 * (rows * depth + depth * cw + rows * cw),
        ),
    )(jnp.reshape(half, (1,)).astype(jnp.int32), attended, weight)


def pick_blocks(kv, local):
    return jnp.concatenate(
        [lax.dynamic_slice_in_dim(kv, local[b] * BLOCK, BLOCK, axis=2) for b in range(local.shape[0])],
        axis=2,
    )


def per_device(queries, keys, values, far_blocks, out_weight):
    rows, heads, width = queries.shape
    per_dev = rows // BLOCK
    device = lax.axis_index("ctx")
    cycle_size = lax.axis_size("ctx")
    scale = 1.0 / math.sqrt(width)
    q_t = jnp.transpose(queries, (1, 0, 2))
    kv_t = jnp.stack([jnp.transpose(keys, (1, 0, 2)), jnp.transpose(values, (1, 0, 2))])
    prev_kv = from_behind(kv_t, "ctx", 1)
    levels = []
    sends = []
    for level in range(1, NOFF):
        offset = 2**level
        if offset >= cycle_size:
            continue
        target = lax.dynamic_slice_in_dim(far_blocks, (device + offset) * per_dev, per_dev, 0)[
            ::offset, level
        ]
        local = jnp.clip(target - device * per_dev, 0, per_dev - 1)
        if level == 1:
            pairs = [(s, s + 2) for s in range(0, cycle_size - 2, 2)]
            nxt = lax.dynamic_slice_in_dim(far_blocks, (device + 1) * per_dev, per_dev, 0)[::2, 1]
            fwd_local = jnp.clip(nxt - (device - 1) * per_dev, 0, per_dev - 1)
        else:
            pairs = [(s, s + offset) for s in range(0, cycle_size - offset)]
        sends.append((pick_blocks(kv_t, local), pairs))
        levels.append(level)
    q_t, kv_t, *operands = lax.optimization_barrier((q_t, kv_t, *[op for op, _ in sends]))
    far_arrays = []
    for (_, pairs), op, level in zip(sends, operands, levels):
        received = lax.ppermute(op, "ctx", pairs)
        far_arrays.append((received, None) if level == 1 else (received,))

    own = lax.dynamic_slice_in_dim(far_blocks, device * per_dev, per_dev, 0)
    query_index = device * per_dev + jnp.arange(per_dev, dtype=jnp.int32)
    used = (own <= (query_index - WINDOW // BLOCK - 1)[:, None]).astype(jnp.int32).reshape(-1)
    pick = jnp.clip(own[:, 0] - (device - 1) * per_dev, 0, per_dev - 1)
    meta = jnp.concatenate(
        [(device > 0).astype(jnp.int32)[None], pick.astype(jnp.int32), (device % 2)[None]]
    )

    hb = math.gcd(heads, HEADS_PER_STEP)
    row_spec = lambda n: pl.BlockSpec((hb, n, width), lambda h, *_: (h, 0, 0))
    out_spec = lambda n: pl.BlockSpec((n, hb * width), lambda h, *_: (0, h))
    k_spec = lambda n: pl.BlockSpec((None, hb, n, width), lambda h, *_: (0, h, 0, 0))
    v_spec = lambda n: pl.BlockSpec((None, hb, n, width), lambda h, *_: (1, h, 0, 0))
    half_rows = rows // 2
    f32 = jnp.float32
    params = pltpu.CompilerParams(dimension_semantics=("arbitrary",))
    state = lambda n: jax.ShapeDtypeStruct((heads, n, width), f32)

    def cost(keys_per_row, n_rows, extra_bytes):
        return pl.CostEstimate(
            flops=4 * n_rows * heads * width * keys_per_row,
            transcendentals=n_rows * heads * keys_per_row,
            bytes_accessed=extra_bytes,
        )

    acc0, st0 = pl.pallas_call(
        per_head(functools.partial(own_kernel, per_dev, width, scale), 0, 5, 0, width, hb),
        out_shape=(state(rows), state(rows)),
        grid=(heads // hb,),
        in_specs=[row_spec(rows), k_spec(rows), v_spec(rows)],
        out_specs=(row_spec(rows), row_spec(rows)),
        compiler_params=params,
        cost_estimate=cost(WINDOW // 2, rows, 2 * heads * rows * width * (3 * 2 + 2 * 4)),
    )(q_t, kv_t, kv_t)

    prev_kv, acc0, st0 = lax.optimization_barrier((prev_kv, acc0, st0))
    if far_arrays and far_arrays[0][1] is None:
        forwarded = lax.ppermute(
            pick_blocks(prev_kv, fwd_local), "ctx",
            [(s, s + 1) for s in range(0, cycle_size - 1, 2)],
        )
        far_arrays[0] = (far_arrays[0][0], forwarded)
    far_specs, far_operands = [], []
    for group in far_arrays:
        for a in group:
            far_specs += [k_spec(a.shape[2]), v_spec(a.shape[2])]
            far_operands += [a, a]
    acc1, st1, att_odd = pl.pallas_call(
        per_head(functools.partial(prev_kernel, per_dev, width, scale), 2, 7, 1, width, hb),
        out_shape=(
            state(half_rows),
            state(half_rows),
            jax.ShapeDtypeStruct((half_rows, heads * width), queries.dtype),
        ),
        grid_spec=pltpu.PrefetchScalarGridSpec(
            num_scalar_prefetch=2,
            grid=(heads // hb,),
            in_specs=[row_spec(rows), k_spec(rows), v_spec(rows), row_spec(rows), row_spec(rows)],
            out_specs=(row_spec(half_rows), row_spec(half_rows), out_spec(half_rows)),
        ),
        compiler_params=params,
        cost_estimate=cost(WINDOW // 2 + BLOCK, rows, heads * rows * width * (3 * 2 + 2 * 4 + 8)),
    )(meta, used, q_t, prev_kv, prev_kv, acc0, st0)

    n_head = lax.axis_size("head")
    if n_head != 2:
        att_even = pl.pallas_call(
            per_head(functools.partial(far_kernel, levels, per_dev, width, scale), 2, 0, 1, width, hb),
            out_shape=jax.ShapeDtypeStruct((half_rows, heads * width), queries.dtype),
            grid_spec=pltpu.PrefetchScalarGridSpec(
                num_scalar_prefetch=2,
                grid=(heads // hb,),
                in_specs=[row_spec(rows), row_spec(half_rows), row_spec(half_rows)] + far_specs,
                out_specs=out_spec(half_rows),
            ),
            compiler_params=params,
            cost_estimate=cost(2 * BLOCK, half_rows, heads * width * (2 * rows + 8 * half_rows + 2 * sum(a.shape[2] for a in far_operands))),
        )(meta, used, q_t, acc1, st1, *far_operands)

        parts = []
        for att in (att_even, att_odd):
            partial_value = jnp.dot(att, out_weight, preferred_element_type=jnp.float32)
            parts.append(lax.psum_scatter(
                partial_value.astype(jnp.bfloat16), "head", scatter_dimension=1, tiled=True
            ))
    else:
        hidx = lax.axis_index("head")
        swap = [(0, 1), (1, 0)]
        received_odd = lax.ppermute(project_half(att_odd, out_weight, 1 - hidx), "head", swap)
        own_odd = project_half(att_odd, out_weight, hidx)
        acc1, st1, own_odd = lax.optimization_barrier((acc1, st1, own_odd))
        att_even = pl.pallas_call(
            per_head(functools.partial(far_kernel, levels, per_dev, width, scale), 2, 0, 1, width, hb),
            out_shape=jax.ShapeDtypeStruct((half_rows, heads * width), queries.dtype),
            grid_spec=pltpu.PrefetchScalarGridSpec(
                num_scalar_prefetch=2,
                grid=(heads // hb,),
                in_specs=[row_spec(rows), row_spec(half_rows), row_spec(half_rows)] + far_specs,
                out_specs=out_spec(half_rows),
            ),
            compiler_params=params,
            cost_estimate=cost(2 * BLOCK, half_rows, heads * width * (2 * rows + 8 * half_rows + 2 * sum(a.shape[2] for a in far_operands))),
        )(meta, used, q_t, acc1, st1, *far_operands)

        received_even = lax.ppermute(project_half(att_even, out_weight, 1 - hidx), "head", swap)
        own_even = project_half(att_even, out_weight, hidx)
        parts = [
            (own.astype(jnp.float32) + got.astype(jnp.float32)).astype(jnp.bfloat16)
            for own, got in ((own_even, received_even), (own_odd, received_odd))
        ]
    even, odd = (p.reshape(per_dev // 2, BLOCK, -1) for p in parts)
    return jnp.stack([even, odd], axis=1).reshape(rows, -1)


def solution(mesh):
    placed = (
        P("ctx", "head", None),
        P("ctx", "head", None),
        P("ctx", "head", None),
        P(),
        P("head", None),
    )
    return jax.shard_map(
        per_device, mesh=mesh, in_specs=placed, out_specs=P("ctx", "head"), check_vma=False
    )
```

```python
import functools
import math

import jax
import jax.numpy as jnp
from jax import lax
from jax.experimental import pallas as pl
from jax.experimental.pallas import tpu as pltpu
from jax.sharding import PartitionSpec as P

BLOCK = 64
WINDOW = 512
NOFF = 5
HEADS_PER_STEP = 4


def from_behind(value, axis, steps):
    count = lax.axis_size(axis)
    initial, last = (max(0, -steps), min(count, count - steps))
    return lax.ppermute(value, axis, [(source, source + steps) for source in range(initial, last)])


def block_scores(q, keys, scale):
    return lax.dot_general(
        q, keys, (((1,), (1,)), ((), ())), preferred_element_type=jnp.float32
    ) * scale


def merge(pieces, m_old, l_old, acc_old):
    top = m_old
    for s, _ in pieces:
        row_max = s.max(axis=1, keepdims=True)
        top = row_max if top is None else jnp.maximum(top, row_max)
    total = None
    summed = None
    for s, v in pieces:
        p = jnp.exp(s - top)
        part_total = p.sum(axis=1, keepdims=True)
        part = jnp.dot(p.astype(jnp.bfloat16), v, preferred_element_type=jnp.float32)
        total = part_total if total is None else total + part_total
        summed = part if summed is None else summed + part
    if m_old is not None:
        alpha = jnp.exp(m_old - top)
        total = total + l_old * alpha
        summed = summed + acc_old * alpha
    return top, total, summed


def pack_stats(m, l, width):
    lane = lax.broadcasted_iota(jnp.int32, (m.shape[0], width), 1)
    return jnp.where(lane == 0, m, jnp.where(lane == 1, l, 0.0))


TILE = 256


class HeadView:
    def __init__(self, ref, head, width=None):
        self.ref, self.head, self.width = ref, head, width

    def _index(self, idx):
        if idx is Ellipsis:
            idx = (slice(None), slice(None))
        if self.width is None:
            return (self.head,) + tuple(idx)
        return (idx[0], pl.ds(self.head * self.width, self.width))

    @property
    def dtype(self):
        return self.ref.dtype

    def __getitem__(self, idx):
        return self.ref[self._index(idx)]

    def __setitem__(self, idx, value):
        self.ref[self._index(idx)] = value


def per_head(body, n_prefetch, n_head_major, n_rows_out, width, heads_per_step):
    def kernel(*refs):
        pre = refs[:n_prefetch]
        rest = refs[n_prefetch:]
        n_major = len(rest) - n_rows_out
        for hh in range(heads_per_step):
            views = [HeadView(r, hh) for r in rest[:n_major]]
            outs = [HeadView(r, hh, width) for r in rest[n_major:]]
            body(*pre, *views, *outs)

    return kernel


def own_kernel(per_dev, width, scale, q_ref, k_ref, v_ref, acc_ref, st_ref):
    neg = jnp.float32(-jnp.inf)
    rows = per_dev * BLOCK
    for lo in range(0, rows, TILE):
        q = q_ref[lo:lo + TILE, :]
        n_own = lo + TILE
        s_o = block_scores(q, k_ref[:n_own, :], scale)
        r_ids = lax.broadcasted_iota(jnp.int32, (TILE, n_own), 0)
        c_ids = lax.broadcasted_iota(jnp.int32, (TILE, n_own), 1)
        s_o = jnp.where(c_ids <= r_ids + lo, s_o, neg)
        m, l, acc = merge([(s_o, v_ref[:n_own, :])], None, None, None)
        acc_ref[lo:lo + TILE, :] = acc
        st_ref[lo:lo + TILE, :] = pack_stats(m, l, width)


def column_map(n_cols, values):
    seg = lax.broadcasted_iota(jnp.int32, (1, n_cols), 1) // BLOCK
    out = jnp.zeros((1, n_cols), jnp.int32)
    for j, value in enumerate(values):
        out = jnp.where(seg == j, value, out)
    return out


def prev_kernel(per_dev, width, scale, meta_ref, used_ref, q_ref, kp_ref, vp_ref, acc_ref, st_ref,
                acc_out, st_out, odd_ref):
    prev_ok = meta_ref[0] > 0
    neg = jnp.float32(-jnp.inf)
    rows = per_dev * BLOCK
    per_tile = TILE // BLOCK
    for lo in range(0, rows, TILE):
        q = q_ref[lo:lo + TILE, :]
        n_prev = rows - lo
        s_p = block_scores(q, kp_ref[lo:, :], scale)
        r_ids = lax.broadcasted_iota(jnp.int32, (TILE, n_prev), 0)
        c_ids = lax.broadcasted_iota(jnp.int32, (TILE, n_prev), 1)
        s_p = jnp.where((c_ids > r_ids) & prev_ok, s_p, neg)
        blocks = range(lo // BLOCK, lo // BLOCK + per_tile)
        starts = [pl.multiple_of(meta_ref[1 + i] * BLOCK, BLOCK) for i in blocks]
        k0 = jnp.concatenate([kp_ref[pl.ds(st, BLOCK), :] for st in starts], axis=0)
        v0 = jnp.concatenate([vp_ref[pl.ds(st, BLOCK), :] for st in starts], axis=0)
        s_f = block_scores(q, k0, scale)
        flags = column_map(TILE, [used_ref[i * NOFF] for i in blocks])
        r_blk = lax.broadcasted_iota(jnp.int32, (TILE, TILE), 0) // BLOCK
        c_blk = lax.broadcasted_iota(jnp.int32, (TILE, TILE), 1) // BLOCK
        s_f = jnp.where((r_blk == c_blk) & (flags > 0), s_f, neg)
        st = st_ref[lo:lo + TILE, :]
        m, l, acc = merge(
            [(s_p, vp_ref[lo:, :]), (s_f, v0)], st[:, 0:1], st[:, 1:2], acc_ref[lo:lo + TILE, :]
        )
        for b, i in enumerate(blocks):
            sl = slice(b * BLOCK, (b + 1) * BLOCK)
            half = (i // 2) * BLOCK
            if i % 2:
                odd_ref[half:half + BLOCK, :] = (acc[sl] / l[sl]).astype(odd_ref.dtype)
            else:
                acc_out[half:half + BLOCK, :] = acc[sl]
                st_out[half:half + BLOCK, :] = pack_stats(m[sl], l[sl], width)


def far_kernel(levels, per_dev, width, scale, meta_ref, used_ref, q_ref, acc_ref, st_ref, *rest):
    far_refs = rest[:-1]
    even_ref = rest[-1]
    neg = jnp.float32(-jnp.inf)
    n_even = per_dev // 2
    q = jnp.concatenate([q_ref[2 * e * BLOCK:(2 * e + 1) * BLOCK, :] for e in range(n_even)], axis=0)
    keys, vals, targets, flags = [], [], [], []
    pos = 0
    for level in levels:
        offset = 2**level
        n_src = 2 if level == 1 else 1
        refs = far_refs[pos:pos + 2 * n_src]
        pos += 2 * n_src
        k_lvl = refs[0][...]
        v_lvl = refs[1][...]
        if n_src == 2:
            odd = meta_ref[1 + per_dev] > 0
            k_lvl = jnp.where(odd, refs[2][...], k_lvl)
            v_lvl = jnp.where(odd, refs[3][...], v_lvl)
        keys.append(k_lvl)
        vals.append(v_lvl)
        for k in range(k_lvl.shape[0] // BLOCK):
            qblock = k * offset
            targets.append(qblock // 2)
            flags.append(used_ref[qblock * NOFF + level])
    k_far = jnp.concatenate(keys, axis=0)
    v_far = jnp.concatenate(vals, axis=0)
    n_keys = k_far.shape[0]
    s_f = block_scores(q, k_far, scale)
    col_target = column_map(n_keys, targets)
    col_flag = column_map(n_keys, flags)
    r_blk = lax.broadcasted_iota(jnp.int32, (n_even * BLOCK, n_keys), 0) // BLOCK
    s_f = jnp.where((r_blk == col_target) & (col_flag > 0), s_f, neg)
    st = st_ref[...]
    m, l, acc = merge([(s_f, v_far)], st[:, 0:1], st[:, 1:2], acc_ref[...])
    even_ref[...] = (acc / l).astype(even_ref.dtype)


def matmul_kernel(sel_ref, a_ref, w_ref, o_ref):
    o_ref[...] = jnp.dot(a_ref[...], w_ref[...], preferred_element_type=jnp.float32).astype(
        o_ref.dtype
    )


def project_half(attended, weight, half, tn=512):
    rows, depth = attended.shape
    cw = weight.shape[1] // 2
    steps = cw // tn
    return pl.pallas_call(
        matmul_kernel,
        out_shape=jax.ShapeDtypeStruct((rows, cw), jnp.bfloat16),
        grid_spec=pltpu.PrefetchScalarGridSpec(
            num_scalar_prefetch=1,
            grid=(steps,),
            in_specs=[
                pl.BlockSpec((rows, depth), lambda j, sel: (0, 0)),
                pl.BlockSpec((depth, tn), lambda j, sel: (0, sel[0] * steps + j)),
            ],
            out_specs=pl.BlockSpec((rows, tn), lambda j, sel: (0, j)),
        ),
        compiler_params=pltpu.CompilerParams(dimension_semantics=("arbitrary",)),
        cost_estimate=pl.CostEstimate(
            flops=2 * rows * depth * cw,
            transcendentals=0,
            bytes_accessed=2 * (rows * depth + depth * cw + rows * cw),
        ),
    )(jnp.reshape(half, (1,)).astype(jnp.int32), attended, weight)


def pick_blocks(kv, local):
    return jnp.concatenate(
        [lax.dynamic_slice_in_dim(kv, local[b] * BLOCK, BLOCK, axis=2) for b in range(local.shape[0])],
        axis=2,
    )


def per_device(queries, keys, values, far_blocks, out_weight):
    rows, heads, width = queries.shape
    per_dev = rows // BLOCK
    device = lax.axis_index("ctx")
    cycle_size = lax.axis_size("ctx")
    scale = 1.0 / math.sqrt(width)
    q_t = jnp.transpose(queries, (1, 0, 2))
    kv_t = jnp.stack([jnp.transpose(keys, (1, 0, 2)), jnp.transpose(values, (1, 0, 2))])
    prev_kv = from_behind(kv_t, "ctx", 1)
    levels = []
    sends = []
    for level in range(1, NOFF):
        offset = 2**level
        if offset >= cycle_size:
            continue
        target = lax.dynamic_slice_in_dim(far_blocks, (device + offset) * per_dev, per_dev, 0)[
            ::offset, level
        ]
        local = jnp.clip(target - device * per_dev, 0, per_dev - 1)
        if level == 1:
            pairs = [(s, s + 2) for s in range(0, cycle_size - 2, 2)]
            nxt = lax.dynamic_slice_in_dim(far_blocks, (device + 1) * per_dev, per_dev, 0)[::2, 1]
            fwd_local = jnp.clip(nxt - (device - 1) * per_dev, 0, per_dev - 1)
        else:
            pairs = [(s, s + offset) for s in range(0, cycle_size - offset)]
        sends.append((pick_blocks(kv_t, local), pairs))
        levels.append(level)
    q_t, kv_t, *operands = lax.optimization_barrier((q_t, kv_t, *[op for op, _ in sends]))
    far_arrays = []
    for (_, pairs), op, level in zip(sends, operands, levels):
        if level == 1:
            far_arrays.append((op, pairs))
        else:
            far_arrays.append((lax.ppermute(op, "ctx", pairs),))

    own = lax.dynamic_slice_in_dim(far_blocks, device * per_dev, per_dev, 0)
    query_index = device * per_dev + jnp.arange(per_dev, dtype=jnp.int32)
    used = (own <= (query_index - WINDOW // BLOCK - 1)[:, None]).astype(jnp.int32).reshape(-1)
    pick = jnp.clip(own[:, 0] - (device - 1) * per_dev, 0, per_dev - 1)
    meta = jnp.concatenate(
        [(device > 0).astype(jnp.int32)[None], pick.astype(jnp.int32), (device % 2)[None]]
    )

    hb = math.gcd(heads, HEADS_PER_STEP)
    row_spec = lambda n: pl.BlockSpec((hb, n, width), lambda h, *_: (h, 0, 0))
    out_spec = lambda n: pl.BlockSpec((n, hb * width), lambda h, *_: (0, h))
    k_spec = lambda n: pl.BlockSpec((None, hb, n, width), lambda h, *_: (0, h, 0, 0))
    v_spec = lambda n: pl.BlockSpec((None, hb, n, width), lambda h, *_: (1, h, 0, 0))
    half_rows = rows // 2
    f32 = jnp.float32
    params = pltpu.CompilerParams(dimension_semantics=("arbitrary",))
    state = lambda n: jax.ShapeDtypeStruct((heads, n, width), f32)

    def cost(keys_per_row, n_rows, extra_bytes):
        return pl.CostEstimate(
            flops=4 * n_rows * heads * width * keys_per_row,
            transcendentals=n_rows * heads * keys_per_row,
            bytes_accessed=extra_bytes,
        )

    acc0, st0 = pl.pallas_call(
        per_head(functools.partial(own_kernel, per_dev, width, scale), 0, 5, 0, width, hb),
        out_shape=(state(rows), state(rows)),
        grid=(heads // hb,),
        in_specs=[row_spec(rows), k_spec(rows), v_spec(rows)],
        out_specs=(row_spec(rows), row_spec(rows)),
        compiler_params=params,
        cost_estimate=cost(WINDOW // 2, rows, 2 * heads * rows * width * (3 * 2 + 2 * 4)),
    )(q_t, kv_t, kv_t)

    if levels and levels[0] == 1:
        direct_op, direct_pairs = far_arrays[0]
        prev_kv, acc0, st0, direct_op = lax.optimization_barrier((prev_kv, acc0, st0, direct_op))
        direct = lax.ppermute(direct_op, "ctx", direct_pairs)
        forwarded = lax.ppermute(
            pick_blocks(prev_kv, fwd_local), "ctx",
            [(s, s + 1) for s in range(0, cycle_size - 1, 2)],
        )
        far_arrays[0] = (direct, forwarded)
    else:
        prev_kv, acc0, st0 = lax.optimization_barrier((prev_kv, acc0, st0))
    far_specs, far_operands = [], []
    for group in far_arrays:
        for a in group:
            far_specs += [k_spec(a.shape[2]), v_spec(a.shape[2])]
            far_operands += [a, a]
    acc1, st1, att_odd = pl.pallas_call(
        per_head(functools.partial(prev_kernel, per_dev, width, scale), 2, 7, 1, width, hb),
        out_shape=(
            state(half_rows),
            state(half_rows),
            jax.ShapeDtypeStruct((half_rows, heads * width), queries.dtype),
        ),
        grid_spec=pltpu.PrefetchScalarGridSpec(
            num_scalar_prefetch=2,
            grid=(heads // hb,),
            in_specs=[row_spec(rows), k_spec(rows), v_spec(rows), row_spec(rows), row_spec(rows)],
            out_specs=(row_spec(half_rows), row_spec(half_rows), out_spec(half_rows)),
        ),
        compiler_params=params,
        cost_estimate=cost(WINDOW // 2 + BLOCK, rows, heads * rows * width * (3 * 2 + 2 * 4 + 8)),
    )(meta, used, q_t, prev_kv, prev_kv, acc0, st0)

    n_head = lax.axis_size("head")
    if n_head != 2:
        att_even = pl.pallas_call(
            per_head(functools.partial(far_kernel, levels, per_dev, width, scale), 2, 0, 1, width, hb),
            out_shape=jax.ShapeDtypeStruct((half_rows, heads * width), queries.dtype),
            grid_spec=pltpu.PrefetchScalarGridSpec(
                num_scalar_prefetch=2,
                grid=(heads // hb,),
                in_specs=[row_spec(rows), row_spec(half_rows), row_spec(half_rows)] + far_specs,
                out_specs=out_spec(half_rows),
            ),
            compiler_params=params,
            cost_estimate=cost(2 * BLOCK, half_rows, heads * width * (2 * rows + 8 * half_rows + 2 * sum(a.shape[2] for a in far_operands))),
        )(meta, used, q_t, acc1, st1, *far_operands)

        parts = []
        for att in (att_even, att_odd):
            partial_value = jnp.dot(att, out_weight, preferred_element_type=jnp.float32)
            parts.append(lax.psum_scatter(
                partial_value.astype(jnp.bfloat16), "head", scatter_dimension=1, tiled=True
            ))
    else:
        hidx = lax.axis_index("head")
        swap = [(0, 1), (1, 0)]
        received_odd = lax.ppermute(project_half(att_odd, out_weight, 1 - hidx), "head", swap)
        own_odd = project_half(att_odd, out_weight, hidx)
        acc1, st1, own_odd = lax.optimization_barrier((acc1, st1, own_odd))
        att_even = pl.pallas_call(
            per_head(functools.partial(far_kernel, levels, per_dev, width, scale), 2, 0, 1, width, hb),
            out_shape=jax.ShapeDtypeStruct((half_rows, heads * width), queries.dtype),
            grid_spec=pltpu.PrefetchScalarGridSpec(
                num_scalar_prefetch=2,
                grid=(heads // hb,),
                in_specs=[row_spec(rows), row_spec(half_rows), row_spec(half_rows)] + far_specs,
                out_specs=out_spec(half_rows),
            ),
            compiler_params=params,
            cost_estimate=cost(2 * BLOCK, half_rows, heads * width * (2 * rows + 8 * half_rows + 2 * sum(a.shape[2] for a in far_operands))),
        )(meta, used, q_t, acc1, st1, *far_operands)

        received_even = lax.ppermute(project_half(att_even, out_weight, 1 - hidx), "head", swap)
        own_even = project_half(att_even, out_weight, hidx)
        parts = [
            (own.astype(jnp.float32) + got.astype(jnp.float32)).astype(jnp.bfloat16)
            for own, got in ((own_even, received_even), (own_odd, received_odd))
        ]
    even, odd = (p.reshape(per_dev // 2, BLOCK, -1) for p in parts)
    return jnp.stack([even, odd], axis=1).reshape(rows, -1)


def solution(mesh):
    placed = (
        P("ctx", "head", None),
        P("ctx", "head", None),
        P("ctx", "head", None),
        P(),
        P("head", None),
    )
    return jax.shard_map(
        per_device, mesh=mesh, in_specs=placed, out_specs=P("ctx", "head"), check_vma=False
    )
```

```python
import functools
import math

import jax
import jax.numpy as jnp
from jax import lax
from jax.experimental import pallas as pl
from jax.experimental.pallas import tpu as pltpu
from jax.sharding import PartitionSpec as P

BLOCK = 64
WINDOW = 512
NOFF = 5
HEADS_PER_STEP = 4


def from_behind(value, axis, steps):
    count = lax.axis_size(axis)
    initial, last = (max(0, -steps), min(count, count - steps))
    return lax.ppermute(value, axis, [(source, source + steps) for source in range(initial, last)])


def block_scores(q, keys, scale):
    return lax.dot_general(
        q, keys, (((1,), (1,)), ((), ())), preferred_element_type=jnp.float32
    ) * scale


def merge(pieces, m_old, l_old, acc_old):
    top = m_old
    for s, _ in pieces:
        row_max = s.max(axis=1, keepdims=True)
        top = row_max if top is None else jnp.maximum(top, row_max)
    total = None
    summed = None
    for s, v in pieces:
        p = jnp.exp(s - top)
        part_total = p.sum(axis=1, keepdims=True)
        part = jnp.dot(p.astype(jnp.bfloat16), v, preferred_element_type=jnp.float32)
        total = part_total if total is None else total + part_total
        summed = part if summed is None else summed + part
    if m_old is not None:
        alpha = jnp.exp(m_old - top)
        total = total + l_old * alpha
        summed = summed + acc_old * alpha
    return top, total, summed


def pack_stats(m, l, width):
    lane = lax.broadcasted_iota(jnp.int32, (m.shape[0], width), 1)
    return jnp.where(lane == 0, m, jnp.where(lane == 1, l, 0.0))


TILE = 256


class HeadView:
    def __init__(self, ref, head, width=None):
        self.ref, self.head, self.width = ref, head, width

    def _index(self, idx):
        if idx is Ellipsis:
            idx = (slice(None), slice(None))
        if self.width is None:
            return (self.head,) + tuple(idx)
        return (idx[0], pl.ds(self.head * self.width, self.width))

    @property
    def dtype(self):
        return self.ref.dtype

    def __getitem__(self, idx):
        return self.ref[self._index(idx)]

    def __setitem__(self, idx, value):
        self.ref[self._index(idx)] = value


def per_head(body, n_prefetch, n_head_major, n_rows_out, width, heads_per_step):
    def kernel(*refs):
        pre = refs[:n_prefetch]
        rest = refs[n_prefetch:]
        n_major = len(rest) - n_rows_out
        for hh in range(heads_per_step):
            views = [HeadView(r, hh) for r in rest[:n_major]]
            outs = [HeadView(r, hh, width) for r in rest[n_major:]]
            body(*pre, *views, *outs)

    return kernel


def own_kernel(per_dev, width, scale, q_ref, k_ref, v_ref, acc_ref, st_ref):
    neg = jnp.float32(-jnp.inf)
    rows = per_dev * BLOCK
    for lo in range(0, rows, TILE):
        q = q_ref[lo:lo + TILE, :]
        n_own = lo + TILE
        s_o = block_scores(q, k_ref[:n_own, :], scale)
        r_ids = lax.broadcasted_iota(jnp.int32, (TILE, n_own), 0)
        c_ids = lax.broadcasted_iota(jnp.int32, (TILE, n_own), 1)
        s_o = jnp.where(c_ids <= r_ids + lo, s_o, neg)
        m, l, acc = merge([(s_o, v_ref[:n_own, :])], None, None, None)
        acc_ref[lo:lo + TILE, :] = acc
        st_ref[lo:lo + TILE, :] = pack_stats(m, l, width)


def column_map(n_cols, values):
    seg = lax.broadcasted_iota(jnp.int32, (1, n_cols), 1) // BLOCK
    out = jnp.zeros((1, n_cols), jnp.int32)
    for j, value in enumerate(values):
        out = jnp.where(seg == j, value, out)
    return out


def prev_kernel(per_dev, width, scale, meta_ref, used_ref, q_ref, kp_ref, vp_ref, acc_ref, st_ref,
                acc_out, st_out, odd_ref):
    prev_ok = meta_ref[0] > 0
    neg = jnp.float32(-jnp.inf)
    rows = per_dev * BLOCK
    per_tile = TILE // BLOCK
    for lo in range(0, rows, TILE):
        q = q_ref[lo:lo + TILE, :]
        n_prev = rows - lo
        s_p = block_scores(q, kp_ref[lo:, :], scale)
        r_ids = lax.broadcasted_iota(jnp.int32, (TILE, n_prev), 0)
        c_ids = lax.broadcasted_iota(jnp.int32, (TILE, n_prev), 1)
        s_p = jnp.where((c_ids > r_ids) & prev_ok, s_p, neg)
        blocks = range(lo // BLOCK, lo // BLOCK + per_tile)
        starts = [pl.multiple_of(meta_ref[1 + i] * BLOCK, BLOCK) for i in blocks]
        k0 = jnp.concatenate([kp_ref[pl.ds(st, BLOCK), :] for st in starts], axis=0)
        v0 = jnp.concatenate([vp_ref[pl.ds(st, BLOCK), :] for st in starts], axis=0)
        s_f = block_scores(q, k0, scale)
        flags = column_map(TILE, [used_ref[i * NOFF] for i in blocks])
        r_blk = lax.broadcasted_iota(jnp.int32, (TILE, TILE), 0) // BLOCK
        c_blk = lax.broadcasted_iota(jnp.int32, (TILE, TILE), 1) // BLOCK
        s_f = jnp.where((r_blk == c_blk) & (flags > 0), s_f, neg)
        st = st_ref[lo:lo + TILE, :]
        m, l, acc = merge(
            [(s_p, vp_ref[lo:, :]), (s_f, v0)], st[:, 0:1], st[:, 1:2], acc_ref[lo:lo + TILE, :]
        )
        for b, i in enumerate(blocks):
            sl = slice(b * BLOCK, (b + 1) * BLOCK)
            half = (i // 2) * BLOCK
            if i % 2:
                odd_ref[half:half + BLOCK, :] = (acc[sl] / l[sl]).astype(odd_ref.dtype)
            else:
                acc_out[half:half + BLOCK, :] = acc[sl]
                st_out[half:half + BLOCK, :] = pack_stats(m[sl], l[sl], width)


def far_kernel(levels, per_dev, width, scale, meta_ref, used_ref, q_ref, acc_ref, st_ref, *rest):
    far_refs = rest[:-1]
    even_ref = rest[-1]
    neg = jnp.float32(-jnp.inf)
    n_even = per_dev // 2
    q = jnp.concatenate([q_ref[2 * e * BLOCK:(2 * e + 1) * BLOCK, :] for e in range(n_even)], axis=0)
    keys, vals, targets, flags = [], [], [], []
    pos = 0
    for level in levels:
        offset = 2**level
        refs = far_refs[pos:pos + 4]
        pos += 4
        second = meta_ref[(1 if level == 1 else 2) + per_dev] > 0
        k_lvl = jnp.where(second, refs[2][...], refs[0][...])
        v_lvl = jnp.where(second, refs[3][...], refs[1][...])
        keys.append(k_lvl)
        vals.append(v_lvl)
        for k in range(k_lvl.shape[0] // BLOCK):
            qblock = k * offset
            targets.append(qblock // 2)
            flags.append(used_ref[qblock * NOFF + level])
    k_far = jnp.concatenate(keys, axis=0)
    v_far = jnp.concatenate(vals, axis=0)
    n_keys = k_far.shape[0]
    s_f = block_scores(q, k_far, scale)
    col_target = column_map(n_keys, targets)
    col_flag = column_map(n_keys, flags)
    r_blk = lax.broadcasted_iota(jnp.int32, (n_even * BLOCK, n_keys), 0) // BLOCK
    s_f = jnp.where((r_blk == col_target) & (col_flag > 0), s_f, neg)
    st = st_ref[...]
    m, l, acc = merge([(s_f, v_far)], st[:, 0:1], st[:, 1:2], acc_ref[...])
    even_ref[...] = (acc / l).astype(even_ref.dtype)


def matmul_kernel(sel_ref, a_ref, w_ref, o_ref):
    o_ref[...] = jnp.dot(a_ref[...], w_ref[...], preferred_element_type=jnp.float32).astype(
        o_ref.dtype
    )


def project_half(attended, weight, half, tn=512):
    rows, depth = attended.shape
    cw = weight.shape[1] // 2
    steps = cw // tn
    return pl.pallas_call(
        matmul_kernel,
        out_shape=jax.ShapeDtypeStruct((rows, cw), jnp.bfloat16),
        grid_spec=pltpu.PrefetchScalarGridSpec(
            num_scalar_prefetch=1,
            grid=(steps,),
            in_specs=[
                pl.BlockSpec((rows, depth), lambda j, sel: (0, 0)),
                pl.BlockSpec((depth, tn), lambda j, sel: (0, sel[0] * steps + j)),
            ],
            out_specs=pl.BlockSpec((rows, tn), lambda j, sel: (0, j)),
        ),
        compiler_params=pltpu.CompilerParams(dimension_semantics=("arbitrary",)),
        cost_estimate=pl.CostEstimate(
            flops=2 * rows * depth * cw,
            transcendentals=0,
            bytes_accessed=2 * (rows * depth + depth * cw + rows * cw),
        ),
    )(jnp.reshape(half, (1,)).astype(jnp.int32), attended, weight)


def pick_blocks(kv, local):
    return jnp.concatenate(
        [lax.dynamic_slice_in_dim(kv, local[b] * BLOCK, BLOCK, axis=2) for b in range(local.shape[0])],
        axis=2,
    )


def per_device(queries, keys, values, far_blocks, out_weight):
    rows, heads, width = queries.shape
    per_dev = rows // BLOCK
    device = lax.axis_index("ctx")
    cycle_size = lax.axis_size("ctx")
    scale = 1.0 / math.sqrt(width)
    q_t = jnp.transpose(queries, (1, 0, 2))
    kv_t = jnp.stack([jnp.transpose(keys, (1, 0, 2)), jnp.transpose(values, (1, 0, 2))])
    prev_kv = from_behind(kv_t, "ctx", 1)
    levels = []
    sends = []
    for level in range(1, NOFF):
        offset = 2**level
        if offset >= cycle_size:
            continue
        target = lax.dynamic_slice_in_dim(far_blocks, (device + offset) * per_dev, per_dev, 0)[
            ::offset, level
        ]
        local = jnp.clip(target - device * per_dev, 0, per_dev - 1)
        if level == 1:
            pairs = [(s, s + 2) for s in range(0, cycle_size - 2, 2)]
            nxt = lax.dynamic_slice_in_dim(far_blocks, (device + 1) * per_dev, per_dev, 0)[::2, 1]
            fwd_local = jnp.clip(nxt - (device - 1) * per_dev, 0, per_dev - 1)
        else:
            pairs = [(s, s + offset) for s in range(0, cycle_size - offset)]
        sends.append((pick_blocks(kv_t, local), pairs))
        levels.append(level)
    q_t, kv_t, *operands = lax.optimization_barrier((q_t, kv_t, *[op for op, _ in sends]))
    far_arrays = []
    early_far = []
    late_far = []
    for (_, pairs), op, level in zip(sends, operands, levels):
        if level == 1:
            far_arrays.append((op, pairs))
        else:
            soon = [(a, b) for a, b in pairs if (b // 2) % 2 == 1]
            later = [(a, b) for a, b in pairs if (b // 2) % 2 == 0]
            early_far.append(lax.ppermute(op, "ctx", soon))
            late_far.append((op, later))
            far_arrays.append(None)

    own = lax.dynamic_slice_in_dim(far_blocks, device * per_dev, per_dev, 0)
    query_index = device * per_dev + jnp.arange(per_dev, dtype=jnp.int32)
    used = (own <= (query_index - WINDOW // BLOCK - 1)[:, None]).astype(jnp.int32).reshape(-1)
    pick = jnp.clip(own[:, 0] - (device - 1) * per_dev, 0, per_dev - 1)
    meta = jnp.concatenate(
        [(device > 0).astype(jnp.int32)[None], pick.astype(jnp.int32), (device % 2)[None],
         ((device // 2) % 2)[None]]
    )

    hb = math.gcd(heads, HEADS_PER_STEP)
    row_spec = lambda n: pl.BlockSpec((hb, n, width), lambda h, *_: (h, 0, 0))
    out_spec = lambda n: pl.BlockSpec((n, hb * width), lambda h, *_: (0, h))
    k_spec = lambda n: pl.BlockSpec((None, hb, n, width), lambda h, *_: (0, h, 0, 0))
    v_spec = lambda n: pl.BlockSpec((None, hb, n, width), lambda h, *_: (1, h, 0, 0))
    half_rows = rows // 2
    f32 = jnp.float32
    params = pltpu.CompilerParams(dimension_semantics=("arbitrary",))
    state = lambda n: jax.ShapeDtypeStruct((heads, n, width), f32)

    def cost(keys_per_row, n_rows, extra_bytes):
        return pl.CostEstimate(
            flops=4 * n_rows * heads * width * keys_per_row,
            transcendentals=n_rows * heads * keys_per_row,
            bytes_accessed=extra_bytes,
        )

    acc0, st0 = pl.pallas_call(
        per_head(functools.partial(own_kernel, per_dev, width, scale), 0, 5, 0, width, hb),
        out_shape=(state(rows), state(rows)),
        grid=(heads // hb,),
        in_specs=[row_spec(rows), k_spec(rows), v_spec(rows)],
        out_specs=(row_spec(rows), row_spec(rows)),
        compiler_params=params,
        cost_estimate=cost(WINDOW // 2, rows, 2 * heads * rows * width * (3 * 2 + 2 * 4)),
    )(q_t, kv_t, kv_t)

    late_ops = [op for op, _ in late_far]
    direct_op = [far_arrays[0][0]] if levels and levels[0] == 1 else []
    prev_kv, acc0, st0, early_far, late_ops, direct_op = lax.optimization_barrier(
        (prev_kv, acc0, st0, early_far, late_ops, direct_op)
    )
    late = iter(zip(early_far, late_ops, [p for _, p in late_far]))
    for index, level in enumerate(levels):
        if level == 1:
            direct = lax.ppermute(direct_op[0], "ctx", far_arrays[0][1])
            forwarded = lax.ppermute(
                pick_blocks(prev_kv, fwd_local), "ctx",
                [(s, s + 1) for s in range(0, cycle_size - 1, 2)],
            )
            far_arrays[index] = (direct, forwarded)
        else:
            got_early, op, pairs = next(late)
            far_arrays[index] = (lax.ppermute(op, "ctx", pairs), got_early)
    far_specs, far_operands = [], []
    for group in far_arrays:
        for a in group:
            far_specs += [k_spec(a.shape[2]), v_spec(a.shape[2])]
            far_operands += [a, a]
    acc1, st1, att_odd = pl.pallas_call(
        per_head(functools.partial(prev_kernel, per_dev, width, scale), 2, 7, 1, width, hb),
        out_shape=(
            state(half_rows),
            state(half_rows),
            jax.ShapeDtypeStruct((half_rows, heads * width), queries.dtype),
        ),
        grid_spec=pltpu.PrefetchScalarGridSpec(
            num_scalar_prefetch=2,
            grid=(heads // hb,),
            in_specs=[row_spec(rows), k_spec(rows), v_spec(rows), row_spec(rows), row_spec(rows)],
            out_specs=(row_spec(half_rows), row_spec(half_rows), out_spec(half_rows)),
        ),
        compiler_params=params,
        cost_estimate=cost(WINDOW // 2 + BLOCK, rows, heads * rows * width * (3 * 2 + 2 * 4 + 8)),
    )(meta, used, q_t, prev_kv, prev_kv, acc0, st0)

    n_head = lax.axis_size("head")
    if n_head != 2:
        att_even = pl.pallas_call(
            per_head(functools.partial(far_kernel, levels, per_dev, width, scale), 2, 0, 1, width, hb),
            out_shape=jax.ShapeDtypeStruct((half_rows, heads * width), queries.dtype),
            grid_spec=pltpu.PrefetchScalarGridSpec(
                num_scalar_prefetch=2,
                grid=(heads // hb,),
                in_specs=[row_spec(rows), row_spec(half_rows), row_spec(half_rows)] + far_specs,
                out_specs=out_spec(half_rows),
            ),
            compiler_params=params,
            cost_estimate=cost(2 * BLOCK, half_rows, heads * width * (2 * rows + 8 * half_rows + 2 * sum(a.shape[2] for a in far_operands))),
        )(meta, used, q_t, acc1, st1, *far_operands)

        parts = []
        for att in (att_even, att_odd):
            partial_value = jnp.dot(att, out_weight, preferred_element_type=jnp.float32)
            parts.append(lax.psum_scatter(
                partial_value.astype(jnp.bfloat16), "head", scatter_dimension=1, tiled=True
            ))
    else:
        hidx = lax.axis_index("head")
        swap = [(0, 1), (1, 0)]
        received_odd = lax.ppermute(project_half(att_odd, out_weight, 1 - hidx), "head", swap)
        own_odd = project_half(att_odd, out_weight, hidx)
        acc1, st1, own_odd = lax.optimization_barrier((acc1, st1, own_odd))
        att_even = pl.pallas_call(
            per_head(functools.partial(far_kernel, levels, per_dev, width, scale), 2, 0, 1, width, hb),
            out_shape=jax.ShapeDtypeStruct((half_rows, heads * width), queries.dtype),
            grid_spec=pltpu.PrefetchScalarGridSpec(
                num_scalar_prefetch=2,
                grid=(heads // hb,),
                in_specs=[row_spec(rows), row_spec(half_rows), row_spec(half_rows)] + far_specs,
                out_specs=out_spec(half_rows),
            ),
            compiler_params=params,
            cost_estimate=cost(2 * BLOCK, half_rows, heads * width * (2 * rows + 8 * half_rows + 2 * sum(a.shape[2] for a in far_operands))),
        )(meta, used, q_t, acc1, st1, *far_operands)

        received_even = lax.ppermute(project_half(att_even, out_weight, 1 - hidx), "head", swap)
        own_even = project_half(att_even, out_weight, hidx)
        parts = [
            (own.astype(jnp.float32) + got.astype(jnp.float32)).astype(jnp.bfloat16)
            for own, got in ((own_even, received_even), (own_odd, received_odd))
        ]
    even, odd = (p.reshape(per_dev // 2, BLOCK, -1) for p in parts)
    return jnp.stack([even, odd], axis=1).reshape(rows, -1)


def solution(mesh):
    placed = (
        P("ctx", "head", None),
        P("ctx", "head", None),
        P("ctx", "head", None),
        P(),
        P("head", None),
    )
    return jax.shard_map(
        per_device, mesh=mesh, in_specs=placed, out_specs=P("ctx", "head"), check_vma=False
    )
```

```python
import functools
import math

import jax
import jax.numpy as jnp
from jax import lax
from jax.experimental import pallas as pl
from jax.experimental.pallas import tpu as pltpu
from jax.sharding import PartitionSpec as P

BLOCK = 64
WINDOW = 512
NOFF = 5
HEADS_PER_STEP = 4


def from_behind(value, axis, steps):
    count = lax.axis_size(axis)
    initial, last = (max(0, -steps), min(count, count - steps))
    return lax.ppermute(value, axis, [(source, source + steps) for source in range(initial, last)])


def block_scores(q, keys, scale):
    return lax.dot_general(
        q, keys, (((1,), (1,)), ((), ())), preferred_element_type=jnp.float32
    ) * scale


def merge(pieces, m_old, l_old, acc_old):
    top = m_old
    for s, _ in pieces:
        row_max = s.max(axis=1, keepdims=True)
        top = row_max if top is None else jnp.maximum(top, row_max)
    total = None
    summed = None
    for s, v in pieces:
        p = jnp.exp(s - top)
        part_total = p.sum(axis=1, keepdims=True)
        part = jnp.dot(p.astype(jnp.bfloat16), v, preferred_element_type=jnp.float32)
        total = part_total if total is None else total + part_total
        summed = part if summed is None else summed + part
    if m_old is not None:
        alpha = jnp.exp(m_old - top)
        total = total + l_old * alpha
        summed = summed + acc_old * alpha
    return top, total, summed


def pack_stats(m, l, width):
    lane = lax.broadcasted_iota(jnp.int32, (m.shape[0], width), 1)
    return jnp.where(lane == 0, m, jnp.where(lane == 1, l, 0.0))


TILE = 256


class HeadView:
    def __init__(self, ref, head, width=None):
        self.ref, self.head, self.width = ref, head, width

    def _index(self, idx):
        if idx is Ellipsis:
            idx = (slice(None), slice(None))
        if self.width is None:
            return (self.head,) + tuple(idx)
        return (idx[0], pl.ds(self.head * self.width, self.width))

    @property
    def dtype(self):
        return self.ref.dtype

    def __getitem__(self, idx):
        return self.ref[self._index(idx)]

    def __setitem__(self, idx, value):
        self.ref[self._index(idx)] = value


def per_head(body, n_prefetch, n_head_major, n_rows_out, width, heads_per_step):
    def kernel(*refs):
        pre = refs[:n_prefetch]
        rest = refs[n_prefetch:]
        n_major = len(rest) - n_rows_out
        for hh in range(heads_per_step):
            views = [HeadView(r, hh) for r in rest[:n_major]]
            outs = [HeadView(r, hh, width) for r in rest[n_major:]]
            body(*pre, *views, *outs)

    return kernel


def own_kernel(per_dev, width, scale, q_ref, k_ref, v_ref, acc_ref, st_ref):
    neg = jnp.float32(-jnp.inf)
    rows = per_dev * BLOCK
    for lo in range(0, rows, TILE):
        q = q_ref[lo:lo + TILE, :]
        n_own = lo + TILE
        s_o = block_scores(q, k_ref[:n_own, :], scale)
        r_ids = lax.broadcasted_iota(jnp.int32, (TILE, n_own), 0)
        c_ids = lax.broadcasted_iota(jnp.int32, (TILE, n_own), 1)
        s_o = jnp.where(c_ids <= r_ids + lo, s_o, neg)
        m, l, acc = merge([(s_o, v_ref[:n_own, :])], None, None, None)
        acc_ref[lo:lo + TILE, :] = acc
        st_ref[lo:lo + TILE, :] = pack_stats(m, l, width)


def column_map(n_cols, values):
    seg = lax.broadcasted_iota(jnp.int32, (1, n_cols), 1) // BLOCK
    out = jnp.zeros((1, n_cols), jnp.int32)
    for j, value in enumerate(values):
        out = jnp.where(seg == j, value, out)
    return out


def prev_kernel(per_dev, width, scale, meta_ref, used_ref, q_ref, kp_ref, vp_ref, acc_ref, st_ref,
                acc_out, st_out, odd_ref):
    prev_ok = meta_ref[0] > 0
    neg = jnp.float32(-jnp.inf)
    rows = per_dev * BLOCK
    per_tile = TILE // BLOCK
    for lo in range(0, rows, TILE):
        q = q_ref[lo:lo + TILE, :]
        n_prev = rows - lo
        s_p = block_scores(q, kp_ref[lo:, :], scale)
        r_ids = lax.broadcasted_iota(jnp.int32, (TILE, n_prev), 0)
        c_ids = lax.broadcasted_iota(jnp.int32, (TILE, n_prev), 1)
        s_p = jnp.where((c_ids > r_ids) & prev_ok, s_p, neg)
        blocks = range(lo // BLOCK, lo // BLOCK + per_tile)
        starts = [pl.multiple_of(meta_ref[1 + i] * BLOCK, BLOCK) for i in blocks]
        k0 = jnp.concatenate([kp_ref[pl.ds(st, BLOCK), :] for st in starts], axis=0)
        v0 = jnp.concatenate([vp_ref[pl.ds(st, BLOCK), :] for st in starts], axis=0)
        s_f = block_scores(q, k0, scale)
        flags = column_map(TILE, [used_ref[i * NOFF] for i in blocks])
        r_blk = lax.broadcasted_iota(jnp.int32, (TILE, TILE), 0) // BLOCK
        c_blk = lax.broadcasted_iota(jnp.int32, (TILE, TILE), 1) // BLOCK
        s_f = jnp.where((r_blk == c_blk) & (flags > 0), s_f, neg)
        st = st_ref[lo:lo + TILE, :]
        m, l, acc = merge(
            [(s_p, vp_ref[lo:, :]), (s_f, v0)], st[:, 0:1], st[:, 1:2], acc_ref[lo:lo + TILE, :]
        )
        for b, i in enumerate(blocks):
            sl = slice(b * BLOCK, (b + 1) * BLOCK)
            half = (i // 2) * BLOCK
            if i % 2:
                odd_ref[half:half + BLOCK, :] = (acc[sl] / l[sl]).astype(odd_ref.dtype)
            else:
                acc_out[half:half + BLOCK, :] = acc[sl]
                st_out[half:half + BLOCK, :] = pack_stats(m[sl], l[sl], width)


def far_kernel(levels, per_dev, width, scale, meta_ref, used_ref, q_ref, acc_ref, st_ref, *rest):
    far_refs = rest[:-1]
    even_ref = rest[-1]
    neg = jnp.float32(-jnp.inf)
    n_even = per_dev // 2
    q = jnp.concatenate([q_ref[2 * e * BLOCK:(2 * e + 1) * BLOCK, :] for e in range(n_even)], axis=0)
    keys, vals, targets, flags = [], [], [], []
    pos = 0
    for level in levels:
        offset = 2**level
        refs = far_refs[pos:pos + 2]
        pos += 2
        k_lvl = refs[0][...]
        v_lvl = refs[1][...]
        keys.append(k_lvl)
        vals.append(v_lvl)
        for k in range(k_lvl.shape[0] // BLOCK):
            qblock = k * offset
            targets.append(qblock // 2)
            flags.append(used_ref[qblock * NOFF + level])
    k_far = jnp.concatenate(keys, axis=0)
    v_far = jnp.concatenate(vals, axis=0)
    n_keys = k_far.shape[0]
    s_f = block_scores(q, k_far, scale)
    col_target = column_map(n_keys, targets)
    col_flag = column_map(n_keys, flags)
    r_blk = lax.broadcasted_iota(jnp.int32, (n_even * BLOCK, n_keys), 0) // BLOCK
    s_f = jnp.where((r_blk == col_target) & (col_flag > 0), s_f, neg)
    st = st_ref[...]
    m, l, acc = merge([(s_f, v_far)], st[:, 0:1], st[:, 1:2], acc_ref[...])
    even_ref[...] = (acc / l).astype(even_ref.dtype)


def matmul_kernel(sel_ref, a_ref, w_ref, o_ref):
    o_ref[...] = jnp.dot(a_ref[...], w_ref[...], preferred_element_type=jnp.float32).astype(
        o_ref.dtype
    )


def project_half(attended, weight, half, tn=512):
    rows, depth = attended.shape
    cw = weight.shape[1] // 2
    steps = cw // tn
    return pl.pallas_call(
        matmul_kernel,
        out_shape=jax.ShapeDtypeStruct((rows, cw), jnp.bfloat16),
        grid_spec=pltpu.PrefetchScalarGridSpec(
            num_scalar_prefetch=1,
            grid=(steps,),
            in_specs=[
                pl.BlockSpec((rows, depth), lambda j, sel: (0, 0)),
                pl.BlockSpec((depth, tn), lambda j, sel: (0, sel[0] * steps + j)),
            ],
            out_specs=pl.BlockSpec((rows, tn), lambda j, sel: (0, j)),
        ),
        compiler_params=pltpu.CompilerParams(dimension_semantics=("arbitrary",)),
        cost_estimate=pl.CostEstimate(
            flops=2 * rows * depth * cw,
            transcendentals=0,
            bytes_accessed=2 * (rows * depth + depth * cw + rows * cw),
        ),
    )(jnp.reshape(half, (1,)).astype(jnp.int32), attended, weight)


def pick_blocks(kv, local):
    return jnp.concatenate(
        [lax.dynamic_slice_in_dim(kv, local[b] * BLOCK, BLOCK, axis=2) for b in range(local.shape[0])],
        axis=2,
    )


def per_device(queries, keys, values, far_blocks, out_weight):
    rows, heads, width = queries.shape
    per_dev = rows // BLOCK
    device = lax.axis_index("ctx")
    cycle_size = lax.axis_size("ctx")
    scale = 1.0 / math.sqrt(width)
    q_t = jnp.transpose(queries, (1, 0, 2))
    kv_t = jnp.stack([jnp.transpose(keys, (1, 0, 2)), jnp.transpose(values, (1, 0, 2))])
    prev_kv = from_behind(kv_t, "ctx", 1)
    levels = []
    sends = []
    for level in range(1, NOFF):
        offset = 2**level
        if offset >= cycle_size:
            continue
        target = lax.dynamic_slice_in_dim(far_blocks, (device + offset) * per_dev, per_dev, 0)[
            ::offset, level
        ]
        local = jnp.clip(target - device * per_dev, 0, per_dev - 1)
        levels.append(level)
        if level == 1:
            nxt = lax.dynamic_slice_in_dim(far_blocks, (device + 1) * per_dev, per_dev, 0)[::2, 1]
            fwd_local = jnp.clip(nxt - (device - 1) * per_dev, 0, per_dev - 1)
            continue
        pairs = [(s, s + offset) for s in range(0, cycle_size - offset)]
        sends.append((pick_blocks(kv_t, local), pairs))
    q_t, kv_t, *operands = lax.optimization_barrier((q_t, kv_t, *[op for op, _ in sends]))
    far_arrays = [(lax.ppermute(op, "ctx", pairs),) for (_, pairs), op in zip(sends, operands)]

    own = lax.dynamic_slice_in_dim(far_blocks, device * per_dev, per_dev, 0)
    query_index = device * per_dev + jnp.arange(per_dev, dtype=jnp.int32)
    used = (own <= (query_index - WINDOW // BLOCK - 1)[:, None]).astype(jnp.int32).reshape(-1)
    pick = jnp.clip(own[:, 0] - (device - 1) * per_dev, 0, per_dev - 1)
    meta = jnp.concatenate(
        [(device > 0).astype(jnp.int32)[None], pick.astype(jnp.int32), (device % 2)[None]]
    )

    hb = math.gcd(heads, HEADS_PER_STEP)
    row_spec = lambda n: pl.BlockSpec((hb, n, width), lambda h, *_: (h, 0, 0))
    out_spec = lambda n: pl.BlockSpec((n, hb * width), lambda h, *_: (0, h))
    k_spec = lambda n: pl.BlockSpec((None, hb, n, width), lambda h, *_: (0, h, 0, 0))
    v_spec = lambda n: pl.BlockSpec((None, hb, n, width), lambda h, *_: (1, h, 0, 0))
    half_rows = rows // 2
    f32 = jnp.float32
    params = pltpu.CompilerParams(dimension_semantics=("arbitrary",))
    state = lambda n: jax.ShapeDtypeStruct((heads, n, width), f32)

    def cost(keys_per_row, n_rows, extra_bytes):
        return pl.CostEstimate(
            flops=4 * n_rows * heads * width * keys_per_row,
            transcendentals=n_rows * heads * keys_per_row,
            bytes_accessed=extra_bytes,
        )

    acc0, st0 = pl.pallas_call(
        per_head(functools.partial(own_kernel, per_dev, width, scale), 0, 5, 0, width, hb),
        out_shape=(state(rows), state(rows)),
        grid=(heads // hb,),
        in_specs=[row_spec(rows), k_spec(rows), v_spec(rows)],
        out_specs=(row_spec(rows), row_spec(rows)),
        compiler_params=params,
        cost_estimate=cost(WINDOW // 2, rows, 2 * heads * rows * width * (3 * 2 + 2 * 4)),
    )(q_t, kv_t, kv_t)

    prev_kv, acc0, st0 = lax.optimization_barrier((prev_kv, acc0, st0))
    if levels and levels[0] == 1:
        far_arrays.insert(0, (from_behind(pick_blocks(prev_kv, fwd_local), "ctx", 1),))
    far_specs, far_operands = [], []
    for group in far_arrays:
        for a in group:
            far_specs += [k_spec(a.shape[2]), v_spec(a.shape[2])]
            far_operands += [a, a]
    acc1, st1, att_odd = pl.pallas_call(
        per_head(functools.partial(prev_kernel, per_dev, width, scale), 2, 7, 1, width, hb),
        out_shape=(
            state(half_rows),
            state(half_rows),
            jax.ShapeDtypeStruct((half_rows, heads * width), queries.dtype),
        ),
        grid_spec=pltpu.PrefetchScalarGridSpec(
            num_scalar_prefetch=2,
            grid=(heads // hb,),
            in_specs=[row_spec(rows), k_spec(rows), v_spec(rows), row_spec(rows), row_spec(rows)],
            out_specs=(row_spec(half_rows), row_spec(half_rows), out_spec(half_rows)),
        ),
        compiler_params=params,
        cost_estimate=cost(WINDOW // 2 + BLOCK, rows, heads * rows * width * (3 * 2 + 2 * 4 + 8)),
    )(meta, used, q_t, prev_kv, prev_kv, acc0, st0)

    n_head = lax.axis_size("head")
    if n_head != 2:
        att_even = pl.pallas_call(
            per_head(functools.partial(far_kernel, levels, per_dev, width, scale), 2, 0, 1, width, hb),
            out_shape=jax.ShapeDtypeStruct((half_rows, heads * width), queries.dtype),
            grid_spec=pltpu.PrefetchScalarGridSpec(
                num_scalar_prefetch=2,
                grid=(heads // hb,),
                in_specs=[row_spec(rows), row_spec(half_rows), row_spec(half_rows)] + far_specs,
                out_specs=out_spec(half_rows),
            ),
            compiler_params=params,
            cost_estimate=cost(2 * BLOCK, half_rows, heads * width * (2 * rows + 8 * half_rows + 2 * sum(a.shape[2] for a in far_operands))),
        )(meta, used, q_t, acc1, st1, *far_operands)

        parts = []
        for att in (att_even, att_odd):
            partial_value = jnp.dot(att, out_weight, preferred_element_type=jnp.float32)
            parts.append(lax.psum_scatter(
                partial_value.astype(jnp.bfloat16), "head", scatter_dimension=1, tiled=True
            ))
    else:
        hidx = lax.axis_index("head")
        swap = [(0, 1), (1, 0)]
        received_odd = lax.ppermute(project_half(att_odd, out_weight, 1 - hidx), "head", swap)
        own_odd = project_half(att_odd, out_weight, hidx)
        acc1, st1, own_odd = lax.optimization_barrier((acc1, st1, own_odd))
        att_even = pl.pallas_call(
            per_head(functools.partial(far_kernel, levels, per_dev, width, scale), 2, 0, 1, width, hb),
            out_shape=jax.ShapeDtypeStruct((half_rows, heads * width), queries.dtype),
            grid_spec=pltpu.PrefetchScalarGridSpec(
                num_scalar_prefetch=2,
                grid=(heads // hb,),
                in_specs=[row_spec(rows), row_spec(half_rows), row_spec(half_rows)] + far_specs,
                out_specs=out_spec(half_rows),
            ),
            compiler_params=params,
            cost_estimate=cost(2 * BLOCK, half_rows, heads * width * (2 * rows + 8 * half_rows + 2 * sum(a.shape[2] for a in far_operands))),
        )(meta, used, q_t, acc1, st1, *far_operands)

        received_even = lax.ppermute(project_half(att_even, out_weight, 1 - hidx), "head", swap)
        own_even = project_half(att_even, out_weight, hidx)
        parts = [
            (own.astype(jnp.float32) + got.astype(jnp.float32)).astype(jnp.bfloat16)
            for own, got in ((own_even, received_even), (own_odd, received_odd))
        ]
    even, odd = (p.reshape(per_dev // 2, BLOCK, -1) for p in parts)
    return jnp.stack([even, odd], axis=1).reshape(rows, -1)


def solution(mesh):
    placed = (
        P("ctx", "head", None),
        P("ctx", "head", None),
        P("ctx", "head", None),
        P(),
        P("head", None),
    )
    return jax.shard_map(
        per_device, mesh=mesh, in_specs=placed, out_specs=P("ctx", "head"), check_vma=False
    )
```

```python
import functools
import math

import jax
import jax.numpy as jnp
from jax import lax
from jax.experimental import pallas as pl
from jax.experimental.pallas import tpu as pltpu
from jax.sharding import PartitionSpec as P

BLOCK = 64
WINDOW = 512
NOFF = 5
HEADS_PER_STEP = 8


def from_behind(value, axis, steps):
    count = lax.axis_size(axis)
    initial, last = (max(0, -steps), min(count, count - steps))
    return lax.ppermute(value, axis, [(source, source + steps) for source in range(initial, last)])


def block_scores(q, keys, scale):
    return lax.dot_general(
        q, keys, (((1,), (1,)), ((), ())), preferred_element_type=jnp.float32
    ) * scale


def merge(pieces, m_old, l_old, acc_old):
    top = m_old
    for s, _ in pieces:
        row_max = s.max(axis=1, keepdims=True)
        top = row_max if top is None else jnp.maximum(top, row_max)
    total = None
    summed = None
    for s, v in pieces:
        p = jnp.exp(s - top)
        part_total = p.sum(axis=1, keepdims=True)
        part = jnp.dot(p.astype(jnp.bfloat16), v, preferred_element_type=jnp.float32)
        total = part_total if total is None else total + part_total
        summed = part if summed is None else summed + part
    if m_old is not None:
        alpha = jnp.exp(m_old - top)
        total = total + l_old * alpha
        summed = summed + acc_old * alpha
    return top, total, summed


def pack_stats(m, l, width):
    lane = lax.broadcasted_iota(jnp.int32, (m.shape[0], width), 1)
    return jnp.where(lane == 0, m, jnp.where(lane == 1, l, 0.0))


TILE = 256


class HeadView:
    def __init__(self, ref, head, width=None):
        self.ref, self.head, self.width = ref, head, width

    def _index(self, idx):
        if idx is Ellipsis:
            idx = (slice(None), slice(None))
        if self.width is None:
            return (self.head,) + tuple(idx)
        return (idx[0], pl.ds(self.head * self.width, self.width))

    @property
    def dtype(self):
        return self.ref.dtype

    def __getitem__(self, idx):
        return self.ref[self._index(idx)]

    def __setitem__(self, idx, value):
        self.ref[self._index(idx)] = value


def per_head(body, n_prefetch, n_head_major, n_rows_out, width, heads_per_step):
    def kernel(*refs):
        pre = refs[:n_prefetch]
        rest = refs[n_prefetch:]
        n_major = len(rest) - n_rows_out
        for hh in range(heads_per_step):
            views = [HeadView(r, hh) for r in rest[:n_major]]
            outs = [HeadView(r, hh, width) for r in rest[n_major:]]
            body(*pre, *views, *outs)

    return kernel


def own_kernel(per_dev, width, scale, q_ref, k_ref, v_ref, acc_ref, st_ref):
    neg = jnp.float32(-jnp.inf)
    rows = per_dev * BLOCK
    for lo in range(0, rows, TILE):
        q = q_ref[lo:lo + TILE, :]
        n_own = lo + TILE
        s_o = block_scores(q, k_ref[:n_own, :], scale)
        r_ids = lax.broadcasted_iota(jnp.int32, (TILE, n_own), 0)
        c_ids = lax.broadcasted_iota(jnp.int32, (TILE, n_own), 1)
        s_o = jnp.where(c_ids <= r_ids + lo, s_o, neg)
        m, l, acc = merge([(s_o, v_ref[:n_own, :])], None, None, None)
        acc_ref[lo:lo + TILE, :] = acc
        st_ref[lo:lo + TILE, :] = pack_stats(m, l, width)


def column_map(n_cols, values):
    seg = lax.broadcasted_iota(jnp.int32, (1, n_cols), 1) // BLOCK
    out = jnp.zeros((1, n_cols), jnp.int32)
    for j, value in enumerate(values):
        out = jnp.where(seg == j, value, out)
    return out


def prev_kernel(per_dev, width, scale, meta_ref, used_ref, q_ref, kp_ref, vp_ref, acc_ref, st_ref,
                acc_out, st_out, odd_ref):
    prev_ok = meta_ref[0] > 0
    neg = jnp.float32(-jnp.inf)
    rows = per_dev * BLOCK
    per_tile = TILE // BLOCK
    for lo in range(0, rows, TILE):
        q = q_ref[lo:lo + TILE, :]
        n_prev = rows - lo
        s_p = block_scores(q, kp_ref[lo:, :], scale)
        r_ids = lax.broadcasted_iota(jnp.int32, (TILE, n_prev), 0)
        c_ids = lax.broadcasted_iota(jnp.int32, (TILE, n_prev), 1)
        s_p = jnp.where((c_ids > r_ids) & prev_ok, s_p, neg)
        blocks = range(lo // BLOCK, lo // BLOCK + per_tile)
        starts = [pl.multiple_of(meta_ref[1 + i] * BLOCK, BLOCK) for i in blocks]
        k0 = jnp.concatenate([kp_ref[pl.ds(st, BLOCK), :] for st in starts], axis=0)
        v0 = jnp.concatenate([vp_ref[pl.ds(st, BLOCK), :] for st in starts], axis=0)
        s_f = block_scores(q, k0, scale)
        flags = column_map(TILE, [used_ref[i * NOFF] for i in blocks])
        r_blk = lax.broadcasted_iota(jnp.int32, (TILE, TILE), 0) // BLOCK
        c_blk = lax.broadcasted_iota(jnp.int32, (TILE, TILE), 1) // BLOCK
        s_f = jnp.where((r_blk == c_blk) & (flags > 0), s_f, neg)
        st = st_ref[lo:lo + TILE, :]
        m, l, acc = merge(
            [(s_p, vp_ref[lo:, :]), (s_f, v0)], st[:, 0:1], st[:, 1:2], acc_ref[lo:lo + TILE, :]
        )
        for b, i in enumerate(blocks):
            sl = slice(b * BLOCK, (b + 1) * BLOCK)
            half = (i // 2) * BLOCK
            if i % 2:
                odd_ref[half:half + BLOCK, :] = (acc[sl] / l[sl]).astype(odd_ref.dtype)
            else:
                acc_out[half:half + BLOCK, :] = acc[sl]
                st_out[half:half + BLOCK, :] = pack_stats(m[sl], l[sl], width)


def far_kernel(levels, per_dev, width, scale, meta_ref, used_ref, q_ref, acc_ref, st_ref, *rest):
    far_refs = rest[:-1]
    even_ref = rest[-1]
    neg = jnp.float32(-jnp.inf)
    n_even = per_dev // 2
    q = jnp.concatenate([q_ref[2 * e * BLOCK:(2 * e + 1) * BLOCK, :] for e in range(n_even)], axis=0)
    keys, vals, targets, flags = [], [], [], []
    pos = 0
    for level in levels:
        offset = 2**level
        n_src = 2 if level == 1 else 1
        refs = far_refs[pos:pos + 2 * n_src]
        pos += 2 * n_src
        k_lvl = refs[0][...]
        v_lvl = refs[1][...]
        if n_src == 2:
            odd = meta_ref[1 + per_dev] > 0
            k_lvl = jnp.where(odd, refs[2][...], k_lvl)
            v_lvl = jnp.where(odd, refs[3][...], v_lvl)
        keys.append(k_lvl)
        vals.append(v_lvl)
        for k in range(k_lvl.shape[0] // BLOCK):
            qblock = k * offset
            targets.append(qblock // 2)
            flags.append(used_ref[qblock * NOFF + level])
    k_far = jnp.concatenate(keys, axis=0)
    v_far = jnp.concatenate(vals, axis=0)
    n_keys = k_far.shape[0]
    s_f = block_scores(q, k_far, scale)
    col_target = column_map(n_keys, targets)
    col_flag = column_map(n_keys, flags)
    r_blk = lax.broadcasted_iota(jnp.int32, (n_even * BLOCK, n_keys), 0) // BLOCK
    s_f = jnp.where((r_blk == col_target) & (col_flag > 0), s_f, neg)
    st = st_ref[...]
    m, l, acc = merge([(s_f, v_far)], st[:, 0:1], st[:, 1:2], acc_ref[...])
    even_ref[...] = (acc / l).astype(even_ref.dtype)


def matmul_kernel(sel_ref, a_ref, w_ref, o_ref):
    o_ref[...] = jnp.dot(a_ref[...], w_ref[...], preferred_element_type=jnp.float32).astype(
        o_ref.dtype
    )


def project_half(attended, weight, half, tn=512):
    rows, depth = attended.shape
    cw = weight.shape[1] // 2
    steps = cw // tn
    return pl.pallas_call(
        matmul_kernel,
        out_shape=jax.ShapeDtypeStruct((rows, cw), jnp.bfloat16),
        grid_spec=pltpu.PrefetchScalarGridSpec(
            num_scalar_prefetch=1,
            grid=(steps,),
            in_specs=[
                pl.BlockSpec((rows, depth), lambda j, sel: (0, 0)),
                pl.BlockSpec((depth, tn), lambda j, sel: (0, sel[0] * steps + j)),
            ],
            out_specs=pl.BlockSpec((rows, tn), lambda j, sel: (0, j)),
        ),
        compiler_params=pltpu.CompilerParams(dimension_semantics=("arbitrary",)),
        cost_estimate=pl.CostEstimate(
            flops=2 * rows * depth * cw,
            transcendentals=0,
            bytes_accessed=2 * (rows * depth + depth * cw + rows * cw),
        ),
    )(jnp.reshape(half, (1,)).astype(jnp.int32), attended, weight)


def pick_blocks(kv, local):
    return jnp.concatenate(
        [lax.dynamic_slice_in_dim(kv, local[b] * BLOCK, BLOCK, axis=2) for b in range(local.shape[0])],
        axis=2,
    )


def per_device(queries, keys, values, far_blocks, out_weight):
    rows, heads, width = queries.shape
    per_dev = rows // BLOCK
    device = lax.axis_index("ctx")
    cycle_size = lax.axis_size("ctx")
    scale = 1.0 / math.sqrt(width)
    q_t = jnp.transpose(queries, (1, 0, 2))
    kv_t = jnp.stack([jnp.transpose(keys, (1, 0, 2)), jnp.transpose(values, (1, 0, 2))])
    prev_kv = from_behind(kv_t, "ctx", 1)
    levels = []
    sends = []
    for level in range(1, NOFF):
        offset = 2**level
        if offset >= cycle_size:
            continue
        target = lax.dynamic_slice_in_dim(far_blocks, (device + offset) * per_dev, per_dev, 0)[
            ::offset, level
        ]
        local = jnp.clip(target - device * per_dev, 0, per_dev - 1)
        if level == 1:
            pairs = [(s, s + 2) for s in range(0, cycle_size - 2, 2)]
            nxt = lax.dynamic_slice_in_dim(far_blocks, (device + 1) * per_dev, per_dev, 0)[::2, 1]
            fwd_local = jnp.clip(nxt - (device - 1) * per_dev, 0, per_dev - 1)
        else:
            pairs = [(s, s + offset) for s in range(0, cycle_size - offset)]
        sends.append((pick_blocks(kv_t, local), pairs))
        levels.append(level)
    q_t, kv_t, *operands = lax.optimization_barrier((q_t, kv_t, *[op for op, _ in sends]))
    far_arrays = []
    for (_, pairs), op, level in zip(sends, operands, levels):
        if level == 1:
            far_arrays.append((op, pairs))
        else:
            far_arrays.append((lax.ppermute(op, "ctx", pairs),))

    own = lax.dynamic_slice_in_dim(far_blocks, device * per_dev, per_dev, 0)
    query_index = device * per_dev + jnp.arange(per_dev, dtype=jnp.int32)
    used = (own <= (query_index - WINDOW // BLOCK - 1)[:, None]).astype(jnp.int32).reshape(-1)
    pick = jnp.clip(own[:, 0] - (device - 1) * per_dev, 0, per_dev - 1)
    meta = jnp.concatenate(
        [(device > 0).astype(jnp.int32)[None], pick.astype(jnp.int32), (device % 2)[None]]
    )

    hb = math.gcd(heads, HEADS_PER_STEP)
    row_spec = lambda n: pl.BlockSpec((hb, n, width), lambda h, *_: (h, 0, 0))
    out_spec = lambda n: pl.BlockSpec((n, hb * width), lambda h, *_: (0, h))
    k_spec = lambda n: pl.BlockSpec((None, hb, n, width), lambda h, *_: (0, h, 0, 0))
    v_spec = lambda n: pl.BlockSpec((None, hb, n, width), lambda h, *_: (1, h, 0, 0))
    half_rows = rows // 2
    f32 = jnp.float32
    params = pltpu.CompilerParams(dimension_semantics=("arbitrary",))
    state = lambda n: jax.ShapeDtypeStruct((heads, n, width), f32)

    def cost(keys_per_row, n_rows, extra_bytes):
        return pl.CostEstimate(
            flops=4 * n_rows * heads * width * keys_per_row,
            transcendentals=n_rows * heads * keys_per_row,
            bytes_accessed=extra_bytes,
        )

    acc0, st0 = pl.pallas_call(
        per_head(functools.partial(own_kernel, per_dev, width, scale), 0, 5, 0, width, hb),
        out_shape=(state(rows), state(rows)),
        grid=(heads // hb,),
        in_specs=[row_spec(rows), k_spec(rows), v_spec(rows)],
        out_specs=(row_spec(rows), row_spec(rows)),
        compiler_params=params,
        cost_estimate=cost(WINDOW // 2, rows, 2 * heads * rows * width * (3 * 2 + 2 * 4)),
    )(q_t, kv_t, kv_t)

    if levels and levels[0] == 1:
        direct_op, direct_pairs = far_arrays[0]
        prev_kv, acc0, st0, direct_op = lax.optimization_barrier((prev_kv, acc0, st0, direct_op))
        direct = lax.ppermute(direct_op, "ctx", direct_pairs)
        forwarded = lax.ppermute(
            pick_blocks(prev_kv, fwd_local), "ctx",
            [(s, s + 1) for s in range(0, cycle_size - 1, 2)],
        )
        far_arrays[0] = (direct, forwarded)
    else:
        prev_kv, acc0, st0 = lax.optimization_barrier((prev_kv, acc0, st0))
    far_specs, far_operands = [], []
    for group in far_arrays:
        for a in group:
            far_specs += [k_spec(a.shape[2]), v_spec(a.shape[2])]
            far_operands += [a, a]
    acc1, st1, att_odd = pl.pallas_call(
        per_head(functools.partial(prev_kernel, per_dev, width, scale), 2, 7, 1, width, hb),
        out_shape=(
            state(half_rows),
            state(half_rows),
            jax.ShapeDtypeStruct((half_rows, heads * width), queries.dtype),
        ),
        grid_spec=pltpu.PrefetchScalarGridSpec(
            num_scalar_prefetch=2,
            grid=(heads // hb,),
            in_specs=[row_spec(rows), k_spec(rows), v_spec(rows), row_spec(rows), row_spec(rows)],
            out_specs=(row_spec(half_rows), row_spec(half_rows), out_spec(half_rows)),
        ),
        compiler_params=params,
        cost_estimate=cost(WINDOW // 2 + BLOCK, rows, heads * rows * width * (3 * 2 + 2 * 4 + 8)),
    )(meta, used, q_t, prev_kv, prev_kv, acc0, st0)

    n_head = lax.axis_size("head")
    if n_head != 2:
        att_even = pl.pallas_call(
            per_head(functools.partial(far_kernel, levels, per_dev, width, scale), 2, 0, 1, width, hb),
            out_shape=jax.ShapeDtypeStruct((half_rows, heads * width), queries.dtype),
            grid_spec=pltpu.PrefetchScalarGridSpec(
                num_scalar_prefetch=2,
                grid=(heads // hb,),
                in_specs=[row_spec(rows), row_spec(half_rows), row_spec(half_rows)] + far_specs,
                out_specs=out_spec(half_rows),
            ),
            compiler_params=params,
            cost_estimate=cost(2 * BLOCK, half_rows, heads * width * (2 * rows + 8 * half_rows + 2 * sum(a.shape[2] for a in far_operands))),
        )(meta, used, q_t, acc1, st1, *far_operands)

        parts = []
        for att in (att_even, att_odd):
            partial_value = jnp.dot(att, out_weight, preferred_element_type=jnp.float32)
            parts.append(lax.psum_scatter(
                partial_value.astype(jnp.bfloat16), "head", scatter_dimension=1, tiled=True
            ))
    else:
        hidx = lax.axis_index("head")
        swap = [(0, 1), (1, 0)]
        received_odd = lax.ppermute(project_half(att_odd, out_weight, 1 - hidx), "head", swap)
        own_odd = project_half(att_odd, out_weight, hidx)
        acc1, st1, own_odd = lax.optimization_barrier((acc1, st1, own_odd))
        att_even = pl.pallas_call(
            per_head(functools.partial(far_kernel, levels, per_dev, width, scale), 2, 0, 1, width, hb),
            out_shape=jax.ShapeDtypeStruct((half_rows, heads * width), queries.dtype),
            grid_spec=pltpu.PrefetchScalarGridSpec(
                num_scalar_prefetch=2,
                grid=(heads // hb,),
                in_specs=[row_spec(rows), row_spec(half_rows), row_spec(half_rows)] + far_specs,
                out_specs=out_spec(half_rows),
            ),
            compiler_params=params,
            cost_estimate=cost(2 * BLOCK, half_rows, heads * width * (2 * rows + 8 * half_rows + 2 * sum(a.shape[2] for a in far_operands))),
        )(meta, used, q_t, acc1, st1, *far_operands)

        received_even = lax.ppermute(project_half(att_even, out_weight, 1 - hidx), "head", swap)
        own_even = project_half(att_even, out_weight, hidx)
        parts = [
            (own.astype(jnp.float32) + got.astype(jnp.float32)).astype(jnp.bfloat16)
            for own, got in ((own_even, received_even), (own_odd, received_odd))
        ]
    even, odd = (p.reshape(per_dev // 2, BLOCK, -1) for p in parts)
    return jnp.stack([even, odd], axis=1).reshape(rows, -1)


def solution(mesh):
    placed = (
        P("ctx", "head", None),
        P("ctx", "head", None),
        P("ctx", "head", None),
        P(),
        P("head", None),
    )
    return jax.shard_map(
        per_device, mesh=mesh, in_specs=placed, out_specs=P("ctx", "head"), check_vma=False
    )
```

```python
import functools
import math

import jax
import jax.numpy as jnp
from jax import lax
from jax.experimental import pallas as pl
from jax.experimental.pallas import tpu as pltpu
from jax.sharding import PartitionSpec as P

BLOCK = 64
WINDOW = 512
NOFF = 5
HEADS_PER_STEP = 4


def from_behind(value, axis, steps):
    count = lax.axis_size(axis)
    initial, last = (max(0, -steps), min(count, count - steps))
    return lax.ppermute(value, axis, [(source, source + steps) for source in range(initial, last)])


def block_scores(q, keys, scale):
    return lax.dot_general(
        q, keys, (((1,), (1,)), ((), ())), preferred_element_type=jnp.float32
    ) * scale


def merge(pieces, m_old, l_old, acc_old):
    top = m_old
    for s, _ in pieces:
        row_max = s.max(axis=1, keepdims=True)
        top = row_max if top is None else jnp.maximum(top, row_max)
    total = None
    summed = None
    for s, v in pieces:
        p = jnp.exp(s - top)
        part_total = p.sum(axis=1, keepdims=True)
        part = jnp.dot(p.astype(jnp.bfloat16), v, preferred_element_type=jnp.float32)
        total = part_total if total is None else total + part_total
        summed = part if summed is None else summed + part
    if m_old is not None:
        alpha = jnp.exp(m_old - top)
        total = total + l_old * alpha
        summed = summed + acc_old * alpha
    return top, total, summed


def pack_stats(m, l, width):
    lane = lax.broadcasted_iota(jnp.int32, (m.shape[0], width), 1)
    return jnp.where(lane == 0, m, jnp.where(lane == 1, l, 0.0))


TILE = 256


class HeadView:
    def __init__(self, ref, head, width=None):
        self.ref, self.head, self.width = ref, head, width

    def _index(self, idx):
        if idx is Ellipsis:
            idx = (slice(None), slice(None))
        if self.width is None:
            return (self.head,) + tuple(idx)
        return (idx[0], pl.ds(self.head * self.width, self.width))

    @property
    def dtype(self):
        return self.ref.dtype

    def __getitem__(self, idx):
        return self.ref[self._index(idx)]

    def __setitem__(self, idx, value):
        self.ref[self._index(idx)] = value


def per_head(body, n_prefetch, n_head_major, n_rows_out, width, heads_per_step):
    def kernel(*refs):
        pre = refs[:n_prefetch]
        rest = refs[n_prefetch:]
        n_major = len(rest) - n_rows_out
        for hh in range(heads_per_step):
            views = [HeadView(r, hh) for r in rest[:n_major]]
            outs = [HeadView(r, hh, width) for r in rest[n_major:]]
            body(*pre, *views, *outs)

    return kernel


def own_kernel(per_dev, width, scale, q_ref, k_ref, v_ref, acc_ref, st_ref):
    neg = jnp.float32(-jnp.inf)
    rows = per_dev * BLOCK
    for lo in range(0, rows, TILE):
        q = q_ref[lo:lo + TILE, :]
        n_own = lo + TILE
        s_o = block_scores(q, k_ref[:n_own, :], scale)
        r_ids = lax.broadcasted_iota(jnp.int32, (TILE, n_own), 0)
        c_ids = lax.broadcasted_iota(jnp.int32, (TILE, n_own), 1)
        s_o = jnp.where(c_ids <= r_ids + lo, s_o, neg)
        m, l, acc = merge([(s_o, v_ref[:n_own, :])], None, None, None)
        acc_ref[lo:lo + TILE, :] = acc
        st_ref[lo:lo + TILE, :] = pack_stats(m, l, width)


def column_map(n_cols, values):
    seg = lax.broadcasted_iota(jnp.int32, (1, n_cols), 1) // BLOCK
    out = jnp.zeros((1, n_cols), jnp.int32)
    for j, value in enumerate(values):
        out = jnp.where(seg == j, value, out)
    return out


def prev_kernel(per_dev, width, scale, meta_ref, used_ref, q_ref, kp_ref, vp_ref, acc_ref, st_ref,
                acc_out, st_out, odd_ref):
    prev_ok = meta_ref[0] > 0
    neg = jnp.float32(-jnp.inf)
    rows = per_dev * BLOCK
    per_tile = TILE // BLOCK
    for lo in range(0, rows, TILE):
        q = q_ref[lo:lo + TILE, :]
        s_p = block_scores(q, kp_ref[...], scale)
        r_ids = lax.broadcasted_iota(jnp.int32, (TILE, rows), 0)
        c_ids = lax.broadcasted_iota(jnp.int32, (TILE, rows), 1)
        blocks = range(lo // BLOCK, lo // BLOCK + per_tile)
        r_blk = lax.broadcasted_iota(jnp.int32, (TILE, 1), 0) // BLOCK
        row_pick = jnp.zeros((TILE, 1), jnp.int32)
        row_used = jnp.zeros((TILE, 1), jnp.int32)
        for b, i in enumerate(blocks):
            row_pick = jnp.where(r_blk == b, meta_ref[1 + i], row_pick)
            row_used = jnp.where(r_blk == b, used_ref[i * NOFF], row_used)
        in_window = (c_ids > r_ids + lo) & prev_ok
        far_zero = ((c_ids // BLOCK) == row_pick) & (row_used > 0)
        s_p = jnp.where(in_window | far_zero, s_p, neg)
        st = st_ref[lo:lo + TILE, :]
        m, l, acc = merge(
            [(s_p, vp_ref[...])], st[:, 0:1], st[:, 1:2], acc_ref[lo:lo + TILE, :]
        )
        for b, i in enumerate(blocks):
            sl = slice(b * BLOCK, (b + 1) * BLOCK)
            half = (i // 2) * BLOCK
            if i % 2:
                odd_ref[half:half + BLOCK, :] = (acc[sl] / l[sl]).astype(odd_ref.dtype)
            else:
                acc_out[half:half + BLOCK, :] = acc[sl]
                st_out[half:half + BLOCK, :] = pack_stats(m[sl], l[sl], width)


def far_kernel(levels, per_dev, width, scale, meta_ref, used_ref, q_ref, acc_ref, st_ref, *rest):
    far_refs = rest[:-1]
    even_ref = rest[-1]
    neg = jnp.float32(-jnp.inf)
    n_even = per_dev // 2
    q = jnp.concatenate([q_ref[2 * e * BLOCK:(2 * e + 1) * BLOCK, :] for e in range(n_even)], axis=0)
    keys, vals, targets, flags = [], [], [], []
    pos = 0
    for level in levels:
        offset = 2**level
        n_src = 2 if level == 1 else 1
        refs = far_refs[pos:pos + 2 * n_src]
        pos += 2 * n_src
        k_lvl = refs[0][...]
        v_lvl = refs[1][...]
        if n_src == 2:
            odd = meta_ref[1 + per_dev] > 0
            k_lvl = jnp.where(odd, refs[2][...], k_lvl)
            v_lvl = jnp.where(odd, refs[3][...], v_lvl)
        keys.append(k_lvl)
        vals.append(v_lvl)
        for k in range(k_lvl.shape[0] // BLOCK):
            qblock = k * offset
            targets.append(qblock // 2)
            flags.append(used_ref[qblock * NOFF + level])
    k_far = jnp.concatenate(keys, axis=0)
    v_far = jnp.concatenate(vals, axis=0)
    n_keys = k_far.shape[0]
    s_f = block_scores(q, k_far, scale)
    col_target = column_map(n_keys, targets)
    col_flag = column_map(n_keys, flags)
    r_blk = lax.broadcasted_iota(jnp.int32, (n_even * BLOCK, n_keys), 0) // BLOCK
    s_f = jnp.where((r_blk == col_target) & (col_flag > 0), s_f, neg)
    st = st_ref[...]
    m, l, acc = merge([(s_f, v_far)], st[:, 0:1], st[:, 1:2], acc_ref[...])
    even_ref[...] = (acc / l).astype(even_ref.dtype)


def matmul_kernel(sel_ref, a_ref, w_ref, o_ref):
    o_ref[...] = jnp.dot(a_ref[...], w_ref[...], preferred_element_type=jnp.float32).astype(
        o_ref.dtype
    )


def project_half(attended, weight, half, tn=512):
    rows, depth = attended.shape
    cw = weight.shape[1] // 2
    steps = cw // tn
    return pl.pallas_call(
        matmul_kernel,
        out_shape=jax.ShapeDtypeStruct((rows, cw), jnp.bfloat16),
        grid_spec=pltpu.PrefetchScalarGridSpec(
            num_scalar_prefetch=1,
            grid=(steps,),
            in_specs=[
                pl.BlockSpec((rows, depth), lambda j, sel: (0, 0)),
                pl.BlockSpec((depth, tn), lambda j, sel: (0, sel[0] * steps + j)),
            ],
            out_specs=pl.BlockSpec((rows, tn), lambda j, sel: (0, j)),
        ),
        compiler_params=pltpu.CompilerParams(dimension_semantics=("arbitrary",)),
        cost_estimate=pl.CostEstimate(
            flops=2 * rows * depth * cw,
            transcendentals=0,
            bytes_accessed=2 * (rows * depth + depth * cw + rows * cw),
        ),
    )(jnp.reshape(half, (1,)).astype(jnp.int32), attended, weight)


def pick_blocks(kv, local):
    return jnp.concatenate(
        [lax.dynamic_slice_in_dim(kv, local[b] * BLOCK, BLOCK, axis=2) for b in range(local.shape[0])],
        axis=2,
    )


def per_device(queries, keys, values, far_blocks, out_weight):
    rows, heads, width = queries.shape
    per_dev = rows // BLOCK
    device = lax.axis_index("ctx")
    cycle_size = lax.axis_size("ctx")
    scale = 1.0 / math.sqrt(width)
    q_t = jnp.transpose(queries, (1, 0, 2))
    kv_t = jnp.stack([jnp.transpose(keys, (1, 0, 2)), jnp.transpose(values, (1, 0, 2))])
    prev_kv = from_behind(kv_t, "ctx", 1)
    levels = []
    sends = []
    for level in range(1, NOFF):
        offset = 2**level
        if offset >= cycle_size:
            continue
        target = lax.dynamic_slice_in_dim(far_blocks, (device + offset) * per_dev, per_dev, 0)[
            ::offset, level
        ]
        local = jnp.clip(target - device * per_dev, 0, per_dev - 1)
        if level == 1:
            pairs = [(s, s + 2) for s in range(0, cycle_size - 2, 2)]
            nxt = lax.dynamic_slice_in_dim(far_blocks, (device + 1) * per_dev, per_dev, 0)[::2, 1]
            fwd_local = jnp.clip(nxt - (device - 1) * per_dev, 0, per_dev - 1)
        else:
            pairs = [(s, s + offset) for s in range(0, cycle_size - offset)]
        sends.append((pick_blocks(kv_t, local), pairs))
        levels.append(level)
    q_t, kv_t, *operands = lax.optimization_barrier((q_t, kv_t, *[op for op, _ in sends]))
    far_arrays = []
    for (_, pairs), op, level in zip(sends, operands, levels):
        if level == 1:
            far_arrays.append((op, pairs))
        else:
            far_arrays.append((lax.ppermute(op, "ctx", pairs),))

    own = lax.dynamic_slice_in_dim(far_blocks, device * per_dev, per_dev, 0)
    query_index = device * per_dev + jnp.arange(per_dev, dtype=jnp.int32)
    used = (own <= (query_index - WINDOW // BLOCK - 1)[:, None]).astype(jnp.int32).reshape(-1)
    pick = jnp.clip(own[:, 0] - (device - 1) * per_dev, 0, per_dev - 1)
    meta = jnp.concatenate(
        [(device > 0).astype(jnp.int32)[None], pick.astype(jnp.int32), (device % 2)[None]]
    )

    hb = math.gcd(heads, HEADS_PER_STEP)
    row_spec = lambda n: pl.BlockSpec((hb, n, width), lambda h, *_: (h, 0, 0))
    out_spec = lambda n: pl.BlockSpec((n, hb * width), lambda h, *_: (0, h))
    k_spec = lambda n: pl.BlockSpec((None, hb, n, width), lambda h, *_: (0, h, 0, 0))
    v_spec = lambda n: pl.BlockSpec((None, hb, n, width), lambda h, *_: (1, h, 0, 0))
    half_rows = rows // 2
    f32 = jnp.float32
    params = pltpu.CompilerParams(dimension_semantics=("arbitrary",))
    state = lambda n: jax.ShapeDtypeStruct((heads, n, width), f32)

    def cost(keys_per_row, n_rows, extra_bytes):
        return pl.CostEstimate(
            flops=4 * n_rows * heads * width * keys_per_row,
            transcendentals=n_rows * heads * keys_per_row,
            bytes_accessed=extra_bytes,
        )

    acc0, st0 = pl.pallas_call(
        per_head(functools.partial(own_kernel, per_dev, width, scale), 0, 5, 0, width, hb),
        out_shape=(state(rows), state(rows)),
        grid=(heads // hb,),
        in_specs=[row_spec(rows), k_spec(rows), v_spec(rows)],
        out_specs=(row_spec(rows), row_spec(rows)),
        compiler_params=params,
        cost_estimate=cost(WINDOW // 2, rows, 2 * heads * rows * width * (3 * 2 + 2 * 4)),
    )(q_t, kv_t, kv_t)

    if levels and levels[0] == 1:
        direct_op, direct_pairs = far_arrays[0]
        prev_kv, acc0, st0, direct_op = lax.optimization_barrier((prev_kv, acc0, st0, direct_op))
        direct = lax.ppermute(direct_op, "ctx", direct_pairs)
        forwarded = lax.ppermute(
            pick_blocks(prev_kv, fwd_local), "ctx",
            [(s, s + 1) for s in range(0, cycle_size - 1, 2)],
        )
        far_arrays[0] = (direct, forwarded)
    else:
        prev_kv, acc0, st0 = lax.optimization_barrier((prev_kv, acc0, st0))
    far_specs, far_operands = [], []
    for group in far_arrays:
        for a in group:
            far_specs += [k_spec(a.shape[2]), v_spec(a.shape[2])]
            far_operands += [a, a]
    acc1, st1, att_odd = pl.pallas_call(
        per_head(functools.partial(prev_kernel, per_dev, width, scale), 2, 7, 1, width, hb),
        out_shape=(
            state(half_rows),
            state(half_rows),
            jax.ShapeDtypeStruct((half_rows, heads * width), queries.dtype),
        ),
        grid_spec=pltpu.PrefetchScalarGridSpec(
            num_scalar_prefetch=2,
            grid=(heads // hb,),
            in_specs=[row_spec(rows), k_spec(rows), v_spec(rows), row_spec(rows), row_spec(rows)],
            out_specs=(row_spec(half_rows), row_spec(half_rows), out_spec(half_rows)),
        ),
        compiler_params=params,
        cost_estimate=cost(WINDOW // 2 + BLOCK, rows, heads * rows * width * (3 * 2 + 2 * 4 + 8)),
    )(meta, used, q_t, prev_kv, prev_kv, acc0, st0)

    n_head = lax.axis_size("head")
    if n_head != 2:
        att_even = pl.pallas_call(
            per_head(functools.partial(far_kernel, levels, per_dev, width, scale), 2, 0, 1, width, hb),
            out_shape=jax.ShapeDtypeStruct((half_rows, heads * width), queries.dtype),
            grid_spec=pltpu.PrefetchScalarGridSpec(
                num_scalar_prefetch=2,
                grid=(heads // hb,),
                in_specs=[row_spec(rows), row_spec(half_rows), row_spec(half_rows)] + far_specs,
                out_specs=out_spec(half_rows),
            ),
            compiler_params=params,
            cost_estimate=cost(2 * BLOCK, half_rows, heads * width * (2 * rows + 8 * half_rows + 2 * sum(a.shape[2] for a in far_operands))),
        )(meta, used, q_t, acc1, st1, *far_operands)

        parts = []
        for att in (att_even, att_odd):
            partial_value = jnp.dot(att, out_weight, preferred_element_type=jnp.float32)
            parts.append(lax.psum_scatter(
                partial_value.astype(jnp.bfloat16), "head", scatter_dimension=1, tiled=True
            ))
    else:
        hidx = lax.axis_index("head")
        swap = [(0, 1), (1, 0)]
        received_odd = lax.ppermute(project_half(att_odd, out_weight, 1 - hidx), "head", swap)
        own_odd = project_half(att_odd, out_weight, hidx)
        acc1, st1, own_odd = lax.optimization_barrier((acc1, st1, own_odd))
        att_even = pl.pallas_call(
            per_head(functools.partial(far_kernel, levels, per_dev, width, scale), 2, 0, 1, width, hb),
            out_shape=jax.ShapeDtypeStruct((half_rows, heads * width), queries.dtype),
            grid_spec=pltpu.PrefetchScalarGridSpec(
                num_scalar_prefetch=2,
                grid=(heads // hb,),
                in_specs=[row_spec(rows), row_spec(half_rows), row_spec(half_rows)] + far_specs,
                out_specs=out_spec(half_rows),
            ),
            compiler_params=params,
            cost_estimate=cost(2 * BLOCK, half_rows, heads * width * (2 * rows + 8 * half_rows + 2 * sum(a.shape[2] for a in far_operands))),
        )(meta, used, q_t, acc1, st1, *far_operands)

        received_even = lax.ppermute(project_half(att_even, out_weight, 1 - hidx), "head", swap)
        own_even = project_half(att_even, out_weight, hidx)
        parts = [
            (own.astype(jnp.float32) + got.astype(jnp.float32)).astype(jnp.bfloat16)
            for own, got in ((own_even, received_even), (own_odd, received_odd))
        ]
    even, odd = (p.reshape(per_dev // 2, BLOCK, -1) for p in parts)
    return jnp.stack([even, odd], axis=1).reshape(rows, -1)


def solution(mesh):
    placed = (
        P("ctx", "head", None),
        P("ctx", "head", None),
        P("ctx", "head", None),
        P(),
        P("head", None),
    )
    return jax.shard_map(
        per_device, mesh=mesh, in_specs=placed, out_specs=P("ctx", "head"), check_vma=False
    )
```

```python
import functools
import math

import jax
import jax.numpy as jnp
from jax import lax
from jax.experimental import pallas as pl
from jax.experimental.pallas import tpu as pltpu
from jax.sharding import PartitionSpec as P

BLOCK = 64
WINDOW = 512
NOFF = 5
HEADS_PER_STEP = 4


def from_behind(value, axis, steps):
    count = lax.axis_size(axis)
    initial, last = (max(0, -steps), min(count, count - steps))
    return lax.ppermute(value, axis, [(source, source + steps) for source in range(initial, last)])


def block_scores(q, keys, scale):
    return lax.dot_general(
        q, keys, (((1,), (1,)), ((), ())), preferred_element_type=jnp.float32
    ) * scale


def merge(pieces, m_old, l_old, acc_old):
    top = m_old
    for s, _ in pieces:
        row_max = s.max(axis=1, keepdims=True)
        top = row_max if top is None else jnp.maximum(top, row_max)
    total = None
    summed = None
    for s, v in pieces:
        p = jnp.exp(s - top)
        part_total = p.sum(axis=1, keepdims=True)
        part = jnp.dot(p.astype(jnp.bfloat16), v, preferred_element_type=jnp.float32)
        total = part_total if total is None else total + part_total
        summed = part if summed is None else summed + part
    if m_old is not None:
        alpha = jnp.exp(m_old - top)
        total = total + l_old * alpha
        summed = summed + acc_old * alpha
    return top, total, summed


def pack_stats(m, l, width):
    lane = lax.broadcasted_iota(jnp.int32, (m.shape[0], width), 1)
    return jnp.where(lane == 0, m, jnp.where(lane == 1, l, 0.0))


TILE = 256


class HeadView:
    def __init__(self, ref, head, width=None):
        self.ref, self.head, self.width = ref, head, width

    def _index(self, idx):
        if idx is Ellipsis:
            idx = (slice(None), slice(None))
        if self.width is None:
            return (self.head,) + tuple(idx)
        return (idx[0], pl.ds(self.head * self.width, self.width))

    @property
    def dtype(self):
        return self.ref.dtype

    def __getitem__(self, idx):
        return self.ref[self._index(idx)]

    def __setitem__(self, idx, value):
        self.ref[self._index(idx)] = value


def per_head(body, n_prefetch, n_head_major, n_rows_out, width, heads_per_step):
    def kernel(*refs):
        pre = refs[:n_prefetch]
        rest = refs[n_prefetch:]
        n_major = len(rest) - n_rows_out
        for hh in range(heads_per_step):
            views = [HeadView(r, hh) for r in rest[:n_major]]
            outs = [HeadView(r, hh, width) for r in rest[n_major:]]
            body(*pre, *views, *outs)

    return kernel


def own_kernel(per_dev, width, scale, q_ref, k_ref, v_ref, acc_ref, st_ref):
    neg = jnp.float32(-jnp.inf)
    rows = per_dev * BLOCK
    for lo in range(0, rows, TILE):
        q = q_ref[lo:lo + TILE, :]
        n_own = lo + TILE
        s_o = block_scores(q, k_ref[:n_own, :], scale)
        r_ids = lax.broadcasted_iota(jnp.int32, (TILE, n_own), 0)
        c_ids = lax.broadcasted_iota(jnp.int32, (TILE, n_own), 1)
        s_o = jnp.where(c_ids <= r_ids + lo, s_o, neg)
        m, l, acc = merge([(s_o, v_ref[:n_own, :])], None, None, None)
        acc_ref[lo:lo + TILE, :] = acc
        st_ref[lo:lo + TILE, :] = pack_stats(m, l, width)


def column_map(n_cols, values):
    seg = lax.broadcasted_iota(jnp.int32, (1, n_cols), 1) // BLOCK
    out = jnp.zeros((1, n_cols), jnp.int32)
    for j, value in enumerate(values):
        out = jnp.where(seg == j, value, out)
    return out


def prev_kernel(per_dev, width, scale, meta_ref, used_ref, q_ref, kp_ref, vp_ref, acc_ref, st_ref,
                acc_out, st_out, odd_ref):
    prev_ok = meta_ref[0] > 0
    neg = jnp.float32(-jnp.inf)
    rows = per_dev * BLOCK
    per_tile = TILE // BLOCK
    for lo in range(0, rows, TILE):
        q = q_ref[lo:lo + TILE, :]
        n_prev = rows - lo
        s_p = block_scores(q, kp_ref[lo:, :], scale)
        r_ids = lax.broadcasted_iota(jnp.int32, (TILE, n_prev), 0)
        c_ids = lax.broadcasted_iota(jnp.int32, (TILE, n_prev), 1)
        s_p = jnp.where((c_ids > r_ids) & prev_ok, s_p, neg)
        blocks = range(lo // BLOCK, lo // BLOCK + per_tile)
        starts = [pl.multiple_of(meta_ref[1 + i] * BLOCK, BLOCK) for i in blocks]
        k0 = jnp.concatenate([kp_ref[pl.ds(st, BLOCK), :] for st in starts], axis=0)
        v0 = jnp.concatenate([vp_ref[pl.ds(st, BLOCK), :] for st in starts], axis=0)
        s_f = block_scores(q, k0, scale)
        flags = column_map(TILE, [used_ref[i * NOFF] for i in blocks])
        r_blk = lax.broadcasted_iota(jnp.int32, (TILE, TILE), 0) // BLOCK
        c_blk = lax.broadcasted_iota(jnp.int32, (TILE, TILE), 1) // BLOCK
        s_f = jnp.where((r_blk == c_blk) & (flags > 0), s_f, neg)
        st = st_ref[lo:lo + TILE, :]
        m, l, acc = merge(
            [(s_p, vp_ref[lo:, :]), (s_f, v0)], st[:, 0:1], st[:, 1:2], acc_ref[lo:lo + TILE, :]
        )
        for b, i in enumerate(blocks):
            sl = slice(b * BLOCK, (b + 1) * BLOCK)
            half = (i // 2) * BLOCK
            if i % 2:
                odd_ref[half:half + BLOCK, :] = (acc[sl] / l[sl]).astype(odd_ref.dtype)
            else:
                acc_out[half:half + BLOCK, :] = acc[sl]
                st_out[half:half + BLOCK, :] = pack_stats(m[sl], l[sl], width)


def far_kernel(levels, per_dev, width, scale, meta_ref, used_ref, q_ref, acc_ref, st_ref, *rest):
    far_refs = rest[:-1]
    even_ref = rest[-1]
    neg = jnp.float32(-jnp.inf)
    n_even = per_dev // 2
    q = jnp.concatenate([q_ref[2 * e * BLOCK:(2 * e + 1) * BLOCK, :] for e in range(n_even)], axis=0)
    keys, vals, targets, flags = [], [], [], []
    pos = 0
    for level in levels:
        offset = 2**level
        n_src = 2 if level == 1 else 1
        refs = far_refs[pos:pos + 2 * n_src]
        pos += 2 * n_src
        k_lvl = refs[0][...]
        v_lvl = refs[1][...]
        if n_src == 2:
            odd = meta_ref[1 + per_dev] > 0
            k_lvl = jnp.where(odd, refs[2][...], k_lvl)
            v_lvl = jnp.where(odd, refs[3][...], v_lvl)
        keys.append(k_lvl)
        vals.append(v_lvl)
        for k in range(k_lvl.shape[0] // BLOCK):
            qblock = k * offset
            targets.append(qblock // 2)
            flags.append(used_ref[qblock * NOFF + level])
    k_far = jnp.concatenate(keys, axis=0)
    v_far = jnp.concatenate(vals, axis=0)
    n_keys = k_far.shape[0]
    s_f = block_scores(q, k_far, scale)
    col_target = column_map(n_keys, targets)
    col_flag = column_map(n_keys, flags)
    r_blk = lax.broadcasted_iota(jnp.int32, (n_even * BLOCK, n_keys), 0) // BLOCK
    s_f = jnp.where((r_blk == col_target) & (col_flag > 0), s_f, neg)
    st = st_ref[...]
    m, l, acc = merge([(s_f, v_far)], st[:, 0:1], st[:, 1:2], acc_ref[...])
    even_ref[...] = (acc / l).astype(even_ref.dtype)


def matmul_kernel(sel_ref, a_ref, w_ref, o_ref):
    o_ref[...] = jnp.dot(a_ref[...], w_ref[...], preferred_element_type=jnp.float32).astype(
        o_ref.dtype
    )


def project_half(attended, weight, half, tn=512):
    rows, depth = attended.shape
    cw = weight.shape[1] // 2
    steps = cw // tn
    return pl.pallas_call(
        matmul_kernel,
        out_shape=jax.ShapeDtypeStruct((rows, cw), jnp.bfloat16),
        grid_spec=pltpu.PrefetchScalarGridSpec(
            num_scalar_prefetch=1,
            grid=(steps,),
            in_specs=[
                pl.BlockSpec((rows, depth), lambda j, sel: (0, 0)),
                pl.BlockSpec((depth, tn), lambda j, sel: (0, sel[0] * steps + j)),
            ],
            out_specs=pl.BlockSpec((rows, tn), lambda j, sel: (0, j)),
        ),
        compiler_params=pltpu.CompilerParams(dimension_semantics=("arbitrary",)),
        cost_estimate=pl.CostEstimate(
            flops=2 * rows * depth * cw,
            transcendentals=0,
            bytes_accessed=2 * (rows * depth + depth * cw + rows * cw),
        ),
    )(jnp.reshape(half, (1,)).astype(jnp.int32), attended, weight)


def pick_blocks(kv, local):
    return jnp.concatenate(
        [lax.dynamic_slice_in_dim(kv, local[b] * BLOCK, BLOCK, axis=2) for b in range(local.shape[0])],
        axis=2,
    )


def per_device(queries, keys, values, far_blocks, out_weight):
    rows, heads, width = queries.shape
    per_dev = rows // BLOCK
    device = lax.axis_index("ctx")
    cycle_size = lax.axis_size("ctx")
    scale = 1.0 / math.sqrt(width)
    q_t = jnp.transpose(queries, (1, 0, 2))
    kv_t = jnp.stack([jnp.transpose(keys, (1, 0, 2)), jnp.transpose(values, (1, 0, 2))])
    prev_kv = from_behind(kv_t, "ctx", 1)
    levels = []
    sends = []
    for level in range(1, NOFF):
        offset = 2**level
        if offset >= cycle_size:
            continue
        target = lax.dynamic_slice_in_dim(far_blocks, (device + offset) * per_dev, per_dev, 0)[
            ::offset, level
        ]
        local = jnp.clip(target - device * per_dev, 0, per_dev - 1)
        if level == 1:
            pairs = [(s, s + 2) for s in range(0, cycle_size - 2, 2)]
            nxt = lax.dynamic_slice_in_dim(far_blocks, (device + 1) * per_dev, per_dev, 0)[::2, 1]
            fwd_local = jnp.clip(nxt - (device - 1) * per_dev, 0, per_dev - 1)
        else:
            pairs = [(s, s + offset) for s in range(0, cycle_size - offset)]
        sends.append((pick_blocks(kv_t, local), pairs))
        levels.append(level)
    q_t, kv_t, *operands = lax.optimization_barrier((q_t, kv_t, *[op for op, _ in sends]))
    far_arrays = []
    for (_, pairs), op, level in zip(sends, operands, levels):
        if level == 1:
            far_arrays.append((op, pairs))
        else:
            far_arrays.append((lax.ppermute(op, "ctx", pairs),))

    own = lax.dynamic_slice_in_dim(far_blocks, device * per_dev, per_dev, 0)
    query_index = device * per_dev + jnp.arange(per_dev, dtype=jnp.int32)
    used = (own <= (query_index - WINDOW // BLOCK - 1)[:, None]).astype(jnp.int32).reshape(-1)
    pick = jnp.clip(own[:, 0] - (device - 1) * per_dev, 0, per_dev - 1)
    meta = jnp.concatenate(
        [(device > 0).astype(jnp.int32)[None], pick.astype(jnp.int32), (device % 2)[None]]
    )

    hb = math.gcd(heads, HEADS_PER_STEP)
    row_spec = lambda n: pl.BlockSpec((hb, n, width), lambda h, *_: (h, 0, 0))
    out_spec = lambda n: pl.BlockSpec((n, hb * width), lambda h, *_: (0, h))
    k_spec = lambda n: pl.BlockSpec((None, hb, n, width), lambda h, *_: (0, h, 0, 0))
    v_spec = lambda n: pl.BlockSpec((None, hb, n, width), lambda h, *_: (1, h, 0, 0))
    half_rows = rows // 2
    f32 = jnp.float32
    params = pltpu.CompilerParams(dimension_semantics=("arbitrary",))
    state = lambda n: jax.ShapeDtypeStruct((heads, n, width), f32)

    def cost(keys_per_row, n_rows, extra_bytes):
        return pl.CostEstimate(
            flops=4 * n_rows * heads * width * keys_per_row,
            transcendentals=n_rows * heads * keys_per_row,
            bytes_accessed=extra_bytes,
        )

    acc0, st0 = pl.pallas_call(
        per_head(functools.partial(own_kernel, per_dev, width, scale), 0, 5, 0, width, hb),
        out_shape=(state(rows), state(rows)),
        grid=(heads // hb,),
        in_specs=[row_spec(rows), k_spec(rows), v_spec(rows)],
        out_specs=(row_spec(rows), row_spec(rows)),
        compiler_params=params,
        cost_estimate=cost(WINDOW // 2, rows, 2 * heads * rows * width * (3 * 2 + 2 * 4)),
    )(q_t, kv_t, kv_t)

    if levels and levels[0] == 1:
        direct_op, direct_pairs = far_arrays[0]
        tied = [g[0] for g in far_arrays[1:]]
        prev_kv, acc0, st0, direct_op, tied = lax.optimization_barrier(
            (prev_kv, acc0, st0, direct_op, tied)
        )
        far_arrays[1:] = [(t,) for t in tied]
        direct = lax.ppermute(direct_op, "ctx", direct_pairs)
        forwarded = lax.ppermute(
            pick_blocks(prev_kv, fwd_local), "ctx",
            [(s, s + 1) for s in range(0, cycle_size - 1, 2)],
        )
        far_arrays[0] = (direct, forwarded)
    else:
        prev_kv, acc0, st0 = lax.optimization_barrier((prev_kv, acc0, st0))
    far_specs, far_operands = [], []
    for group in far_arrays:
        for a in group:
            far_specs += [k_spec(a.shape[2]), v_spec(a.shape[2])]
            far_operands += [a, a]
    acc1, st1, att_odd = pl.pallas_call(
        per_head(functools.partial(prev_kernel, per_dev, width, scale), 2, 7, 1, width, hb),
        out_shape=(
            state(half_rows),
            state(half_rows),
            jax.ShapeDtypeStruct((half_rows, heads * width), queries.dtype),
        ),
        grid_spec=pltpu.PrefetchScalarGridSpec(
            num_scalar_prefetch=2,
            grid=(heads // hb,),
            in_specs=[row_spec(rows), k_spec(rows), v_spec(rows), row_spec(rows), row_spec(rows)],
            out_specs=(row_spec(half_rows), row_spec(half_rows), out_spec(half_rows)),
        ),
        compiler_params=params,
        cost_estimate=cost(WINDOW // 2 + BLOCK, rows, heads * rows * width * (3 * 2 + 2 * 4 + 8)),
    )(meta, used, q_t, prev_kv, prev_kv, acc0, st0)

    n_head = lax.axis_size("head")
    if n_head != 2:
        att_even = pl.pallas_call(
            per_head(functools.partial(far_kernel, levels, per_dev, width, scale), 2, 0, 1, width, hb),
            out_shape=jax.ShapeDtypeStruct((half_rows, heads * width), queries.dtype),
            grid_spec=pltpu.PrefetchScalarGridSpec(
                num_scalar_prefetch=2,
                grid=(heads // hb,),
                in_specs=[row_spec(rows), row_spec(half_rows), row_spec(half_rows)] + far_specs,
                out_specs=out_spec(half_rows),
            ),
            compiler_params=params,
            cost_estimate=cost(2 * BLOCK, half_rows, heads * width * (2 * rows + 8 * half_rows + 2 * sum(a.shape[2] for a in far_operands))),
        )(meta, used, q_t, acc1, st1, *far_operands)

        parts = []
        for att in (att_even, att_odd):
            partial_value = jnp.dot(att, out_weight, preferred_element_type=jnp.float32)
            parts.append(lax.psum_scatter(
                partial_value.astype(jnp.bfloat16), "head", scatter_dimension=1, tiled=True
            ))
    else:
        hidx = lax.axis_index("head")
        swap = [(0, 1), (1, 0)]
        received_odd = lax.ppermute(project_half(att_odd, out_weight, 1 - hidx), "head", swap)
        own_odd = project_half(att_odd, out_weight, hidx)
        acc1, st1, own_odd = lax.optimization_barrier((acc1, st1, own_odd))
        att_even = pl.pallas_call(
            per_head(functools.partial(far_kernel, levels, per_dev, width, scale), 2, 0, 1, width, hb),
            out_shape=jax.ShapeDtypeStruct((half_rows, heads * width), queries.dtype),
            grid_spec=pltpu.PrefetchScalarGridSpec(
                num_scalar_prefetch=2,
                grid=(heads // hb,),
                in_specs=[row_spec(rows), row_spec(half_rows), row_spec(half_rows)] + far_specs,
                out_specs=out_spec(half_rows),
            ),
            compiler_params=params,
            cost_estimate=cost(2 * BLOCK, half_rows, heads * width * (2 * rows + 8 * half_rows + 2 * sum(a.shape[2] for a in far_operands))),
        )(meta, used, q_t, acc1, st1, *far_operands)

        received_even = lax.ppermute(project_half(att_even, out_weight, 1 - hidx), "head", swap)
        own_even = project_half(att_even, out_weight, hidx)
        parts = [
            (own.astype(jnp.float32) + got.astype(jnp.float32)).astype(jnp.bfloat16)
            for own, got in ((own_even, received_even), (own_odd, received_odd))
        ]
    even, odd = (p.reshape(per_dev // 2, BLOCK, -1) for p in parts)
    return jnp.stack([even, odd], axis=1).reshape(rows, -1)


def solution(mesh):
    placed = (
        P("ctx", "head", None),
        P("ctx", "head", None),
        P("ctx", "head", None),
        P(),
        P("head", None),
    )
    return jax.shard_map(
        per_device, mesh=mesh, in_specs=placed, out_specs=P("ctx", "head"), check_vma=False
    )
```

```python
import functools
import math

import jax
import jax.numpy as jnp
from jax import lax
from jax.experimental import pallas as pl
from jax.experimental.pallas import tpu as pltpu
from jax.sharding import PartitionSpec as P

BLOCK = 64
WINDOW = 512
NOFF = 5
HEADS_PER_STEP = 4


def from_behind(value, axis, steps):
    count = lax.axis_size(axis)
    initial, last = (max(0, -steps), min(count, count - steps))
    return lax.ppermute(value, axis, [(source, source + steps) for source in range(initial, last)])


def block_scores(q, keys, scale):
    return lax.dot_general(
        q, keys, (((1,), (1,)), ((), ())), preferred_element_type=jnp.float32
    ) * scale


def merge(pieces, m_old, l_old, acc_old):
    top = m_old
    for s, _ in pieces:
        row_max = s.max(axis=1, keepdims=True)
        top = row_max if top is None else jnp.maximum(top, row_max)
    total = None
    summed = None
    for s, v in pieces:
        p = jnp.exp(s - top)
        part_total = p.sum(axis=1, keepdims=True)
        part = jnp.dot(p.astype(jnp.bfloat16), v, preferred_element_type=jnp.float32)
        total = part_total if total is None else total + part_total
        summed = part if summed is None else summed + part
    if m_old is not None:
        alpha = jnp.exp(m_old - top)
        total = total + l_old * alpha
        summed = summed + acc_old * alpha
    return top, total, summed


def pack_stats(m, l, width):
    lane = lax.broadcasted_iota(jnp.int32, (m.shape[0], width), 1)
    return jnp.where(lane == 0, m, jnp.where(lane == 1, l, 0.0))


TILE = 256


class HeadView:
    def __init__(self, ref, head, width=None):
        self.ref, self.head, self.width = ref, head, width

    def _index(self, idx):
        if idx is Ellipsis:
            idx = (slice(None), slice(None))
        if self.width is None:
            return (self.head,) + tuple(idx)
        return (idx[0], pl.ds(self.head * self.width, self.width))

    @property
    def dtype(self):
        return self.ref.dtype

    def __getitem__(self, idx):
        return self.ref[self._index(idx)]

    def __setitem__(self, idx, value):
        self.ref[self._index(idx)] = value


def per_head(body, n_prefetch, n_head_major, n_rows_out, width, heads_per_step):
    def kernel(*refs):
        pre = refs[:n_prefetch]
        rest = refs[n_prefetch:]
        n_major = len(rest) - n_rows_out
        for hh in range(heads_per_step):
            views = [HeadView(r, hh) for r in rest[:n_major]]
            outs = [HeadView(r, hh, width) for r in rest[n_major:]]
            body(*pre, *views, *outs)

    return kernel


def own_kernel(per_dev, width, scale, q_ref, k_ref, v_ref, acc_ref, st_ref):
    neg = jnp.float32(-jnp.inf)
    rows = per_dev * BLOCK
    for lo in range(0, rows, TILE):
        q = q_ref[lo:lo + TILE, :]
        n_own = lo + TILE
        s_o = block_scores(q, k_ref[:n_own, :], scale)
        r_ids = lax.broadcasted_iota(jnp.int32, (TILE, n_own), 0)
        c_ids = lax.broadcasted_iota(jnp.int32, (TILE, n_own), 1)
        s_o = jnp.where(c_ids <= r_ids + lo, s_o, neg)
        m, l, acc = merge([(s_o, v_ref[:n_own, :])], None, None, None)
        acc_ref[lo:lo + TILE, :] = acc
        st_ref[lo:lo + TILE, :] = pack_stats(m, l, width)


def column_map(n_cols, values):
    seg = lax.broadcasted_iota(jnp.int32, (1, n_cols), 1) // BLOCK
    out = jnp.zeros((1, n_cols), jnp.int32)
    for j, value in enumerate(values):
        out = jnp.where(seg == j, value, out)
    return out


def prev_kernel(per_dev, width, scale, meta_ref, used_ref, q_ref, kp_ref, vp_ref, acc_ref, st_ref,
                acc_out, st_out, odd_ref):
    prev_ok = meta_ref[0] > 0
    neg = jnp.float32(-jnp.inf)
    rows = per_dev * BLOCK
    per_tile = TILE // BLOCK
    for lo in range(0, rows, TILE):
        q = q_ref[lo:lo + TILE, :]
        n_prev = rows - lo
        s_p = block_scores(q, kp_ref[lo:, :], scale)
        r_ids = lax.broadcasted_iota(jnp.int32, (TILE, n_prev), 0)
        c_ids = lax.broadcasted_iota(jnp.int32, (TILE, n_prev), 1)
        s_p = jnp.where((c_ids > r_ids) & prev_ok, s_p, neg)
        blocks = range(lo // BLOCK, lo // BLOCK + per_tile)
        starts = [pl.multiple_of(meta_ref[1 + i] * BLOCK, BLOCK) for i in blocks]
        k0 = jnp.concatenate([kp_ref[pl.ds(st, BLOCK), :] for st in starts], axis=0)
        v0 = jnp.concatenate([vp_ref[pl.ds(st, BLOCK), :] for st in starts], axis=0)
        s_f = block_scores(q, k0, scale)
        flags = column_map(TILE, [used_ref[i * NOFF] for i in blocks])
        r_blk = lax.broadcasted_iota(jnp.int32, (TILE, TILE), 0) // BLOCK
        c_blk = lax.broadcasted_iota(jnp.int32, (TILE, TILE), 1) // BLOCK
        s_f = jnp.where((r_blk == c_blk) & (flags > 0), s_f, neg)
        st = st_ref[lo:lo + TILE, :]
        m, l, acc = merge(
            [(s_p, vp_ref[lo:, :]), (s_f, v0)], st[:, 0:1], st[:, 1:2], acc_ref[lo:lo + TILE, :]
        )
        for b, i in enumerate(blocks):
            sl = slice(b * BLOCK, (b + 1) * BLOCK)
            half = (i // 2) * BLOCK
            if i % 2:
                odd_ref[half:half + BLOCK, :] = (acc[sl] / l[sl]).astype(odd_ref.dtype)
            else:
                acc_out[half:half + BLOCK, :] = acc[sl]
                st_out[half:half + BLOCK, :] = pack_stats(m[sl], l[sl], width)


def far_kernel(levels, per_dev, width, scale, meta_ref, used_ref, q_ref, acc_ref, st_ref, *rest):
    far_refs = rest[:-1]
    even_ref = rest[-1]
    neg = jnp.float32(-jnp.inf)
    n_even = per_dev // 2
    q = jnp.concatenate([q_ref[2 * e * BLOCK:(2 * e + 1) * BLOCK, :] for e in range(n_even)], axis=0)
    keys, vals, targets, flags = [], [], [], []
    pos = 0
    for level in levels:
        offset = 2**level
        n_src = 2 if level == 1 else 1
        refs = far_refs[pos:pos + 2 * n_src]
        pos += 2 * n_src
        k_lvl = refs[0][...]
        v_lvl = refs[1][...]
        if n_src == 2:
            odd = meta_ref[1 + per_dev] > 0
            k_lvl = jnp.where(odd, refs[2][...], k_lvl)
            v_lvl = jnp.where(odd, refs[3][...], v_lvl)
        keys.append(k_lvl)
        vals.append(v_lvl)
        for k in range(k_lvl.shape[0] // BLOCK):
            qblock = k * offset
            targets.append(qblock // 2)
            flags.append(used_ref[qblock * NOFF + level])
    k_far = jnp.concatenate(keys, axis=0)
    v_far = jnp.concatenate(vals, axis=0)
    n_keys = k_far.shape[0]
    s_f = block_scores(q, k_far, scale)
    col_target = column_map(n_keys, targets)
    col_flag = column_map(n_keys, flags)
    r_blk = lax.broadcasted_iota(jnp.int32, (n_even * BLOCK, n_keys), 0) // BLOCK
    s_f = jnp.where((r_blk == col_target) & (col_flag > 0), s_f, neg)
    st = st_ref[...]
    m, l, acc = merge([(s_f, v_far)], st[:, 0:1], st[:, 1:2], acc_ref[...])
    even_ref[...] = (acc / l).astype(even_ref.dtype)


def matmul_kernel(sel_ref, a_ref, w_ref, o_ref):
    o_ref[...] = jnp.dot(a_ref[...], w_ref[...], preferred_element_type=jnp.float32).astype(
        o_ref.dtype
    )


def project_half(attended, weight, half, tn=512, part=0, parts=1):
    rows, depth = attended.shape
    cw = weight.shape[1] // 2
    total_steps = cw // tn
    steps = total_steps // parts
    first = part * steps
    cw = steps * tn
    return pl.pallas_call(
        matmul_kernel,
        out_shape=jax.ShapeDtypeStruct((rows, cw), jnp.bfloat16),
        grid_spec=pltpu.PrefetchScalarGridSpec(
            num_scalar_prefetch=1,
            grid=(steps,),
            in_specs=[
                pl.BlockSpec((rows, depth), lambda j, sel: (0, 0)),
                pl.BlockSpec((depth, tn), lambda j, sel: (0, sel[0] * total_steps + first + j)),
            ],
            out_specs=pl.BlockSpec((rows, tn), lambda j, sel: (0, j)),
        ),
        compiler_params=pltpu.CompilerParams(dimension_semantics=("arbitrary",)),
        cost_estimate=pl.CostEstimate(
            flops=2 * rows * depth * cw,
            transcendentals=0,
            bytes_accessed=2 * (rows * depth + depth * cw + rows * cw),
        ),
    )(jnp.reshape(half, (1,)).astype(jnp.int32), attended, weight)


def pick_blocks(kv, local):
    return jnp.concatenate(
        [lax.dynamic_slice_in_dim(kv, local[b] * BLOCK, BLOCK, axis=2) for b in range(local.shape[0])],
        axis=2,
    )


def per_device(queries, keys, values, far_blocks, out_weight):
    rows, heads, width = queries.shape
    per_dev = rows // BLOCK
    device = lax.axis_index("ctx")
    cycle_size = lax.axis_size("ctx")
    scale = 1.0 / math.sqrt(width)
    q_t = jnp.transpose(queries, (1, 0, 2))
    kv_t = jnp.stack([jnp.transpose(keys, (1, 0, 2)), jnp.transpose(values, (1, 0, 2))])
    prev_kv = from_behind(kv_t, "ctx", 1)
    levels = []
    sends = []
    for level in range(1, NOFF):
        offset = 2**level
        if offset >= cycle_size:
            continue
        target = lax.dynamic_slice_in_dim(far_blocks, (device + offset) * per_dev, per_dev, 0)[
            ::offset, level
        ]
        local = jnp.clip(target - device * per_dev, 0, per_dev - 1)
        if level == 1:
            pairs = [(s, s + 2) for s in range(0, cycle_size - 2, 2)]
            nxt = lax.dynamic_slice_in_dim(far_blocks, (device + 1) * per_dev, per_dev, 0)[::2, 1]
            fwd_local = jnp.clip(nxt - (device - 1) * per_dev, 0, per_dev - 1)
        else:
            pairs = [(s, s + offset) for s in range(0, cycle_size - offset)]
        sends.append((pick_blocks(kv_t, local), pairs))
        levels.append(level)
    q_t, kv_t, *operands = lax.optimization_barrier((q_t, kv_t, *[op for op, _ in sends]))
    far_arrays = []
    for (_, pairs), op, level in zip(sends, operands, levels):
        if level == 1:
            far_arrays.append((op, pairs))
        else:
            far_arrays.append((lax.ppermute(op, "ctx", pairs),))

    own = lax.dynamic_slice_in_dim(far_blocks, device * per_dev, per_dev, 0)
    query_index = device * per_dev + jnp.arange(per_dev, dtype=jnp.int32)
    used = (own <= (query_index - WINDOW // BLOCK - 1)[:, None]).astype(jnp.int32).reshape(-1)
    pick = jnp.clip(own[:, 0] - (device - 1) * per_dev, 0, per_dev - 1)
    meta = jnp.concatenate(
        [(device > 0).astype(jnp.int32)[None], pick.astype(jnp.int32), (device % 2)[None]]
    )

    hb = math.gcd(heads, HEADS_PER_STEP)
    row_spec = lambda n: pl.BlockSpec((hb, n, width), lambda h, *_: (h, 0, 0))
    out_spec = lambda n: pl.BlockSpec((n, hb * width), lambda h, *_: (0, h))
    k_spec = lambda n: pl.BlockSpec((None, hb, n, width), lambda h, *_: (0, h, 0, 0))
    v_spec = lambda n: pl.BlockSpec((None, hb, n, width), lambda h, *_: (1, h, 0, 0))
    half_rows = rows // 2
    f32 = jnp.float32
    params = pltpu.CompilerParams(dimension_semantics=("arbitrary",))
    state = lambda n: jax.ShapeDtypeStruct((heads, n, width), f32)

    def cost(keys_per_row, n_rows, extra_bytes):
        return pl.CostEstimate(
            flops=4 * n_rows * heads * width * keys_per_row,
            transcendentals=n_rows * heads * keys_per_row,
            bytes_accessed=extra_bytes,
        )

    acc0, st0 = pl.pallas_call(
        per_head(functools.partial(own_kernel, per_dev, width, scale), 0, 5, 0, width, hb),
        out_shape=(state(rows), state(rows)),
        grid=(heads // hb,),
        in_specs=[row_spec(rows), k_spec(rows), v_spec(rows)],
        out_specs=(row_spec(rows), row_spec(rows)),
        compiler_params=params,
        cost_estimate=cost(WINDOW // 2, rows, 2 * heads * rows * width * (3 * 2 + 2 * 4)),
    )(q_t, kv_t, kv_t)

    if levels and levels[0] == 1:
        direct_op, direct_pairs = far_arrays[0]
        prev_kv, acc0, st0, direct_op = lax.optimization_barrier((prev_kv, acc0, st0, direct_op))
        direct = lax.ppermute(direct_op, "ctx", direct_pairs)
        forwarded = lax.ppermute(
            pick_blocks(prev_kv, fwd_local), "ctx",
            [(s, s + 1) for s in range(0, cycle_size - 1, 2)],
        )
        far_arrays[0] = (direct, forwarded)
    else:
        prev_kv, acc0, st0 = lax.optimization_barrier((prev_kv, acc0, st0))
    far_specs, far_operands = [], []
    for group in far_arrays:
        for a in group:
            far_specs += [k_spec(a.shape[2]), v_spec(a.shape[2])]
            far_operands += [a, a]
    acc1, st1, att_odd = pl.pallas_call(
        per_head(functools.partial(prev_kernel, per_dev, width, scale), 2, 7, 1, width, hb),
        out_shape=(
            state(half_rows),
            state(half_rows),
            jax.ShapeDtypeStruct((half_rows, heads * width), queries.dtype),
        ),
        grid_spec=pltpu.PrefetchScalarGridSpec(
            num_scalar_prefetch=2,
            grid=(heads // hb,),
            in_specs=[row_spec(rows), k_spec(rows), v_spec(rows), row_spec(rows), row_spec(rows)],
            out_specs=(row_spec(half_rows), row_spec(half_rows), out_spec(half_rows)),
        ),
        compiler_params=params,
        cost_estimate=cost(WINDOW // 2 + BLOCK, rows, heads * rows * width * (3 * 2 + 2 * 4 + 8)),
    )(meta, used, q_t, prev_kv, prev_kv, acc0, st0)

    n_head = lax.axis_size("head")
    if n_head != 2:
        att_even = pl.pallas_call(
            per_head(functools.partial(far_kernel, levels, per_dev, width, scale), 2, 0, 1, width, hb),
            out_shape=jax.ShapeDtypeStruct((half_rows, heads * width), queries.dtype),
            grid_spec=pltpu.PrefetchScalarGridSpec(
                num_scalar_prefetch=2,
                grid=(heads // hb,),
                in_specs=[row_spec(rows), row_spec(half_rows), row_spec(half_rows)] + far_specs,
                out_specs=out_spec(half_rows),
            ),
            compiler_params=params,
            cost_estimate=cost(2 * BLOCK, half_rows, heads * width * (2 * rows + 8 * half_rows + 2 * sum(a.shape[2] for a in far_operands))),
        )(meta, used, q_t, acc1, st1, *far_operands)

        parts = []
        for att in (att_even, att_odd):
            partial_value = jnp.dot(att, out_weight, preferred_element_type=jnp.float32)
            parts.append(lax.psum_scatter(
                partial_value.astype(jnp.bfloat16), "head", scatter_dimension=1, tiled=True
            ))
    else:
        hidx = lax.axis_index("head")
        swap = [(0, 1), (1, 0)]
        received_odd = lax.ppermute(project_half(att_odd, out_weight, 1 - hidx), "head", swap)
        own_odd = project_half(att_odd, out_weight, hidx)
        acc1, st1, own_odd = lax.optimization_barrier((acc1, st1, own_odd))
        att_even = pl.pallas_call(
            per_head(functools.partial(far_kernel, levels, per_dev, width, scale), 2, 0, 1, width, hb),
            out_shape=jax.ShapeDtypeStruct((half_rows, heads * width), queries.dtype),
            grid_spec=pltpu.PrefetchScalarGridSpec(
                num_scalar_prefetch=2,
                grid=(heads // hb,),
                in_specs=[row_spec(rows), row_spec(half_rows), row_spec(half_rows)] + far_specs,
                out_specs=out_spec(half_rows),
            ),
            compiler_params=params,
            cost_estimate=cost(2 * BLOCK, half_rows, heads * width * (2 * rows + 8 * half_rows + 2 * sum(a.shape[2] for a in far_operands))),
        )(meta, used, q_t, acc1, st1, *far_operands)

        received_even = jnp.concatenate(
            [
                lax.ppermute(project_half(att_even, out_weight, 1 - hidx, part=p, parts=2), "head", swap)
                for p in range(2)
            ],
            axis=1,
        )
        own_even = project_half(att_even, out_weight, hidx)
        parts = [
            (own.astype(jnp.float32) + got.astype(jnp.float32)).astype(jnp.bfloat16)
            for own, got in ((own_even, received_even), (own_odd, received_odd))
        ]
    even, odd = (p.reshape(per_dev // 2, BLOCK, -1) for p in parts)
    return jnp.stack([even, odd], axis=1).reshape(rows, -1)


def solution(mesh):
    placed = (
        P("ctx", "head", None),
        P("ctx", "head", None),
        P("ctx", "head", None),
        P(),
        P("head", None),
    )
    return jax.shard_map(
        per_device, mesh=mesh, in_specs=placed, out_specs=P("ctx", "head"), check_vma=False
    )
```

```python
import functools
import math

import jax
import jax.numpy as jnp
from jax import lax
from jax.experimental import pallas as pl
from jax.experimental.pallas import tpu as pltpu
from jax.sharding import PartitionSpec as P

BLOCK = 64
WINDOW = 512
NOFF = 5
HEADS_PER_STEP = 4


def from_behind(value, axis, steps):
    count = lax.axis_size(axis)
    initial, last = (max(0, -steps), min(count, count - steps))
    return lax.ppermute(value, axis, [(source, source + steps) for source in range(initial, last)])


def block_scores(q, keys, scale):
    return lax.dot_general(
        q, keys, (((1,), (1,)), ((), ())), preferred_element_type=jnp.float32
    ) * scale


def merge(pieces, m_old, l_old, acc_old):
    top = m_old
    for s, _ in pieces:
        row_max = s.max(axis=1, keepdims=True)
        top = row_max if top is None else jnp.maximum(top, row_max)
    total = None
    summed = None
    for s, v in pieces:
        p = jnp.exp(s - top)
        part_total = p.sum(axis=1, keepdims=True)
        part = jnp.dot(p.astype(jnp.bfloat16), v, preferred_element_type=jnp.float32)
        total = part_total if total is None else total + part_total
        summed = part if summed is None else summed + part
    if m_old is not None:
        alpha = jnp.exp(m_old - top)
        total = total + l_old * alpha
        summed = summed + acc_old * alpha
    return top, total, summed


def pack_stats(m, l, width):
    lane = lax.broadcasted_iota(jnp.int32, (m.shape[0], width), 1)
    return jnp.where(lane == 0, m, jnp.where(lane == 1, l, 0.0))


TILE = 256


class HeadView:
    def __init__(self, ref, head, width=None):
        self.ref, self.head, self.width = ref, head, width

    def _index(self, idx):
        if idx is Ellipsis:
            idx = (slice(None), slice(None))
        if self.width is None:
            return (self.head,) + tuple(idx)
        return (idx[0], pl.ds(self.head * self.width, self.width))

    @property
    def dtype(self):
        return self.ref.dtype

    def __getitem__(self, idx):
        return self.ref[self._index(idx)]

    def __setitem__(self, idx, value):
        self.ref[self._index(idx)] = value


def per_head(body, n_prefetch, n_head_major, n_rows_out, width, heads_per_step):
    def kernel(*refs):
        pre = refs[:n_prefetch]
        rest = refs[n_prefetch:]
        n_major = len(rest) - n_rows_out
        for hh in range(heads_per_step):
            views = [HeadView(r, hh) for r in rest[:n_major]]
            outs = [HeadView(r, hh, width) for r in rest[n_major:]]
            body(*pre, *views, *outs)

    return kernel


def own_kernel(per_dev, width, scale, q_ref, k_ref, v_ref, acc_ref, st_ref):
    neg = jnp.float32(-jnp.inf)
    rows = per_dev * BLOCK
    for lo in range(0, rows, TILE):
        q = q_ref[lo:lo + TILE, :]
        n_own = lo + TILE
        s_o = block_scores(q, k_ref[:n_own, :], scale)
        r_ids = lax.broadcasted_iota(jnp.int32, (TILE, n_own), 0)
        c_ids = lax.broadcasted_iota(jnp.int32, (TILE, n_own), 1)
        s_o = jnp.where(c_ids <= r_ids + lo, s_o, neg)
        m, l, acc = merge([(s_o, v_ref[:n_own, :])], None, None, None)
        acc_ref[lo:lo + TILE, :] = acc
        st_ref[lo:lo + TILE, :] = pack_stats(m, l, width)


def column_map(n_cols, values):
    seg = lax.broadcasted_iota(jnp.int32, (1, n_cols), 1) // BLOCK
    out = jnp.zeros((1, n_cols), jnp.int32)
    for j, value in enumerate(values):
        out = jnp.where(seg == j, value, out)
    return out


def prev_kernel(per_dev, width, scale, meta_ref, used_ref, q_ref, kp_ref, vp_ref, acc_ref, st_ref,
                acc_out, st_out, odd_ref):
    prev_ok = meta_ref[0] > 0
    neg = jnp.float32(-jnp.inf)
    rows = per_dev * BLOCK
    per_tile = TILE // BLOCK
    for lo in range(0, rows, TILE):
        q = q_ref[lo:lo + TILE, :]
        n_prev = rows - lo
        s_p = block_scores(q, kp_ref[lo:, :], scale)
        r_ids = lax.broadcasted_iota(jnp.int32, (TILE, n_prev), 0)
        c_ids = lax.broadcasted_iota(jnp.int32, (TILE, n_prev), 1)
        s_p = jnp.where((c_ids > r_ids) & prev_ok, s_p, neg)
        blocks = range(lo // BLOCK, lo // BLOCK + per_tile)
        starts = [pl.multiple_of(meta_ref[1 + i] * BLOCK, BLOCK) for i in blocks]
        k0 = jnp.concatenate([kp_ref[pl.ds(st, BLOCK), :] for st in starts], axis=0)
        v0 = jnp.concatenate([vp_ref[pl.ds(st, BLOCK), :] for st in starts], axis=0)
        s_f = block_scores(q, k0, scale)
        flags = column_map(TILE, [used_ref[i * NOFF] for i in blocks])
        r_blk = lax.broadcasted_iota(jnp.int32, (TILE, TILE), 0) // BLOCK
        c_blk = lax.broadcasted_iota(jnp.int32, (TILE, TILE), 1) // BLOCK
        s_f = jnp.where((r_blk == c_blk) & (flags > 0), s_f, neg)
        st = st_ref[lo:lo + TILE, :]
        m, l, acc = merge(
            [(s_p, vp_ref[lo:, :]), (s_f, v0)], st[:, 0:1], st[:, 1:2], acc_ref[lo:lo + TILE, :]
        )
        for b, i in enumerate(blocks):
            sl = slice(b * BLOCK, (b + 1) * BLOCK)
            half = (i // 2) * BLOCK
            if i % 2:
                odd_ref[half:half + BLOCK, :] = (acc[sl] / l[sl]).astype(odd_ref.dtype)
            else:
                acc_out[half:half + BLOCK, :] = acc[sl]
                st_out[half:half + BLOCK, :] = pack_stats(m[sl], l[sl], width)


def far_kernel(levels, per_dev, width, scale, meta_ref, used_ref, q_ref, acc_ref, st_ref, *rest):
    far_refs = rest[:-1]
    even_ref = rest[-1]
    neg = jnp.float32(-jnp.inf)
    n_even = per_dev // 2
    q = jnp.concatenate([q_ref[2 * e * BLOCK:(2 * e + 1) * BLOCK, :] for e in range(n_even)], axis=0)
    keys, vals, targets, flags = [], [], [], []
    pos = 0
    for level in levels:
        offset = 2**level
        n_src = 2 if level == 1 else 1
        refs = far_refs[pos:pos + 2 * n_src]
        pos += 2 * n_src
        k_lvl = refs[0][...]
        v_lvl = refs[1][...]
        if n_src == 2:
            odd = meta_ref[1 + per_dev] > 0
            k_lvl = jnp.where(odd, refs[2][...], k_lvl)
            v_lvl = jnp.where(odd, refs[3][...], v_lvl)
        keys.append(k_lvl)
        vals.append(v_lvl)
        for k in range(k_lvl.shape[0] // BLOCK):
            qblock = k * offset
            targets.append(qblock // 2)
            flags.append(used_ref[qblock * NOFF + level])
    k_far = jnp.concatenate(keys, axis=0)
    v_far = jnp.concatenate(vals, axis=0)
    n_keys = k_far.shape[0]
    s_f = block_scores(q, k_far, scale)
    col_target = column_map(n_keys, targets)
    col_flag = column_map(n_keys, flags)
    r_blk = lax.broadcasted_iota(jnp.int32, (n_even * BLOCK, n_keys), 0) // BLOCK
    s_f = jnp.where((r_blk == col_target) & (col_flag > 0), s_f, neg)
    st = st_ref[...]
    m, l, acc = merge([(s_f, v_far)], st[:, 0:1], st[:, 1:2], acc_ref[...])
    even_ref[...] = (acc / l).astype(even_ref.dtype)


def matmul_kernel(sel_ref, a_ref, w_ref, o_ref):
    o_ref[...] = jnp.dot(a_ref[...], w_ref[...], preferred_element_type=jnp.float32).astype(
        o_ref.dtype
    )


def project_half(attended, weight, half, tn=512, part=0, parts=1):
    rows, depth = attended.shape
    cw = weight.shape[1] // 2
    total_steps = cw // tn
    steps = total_steps // parts
    first = part * steps
    cw = steps * tn
    return pl.pallas_call(
        matmul_kernel,
        out_shape=jax.ShapeDtypeStruct((rows, cw), jnp.bfloat16),
        grid_spec=pltpu.PrefetchScalarGridSpec(
            num_scalar_prefetch=1,
            grid=(steps,),
            in_specs=[
                pl.BlockSpec((rows, depth), lambda j, sel: (0, 0)),
                pl.BlockSpec((depth, tn), lambda j, sel: (0, sel[0] * total_steps + first + j)),
            ],
            out_specs=pl.BlockSpec((rows, tn), lambda j, sel: (0, j)),
        ),
        compiler_params=pltpu.CompilerParams(dimension_semantics=("arbitrary",)),
        cost_estimate=pl.CostEstimate(
            flops=2 * rows * depth * cw,
            transcendentals=0,
            bytes_accessed=2 * (rows * depth + depth * cw + rows * cw),
        ),
    )(jnp.reshape(half, (1,)).astype(jnp.int32), attended, weight)


def pick_blocks(kv, local):
    return jnp.concatenate(
        [lax.dynamic_slice_in_dim(kv, local[b] * BLOCK, BLOCK, axis=2) for b in range(local.shape[0])],
        axis=2,
    )


def per_device(queries, keys, values, far_blocks, out_weight):
    rows, heads, width = queries.shape
    per_dev = rows // BLOCK
    device = lax.axis_index("ctx")
    cycle_size = lax.axis_size("ctx")
    scale = 1.0 / math.sqrt(width)
    q_t = jnp.transpose(queries, (1, 0, 2))
    kv_t = jnp.stack([jnp.transpose(keys, (1, 0, 2)), jnp.transpose(values, (1, 0, 2))])
    prev_kv = from_behind(kv_t, "ctx", 1)
    levels = []
    sends = []
    for level in range(1, NOFF):
        offset = 2**level
        if offset >= cycle_size:
            continue
        target = lax.dynamic_slice_in_dim(far_blocks, (device + offset) * per_dev, per_dev, 0)[
            ::offset, level
        ]
        local = jnp.clip(target - device * per_dev, 0, per_dev - 1)
        if level == 1:
            pairs = [(s, s + 2) for s in range(0, cycle_size - 2, 2)]
            nxt = lax.dynamic_slice_in_dim(far_blocks, (device + 1) * per_dev, per_dev, 0)[::2, 1]
            fwd_local = jnp.clip(nxt - (device - 1) * per_dev, 0, per_dev - 1)
        else:
            pairs = [(s, s + offset) for s in range(0, cycle_size - offset)]
        sends.append((pick_blocks(kv_t, local), pairs))
        levels.append(level)
    q_t, kv_t, *operands = lax.optimization_barrier((q_t, kv_t, *[op for op, _ in sends]))
    far_arrays = []
    for (_, pairs), op, level in zip(sends, operands, levels):
        if level == 1:
            far_arrays.append((op, pairs))
        else:
            far_arrays.append((lax.ppermute(op, "ctx", pairs),))

    own = lax.dynamic_slice_in_dim(far_blocks, device * per_dev, per_dev, 0)
    query_index = device * per_dev + jnp.arange(per_dev, dtype=jnp.int32)
    used = (own <= (query_index - WINDOW // BLOCK - 1)[:, None]).astype(jnp.int32).reshape(-1)
    pick = jnp.clip(own[:, 0] - (device - 1) * per_dev, 0, per_dev - 1)
    meta = jnp.concatenate(
        [(device > 0).astype(jnp.int32)[None], pick.astype(jnp.int32), (device % 2)[None]]
    )

    hb = math.gcd(heads, HEADS_PER_STEP)
    row_spec = lambda n: pl.BlockSpec((hb, n, width), lambda h, *_: (h, 0, 0))
    out_spec = lambda n: pl.BlockSpec((n, hb * width), lambda h, *_: (0, h))
    k_spec = lambda n: pl.BlockSpec((None, hb, n, width), lambda h, *_: (0, h, 0, 0))
    v_spec = lambda n: pl.BlockSpec((None, hb, n, width), lambda h, *_: (1, h, 0, 0))
    half_rows = rows // 2
    f32 = jnp.float32
    params = pltpu.CompilerParams(dimension_semantics=("arbitrary",))
    state = lambda n: jax.ShapeDtypeStruct((heads, n, width), f32)

    def cost(keys_per_row, n_rows, extra_bytes):
        return pl.CostEstimate(
            flops=4 * n_rows * heads * width * keys_per_row,
            transcendentals=n_rows * heads * keys_per_row,
            bytes_accessed=extra_bytes,
        )

    acc0, st0 = pl.pallas_call(
        per_head(functools.partial(own_kernel, per_dev, width, scale), 0, 5, 0, width, hb),
        out_shape=(state(rows), state(rows)),
        grid=(heads // hb,),
        in_specs=[row_spec(rows), k_spec(rows), v_spec(rows)],
        out_specs=(row_spec(rows), row_spec(rows)),
        compiler_params=params,
        cost_estimate=cost(WINDOW // 2, rows, 2 * heads * rows * width * (3 * 2 + 2 * 4)),
    )(q_t, kv_t, kv_t)

    if levels and levels[0] == 1:
        direct_op, direct_pairs = far_arrays[0]
        prev_kv, acc0, st0, direct_op = lax.optimization_barrier((prev_kv, acc0, st0, direct_op))
        direct = lax.ppermute(direct_op, "ctx", direct_pairs)
        forwarded = lax.ppermute(
            pick_blocks(prev_kv, fwd_local), "ctx",
            [(s, s + 1) for s in range(0, cycle_size - 1, 2)],
        )
        far_arrays[0] = (direct, forwarded)
    else:
        prev_kv, acc0, st0 = lax.optimization_barrier((prev_kv, acc0, st0))
    far_specs, far_operands = [], []
    for group in far_arrays:
        for a in group:
            far_specs += [k_spec(a.shape[2]), v_spec(a.shape[2])]
            far_operands += [a, a]
    acc1, st1, att_odd = pl.pallas_call(
        per_head(functools.partial(prev_kernel, per_dev, width, scale), 2, 7, 1, width, hb),
        out_shape=(
            state(half_rows),
            state(half_rows),
            jax.ShapeDtypeStruct((half_rows, heads * width), queries.dtype),
        ),
        grid_spec=pltpu.PrefetchScalarGridSpec(
            num_scalar_prefetch=2,
            grid=(heads // hb,),
            in_specs=[row_spec(rows), k_spec(rows), v_spec(rows), row_spec(rows), row_spec(rows)],
            out_specs=(row_spec(half_rows), row_spec(half_rows), out_spec(half_rows)),
        ),
        compiler_params=params,
        cost_estimate=cost(WINDOW // 2 + BLOCK, rows, heads * rows * width * (3 * 2 + 2 * 4 + 8)),
    )(meta, used, q_t, prev_kv, prev_kv, acc0, st0)

    n_head = lax.axis_size("head")
    if n_head != 2:
        att_even = pl.pallas_call(
            per_head(functools.partial(far_kernel, levels, per_dev, width, scale), 2, 0, 1, width, hb),
            out_shape=jax.ShapeDtypeStruct((half_rows, heads * width), queries.dtype),
            grid_spec=pltpu.PrefetchScalarGridSpec(
                num_scalar_prefetch=2,
                grid=(heads // hb,),
                in_specs=[row_spec(rows), row_spec(half_rows), row_spec(half_rows)] + far_specs,
                out_specs=out_spec(half_rows),
            ),
            compiler_params=params,
            cost_estimate=cost(2 * BLOCK, half_rows, heads * width * (2 * rows + 8 * half_rows + 2 * sum(a.shape[2] for a in far_operands))),
        )(meta, used, q_t, acc1, st1, *far_operands)

        parts = []
        for att in (att_even, att_odd):
            partial_value = jnp.dot(att, out_weight, preferred_element_type=jnp.float32)
            parts.append(lax.psum_scatter(
                partial_value.astype(jnp.bfloat16), "head", scatter_dimension=1, tiled=True
            ))
    else:
        hidx = lax.axis_index("head")
        swap = [(0, 1), (1, 0)]
        received_odd = lax.ppermute(project_half(att_odd, out_weight, 1 - hidx), "head", swap)
        own_odd = project_half(att_odd, out_weight, hidx)
        acc1, st1, own_odd = lax.optimization_barrier((acc1, st1, own_odd))
        att_even = pl.pallas_call(
            per_head(functools.partial(far_kernel, levels, per_dev, width, scale), 2, 0, 1, width, hb),
            out_shape=jax.ShapeDtypeStruct((half_rows, heads * width), queries.dtype),
            grid_spec=pltpu.PrefetchScalarGridSpec(
                num_scalar_prefetch=2,
                grid=(heads // hb,),
                in_specs=[row_spec(rows), row_spec(half_rows), row_spec(half_rows)] + far_specs,
                out_specs=out_spec(half_rows),
            ),
            compiler_params=params,
            cost_estimate=cost(2 * BLOCK, half_rows, heads * width * (2 * rows + 8 * half_rows + 2 * sum(a.shape[2] for a in far_operands))),
        )(meta, used, q_t, acc1, st1, *far_operands)

        received_even = jnp.concatenate(
            [
                lax.ppermute(
                    project_half(att_even, out_weight, 1 - hidx, tn=256, part=p, parts=4), "head", swap
                )
                for p in range(4)
            ],
            axis=1,
        )
        own_even = project_half(att_even, out_weight, hidx)
        parts = [
            (own.astype(jnp.float32) + got.astype(jnp.float32)).astype(jnp.bfloat16)
            for own, got in ((own_even, received_even), (own_odd, received_odd))
        ]
    even, odd = (p.reshape(per_dev // 2, BLOCK, -1) for p in parts)
    return jnp.stack([even, odd], axis=1).reshape(rows, -1)


def solution(mesh):
    placed = (
        P("ctx", "head", None),
        P("ctx", "head", None),
        P("ctx", "head", None),
        P(),
        P("head", None),
    )
    return jax.shard_map(
        per_device, mesh=mesh, in_specs=placed, out_specs=P("ctx", "head"), check_vma=False
    )
```

```python
import functools
import math

import jax
import jax.numpy as jnp
from jax import lax
from jax.experimental import pallas as pl
from jax.experimental.pallas import tpu as pltpu
from jax.sharding import PartitionSpec as P

BLOCK = 64
WINDOW = 512
NOFF = 5
HEADS_PER_STEP = 4


def from_behind(value, axis, steps):
    count = lax.axis_size(axis)
    initial, last = (max(0, -steps), min(count, count - steps))
    return lax.ppermute(value, axis, [(source, source + steps) for source in range(initial, last)])


def block_scores(q, keys, scale):
    return lax.dot_general(
        q, keys, (((1,), (1,)), ((), ())), preferred_element_type=jnp.float32
    ) * scale


def merge(pieces, m_old, l_old, acc_old):
    top = m_old
    for s, _ in pieces:
        row_max = s.max(axis=1, keepdims=True)
        top = row_max if top is None else jnp.maximum(top, row_max)
    total = None
    summed = None
    for s, v in pieces:
        p = jnp.exp(s - top)
        part_total = p.sum(axis=1, keepdims=True)
        part = jnp.dot(p.astype(jnp.bfloat16), v, preferred_element_type=jnp.float32)
        total = part_total if total is None else total + part_total
        summed = part if summed is None else summed + part
    if m_old is not None:
        alpha = jnp.exp(m_old - top)
        total = total + l_old * alpha
        summed = summed + acc_old * alpha
    return top, total, summed


def pack_stats(m, l, width):
    lane = lax.broadcasted_iota(jnp.int32, (m.shape[0], width), 1)
    return jnp.where(lane == 0, m, jnp.where(lane == 1, l, 0.0))


TILE = 256


class HeadView:
    def __init__(self, ref, head, width=None):
        self.ref, self.head, self.width = ref, head, width

    def _index(self, idx):
        if idx is Ellipsis:
            idx = (slice(None), slice(None))
        if self.width is None:
            return (self.head,) + tuple(idx)
        return (idx[0], pl.ds(self.head * self.width, self.width))

    @property
    def dtype(self):
        return self.ref.dtype

    def __getitem__(self, idx):
        return self.ref[self._index(idx)]

    def __setitem__(self, idx, value):
        self.ref[self._index(idx)] = value


def per_head(body, n_prefetch, n_head_major, n_rows_out, width, heads_per_step):
    def kernel(*refs):
        pre = refs[:n_prefetch]
        rest = refs[n_prefetch:]
        n_major = len(rest) - n_rows_out
        for hh in range(heads_per_step):
            views = [HeadView(r, hh) for r in rest[:n_major]]
            outs = [HeadView(r, hh, width) for r in rest[n_major:]]
            body(*pre, *views, *outs)

    return kernel


def own_kernel(per_dev, width, scale, q_ref, k_ref, v_ref, acc_ref, st_ref):
    neg = jnp.float32(-jnp.inf)
    rows = per_dev * BLOCK
    for lo in range(0, rows, TILE):
        q = q_ref[lo:lo + TILE, :]
        n_own = lo + TILE
        s_o = block_scores(q, k_ref[:n_own, :], scale)
        r_ids = lax.broadcasted_iota(jnp.int32, (TILE, n_own), 0)
        c_ids = lax.broadcasted_iota(jnp.int32, (TILE, n_own), 1)
        s_o = jnp.where(c_ids <= r_ids + lo, s_o, neg)
        m, l, acc = merge([(s_o, v_ref[:n_own, :])], None, None, None)
        acc_ref[lo:lo + TILE, :] = acc
        st_ref[lo:lo + TILE, :] = pack_stats(m, l, width)


def column_map(n_cols, values):
    seg = lax.broadcasted_iota(jnp.int32, (1, n_cols), 1) // BLOCK
    out = jnp.zeros((1, n_cols), jnp.int32)
    for j, value in enumerate(values):
        out = jnp.where(seg == j, value, out)
    return out


def prev_kernel(per_dev, width, scale, meta_ref, used_ref, q_ref, kp_ref, vp_ref, acc_ref, st_ref,
                acc_out, st_out, odd_ref):
    prev_ok = meta_ref[0] > 0
    neg = jnp.float32(-jnp.inf)
    rows = per_dev * BLOCK
    per_tile = TILE // BLOCK
    for lo in range(0, rows, TILE):
        q = q_ref[lo:lo + TILE, :]
        n_prev = rows - lo
        s_p = block_scores(q, kp_ref[lo:, :], scale)
        r_ids = lax.broadcasted_iota(jnp.int32, (TILE, n_prev), 0)
        c_ids = lax.broadcasted_iota(jnp.int32, (TILE, n_prev), 1)
        s_p = jnp.where((c_ids > r_ids) & prev_ok, s_p, neg)
        blocks = range(lo // BLOCK, lo // BLOCK + per_tile)
        starts = [pl.multiple_of(meta_ref[1 + i] * BLOCK, BLOCK) for i in blocks]
        k0 = jnp.concatenate([kp_ref[pl.ds(st, BLOCK), :] for st in starts], axis=0)
        v0 = jnp.concatenate([vp_ref[pl.ds(st, BLOCK), :] for st in starts], axis=0)
        s_f = block_scores(q, k0, scale)
        flags = column_map(TILE, [used_ref[i * NOFF] for i in blocks])
        r_blk = lax.broadcasted_iota(jnp.int32, (TILE, TILE), 0) // BLOCK
        c_blk = lax.broadcasted_iota(jnp.int32, (TILE, TILE), 1) // BLOCK
        s_f = jnp.where((r_blk == c_blk) & (flags > 0), s_f, neg)
        st = st_ref[lo:lo + TILE, :]
        m, l, acc = merge(
            [(s_p, vp_ref[lo:, :]), (s_f, v0)], st[:, 0:1], st[:, 1:2], acc_ref[lo:lo + TILE, :]
        )
        for b, i in enumerate(blocks):
            sl = slice(b * BLOCK, (b + 1) * BLOCK)
            half = (i // 2) * BLOCK
            if i % 2:
                odd_ref[half:half + BLOCK, :] = (acc[sl] / l[sl]).astype(odd_ref.dtype)
            else:
                acc_out[half:half + BLOCK, :] = acc[sl]
                st_out[half:half + BLOCK, :] = pack_stats(m[sl], l[sl], width)


def far_kernel(levels, per_dev, width, scale, meta_ref, used_ref, q_ref, acc_ref, st_ref, *rest):
    far_refs = rest[:-1]
    even_ref = rest[-1]
    neg = jnp.float32(-jnp.inf)
    n_even = per_dev // 2
    q = jnp.concatenate([q_ref[2 * e * BLOCK:(2 * e + 1) * BLOCK, :] for e in range(n_even)], axis=0)
    keys, vals, targets, flags = [], [], [], []
    pos = 0
    for level in levels:
        offset = 2**level
        n_src = 2 if level == 1 else 1
        refs = far_refs[pos:pos + 2 * n_src]
        pos += 2 * n_src
        k_lvl = refs[0][...]
        v_lvl = refs[1][...]
        if n_src == 2:
            odd = meta_ref[1 + per_dev] > 0
            k_lvl = jnp.where(odd, refs[2][...], k_lvl)
            v_lvl = jnp.where(odd, refs[3][...], v_lvl)
        keys.append(k_lvl)
        vals.append(v_lvl)
        for k in range(k_lvl.shape[0] // BLOCK):
            qblock = k * offset
            targets.append(qblock // 2)
            flags.append(used_ref[qblock * NOFF + level])
    k_far = jnp.concatenate(keys, axis=0)
    v_far = jnp.concatenate(vals, axis=0)
    n_keys = k_far.shape[0]
    s_f = block_scores(q, k_far, scale)
    col_target = column_map(n_keys, targets)
    col_flag = column_map(n_keys, flags)
    r_blk = lax.broadcasted_iota(jnp.int32, (n_even * BLOCK, n_keys), 0) // BLOCK
    s_f = jnp.where((r_blk == col_target) & (col_flag > 0), s_f, neg)
    st = st_ref[...]
    m, l, acc = merge([(s_f, v_far)], st[:, 0:1], st[:, 1:2], acc_ref[...])
    even_ref[...] = (acc / l).astype(even_ref.dtype)


def matmul_kernel(sel_ref, a_ref, w_ref, o_ref):
    o_ref[...] = jnp.dot(a_ref[...], w_ref[...], preferred_element_type=jnp.float32).astype(
        o_ref.dtype
    )


def project_half(attended, weight, half, tn=512, part=0, parts=1):
    rows, depth = attended.shape
    cw = weight.shape[1] // 2
    total_steps = cw // tn
    steps = total_steps // parts
    first = part * steps
    cw = steps * tn
    return pl.pallas_call(
        matmul_kernel,
        out_shape=jax.ShapeDtypeStruct((rows, cw), jnp.bfloat16),
        grid_spec=pltpu.PrefetchScalarGridSpec(
            num_scalar_prefetch=1,
            grid=(steps,),
            in_specs=[
                pl.BlockSpec((rows, depth), lambda j, sel: (0, 0)),
                pl.BlockSpec((depth, tn), lambda j, sel: (0, sel[0] * total_steps + first + j)),
            ],
            out_specs=pl.BlockSpec((rows, tn), lambda j, sel: (0, j)),
        ),
        compiler_params=pltpu.CompilerParams(dimension_semantics=("arbitrary",)),
        cost_estimate=pl.CostEstimate(
            flops=2 * rows * depth * cw,
            transcendentals=0,
            bytes_accessed=2 * (rows * depth + depth * cw + rows * cw),
        ),
    )(jnp.reshape(half, (1,)).astype(jnp.int32), attended, weight)


def pick_blocks(kv, local):
    return jnp.concatenate(
        [lax.dynamic_slice_in_dim(kv, local[b] * BLOCK, BLOCK, axis=2) for b in range(local.shape[0])],
        axis=2,
    )


def per_device(queries, keys, values, far_blocks, out_weight):
    rows, heads, width = queries.shape
    per_dev = rows // BLOCK
    device = lax.axis_index("ctx")
    cycle_size = lax.axis_size("ctx")
    scale = 1.0 / math.sqrt(width)
    q_t = jnp.transpose(queries, (1, 0, 2))
    kv_t = jnp.stack([jnp.transpose(keys, (1, 0, 2)), jnp.transpose(values, (1, 0, 2))])
    prev_kv = from_behind(kv_t, "ctx", 1)
    levels = []
    sends = []
    for level in range(1, NOFF):
        offset = 2**level
        if offset >= cycle_size:
            continue
        target = lax.dynamic_slice_in_dim(far_blocks, (device + offset) * per_dev, per_dev, 0)[
            ::offset, level
        ]
        local = jnp.clip(target - device * per_dev, 0, per_dev - 1)
        if level == 1:
            pairs = [(s, s + 2) for s in range(0, cycle_size - 2, 2)]
            nxt = lax.dynamic_slice_in_dim(far_blocks, (device + 1) * per_dev, per_dev, 0)[::2, 1]
            fwd_local = jnp.clip(nxt - (device - 1) * per_dev, 0, per_dev - 1)
        else:
            pairs = [(s, s + offset) for s in range(0, cycle_size - offset)]
        sends.append((pick_blocks(kv_t, local), pairs))
        levels.append(level)
    q_t, kv_t, *operands = lax.optimization_barrier((q_t, kv_t, *[op for op, _ in sends]))
    far_arrays = []
    for (_, pairs), op, level in zip(sends, operands, levels):
        if level == 1:
            far_arrays.append((op, pairs))
        else:
            far_arrays.append((lax.ppermute(op, "ctx", pairs),))

    own = lax.dynamic_slice_in_dim(far_blocks, device * per_dev, per_dev, 0)
    query_index = device * per_dev + jnp.arange(per_dev, dtype=jnp.int32)
    used = (own <= (query_index - WINDOW // BLOCK - 1)[:, None]).astype(jnp.int32).reshape(-1)
    pick = jnp.clip(own[:, 0] - (device - 1) * per_dev, 0, per_dev - 1)
    meta = jnp.concatenate(
        [(device > 0).astype(jnp.int32)[None], pick.astype(jnp.int32), (device % 2)[None]]
    )

    hb = math.gcd(heads, HEADS_PER_STEP)
    row_spec = lambda n: pl.BlockSpec((hb, n, width), lambda h, *_: (h, 0, 0))
    out_spec = lambda n: pl.BlockSpec((n, hb * width), lambda h, *_: (0, h))
    k_spec = lambda n: pl.BlockSpec((None, hb, n, width), lambda h, *_: (0, h, 0, 0))
    v_spec = lambda n: pl.BlockSpec((None, hb, n, width), lambda h, *_: (1, h, 0, 0))
    half_rows = rows // 2
    f32 = jnp.float32
    params = pltpu.CompilerParams(dimension_semantics=("arbitrary",))
    state = lambda n: jax.ShapeDtypeStruct((heads, n, width), f32)

    def cost(keys_per_row, n_rows, extra_bytes):
        return pl.CostEstimate(
            flops=4 * n_rows * heads * width * keys_per_row,
            transcendentals=n_rows * heads * keys_per_row,
            bytes_accessed=extra_bytes,
        )

    acc0, st0 = pl.pallas_call(
        per_head(functools.partial(own_kernel, per_dev, width, scale), 0, 5, 0, width, hb),
        out_shape=(state(rows), state(rows)),
        grid=(heads // hb,),
        in_specs=[row_spec(rows), k_spec(rows), v_spec(rows)],
        out_specs=(row_spec(rows), row_spec(rows)),
        compiler_params=params,
        cost_estimate=cost(WINDOW // 2, rows, 2 * heads * rows * width * (3 * 2 + 2 * 4)),
    )(q_t, kv_t, kv_t)

    if levels and levels[0] == 1:
        direct_op, direct_pairs = far_arrays[0]
        prev_kv, acc0, st0, direct_op = lax.optimization_barrier((prev_kv, acc0, st0, direct_op))
        direct = lax.ppermute(direct_op, "ctx", direct_pairs)
        forwarded = lax.ppermute(
            pick_blocks(prev_kv, fwd_local), "ctx",
            [(s, s + 1) for s in range(0, cycle_size - 1, 2)],
        )
        far_arrays[0] = (direct, forwarded)
    else:
        prev_kv, acc0, st0 = lax.optimization_barrier((prev_kv, acc0, st0))
    far_specs, far_operands = [], []
    for group in far_arrays:
        for a in group:
            far_specs += [k_spec(a.shape[2]), v_spec(a.shape[2])]
            far_operands += [a, a]
    acc1, st1, att_odd = pl.pallas_call(
        per_head(functools.partial(prev_kernel, per_dev, width, scale), 2, 7, 1, width, hb),
        out_shape=(
            state(half_rows),
            state(half_rows),
            jax.ShapeDtypeStruct((half_rows, heads * width), queries.dtype),
        ),
        grid_spec=pltpu.PrefetchScalarGridSpec(
            num_scalar_prefetch=2,
            grid=(heads // hb,),
            in_specs=[row_spec(rows), k_spec(rows), v_spec(rows), row_spec(rows), row_spec(rows)],
            out_specs=(row_spec(half_rows), row_spec(half_rows), out_spec(half_rows)),
        ),
        compiler_params=params,
        cost_estimate=cost(WINDOW // 2 + BLOCK, rows, heads * rows * width * (3 * 2 + 2 * 4 + 8)),
    )(meta, used, q_t, prev_kv, prev_kv, acc0, st0)

    n_head = lax.axis_size("head")
    if n_head != 2:
        att_even = pl.pallas_call(
            per_head(functools.partial(far_kernel, levels, per_dev, width, scale), 2, 0, 1, width, hb),
            out_shape=jax.ShapeDtypeStruct((half_rows, heads * width), queries.dtype),
            grid_spec=pltpu.PrefetchScalarGridSpec(
                num_scalar_prefetch=2,
                grid=(heads // hb,),
                in_specs=[row_spec(rows), row_spec(half_rows), row_spec(half_rows)] + far_specs,
                out_specs=out_spec(half_rows),
            ),
            compiler_params=params,
            cost_estimate=cost(2 * BLOCK, half_rows, heads * width * (2 * rows + 8 * half_rows + 2 * sum(a.shape[2] for a in far_operands))),
        )(meta, used, q_t, acc1, st1, *far_operands)

        parts = []
        for att in (att_even, att_odd):
            partial_value = jnp.dot(att, out_weight, preferred_element_type=jnp.float32)
            parts.append(lax.psum_scatter(
                partial_value.astype(jnp.bfloat16), "head", scatter_dimension=1, tiled=True
            ))
    else:
        hidx = lax.axis_index("head")
        swap = [(0, 1), (1, 0)]
        received_odd = lax.ppermute(project_half(att_odd, out_weight, 1 - hidx), "head", swap)
        own_odd = project_half(att_odd, out_weight, hidx)
        acc1, st1, own_odd = lax.optimization_barrier((acc1, st1, own_odd))
        att_even = pl.pallas_call(
            per_head(functools.partial(far_kernel, levels, per_dev, width, scale), 2, 0, 1, width, hb),
            out_shape=jax.ShapeDtypeStruct((half_rows, heads * width), queries.dtype),
            grid_spec=pltpu.PrefetchScalarGridSpec(
                num_scalar_prefetch=2,
                grid=(heads // hb,),
                in_specs=[row_spec(rows), row_spec(half_rows), row_spec(half_rows)] + far_specs,
                out_specs=out_spec(half_rows),
            ),
            compiler_params=params,
            cost_estimate=cost(2 * BLOCK, half_rows, heads * width * (2 * rows + 8 * half_rows + 2 * sum(a.shape[2] for a in far_operands))),
        )(meta, used, q_t, acc1, st1, *far_operands)

        received_even = jnp.concatenate(
            [
                lax.ppermute(project_half(att_even, out_weight, 1 - hidx, part=p, parts=2), "head", swap)
                for p in range(2)
            ],
            axis=1,
        )
        own_even = project_half(att_even, out_weight, hidx)
        out_blocks = []
        for e in range(per_dev // 2):
            for own, got in ((own_even, received_even), (own_odd, received_odd)):
                rows_e = slice(e * BLOCK, (e + 1) * BLOCK)
                out_blocks.append(
                    (own[rows_e].astype(jnp.float32) + got[rows_e].astype(jnp.float32)).astype(jnp.bfloat16)
                )
        return jnp.concatenate(out_blocks, axis=0)
    even, odd = (p.reshape(per_dev // 2, BLOCK, -1) for p in parts)
    return jnp.stack([even, odd], axis=1).reshape(rows, -1)


def solution(mesh):
    placed = (
        P("ctx", "head", None),
        P("ctx", "head", None),
        P("ctx", "head", None),
        P(),
        P("head", None),
    )
    return jax.shard_map(
        per_device, mesh=mesh, in_specs=placed, out_specs=P("ctx", "head"), check_vma=False
    )
```

```python
import functools
import math

import jax
import jax.numpy as jnp
from jax import lax
from jax.experimental import pallas as pl
from jax.experimental.pallas import tpu as pltpu
from jax.sharding import PartitionSpec as P

BLOCK = 64
WINDOW = 512
NOFF = 5
HEADS_PER_STEP = 4


def from_behind(value, axis, steps):
    count = lax.axis_size(axis)
    initial, last = (max(0, -steps), min(count, count - steps))
    return lax.ppermute(value, axis, [(source, source + steps) for source in range(initial, last)])


def block_scores(q, keys, scale):
    return lax.dot_general(
        q, keys, (((1,), (1,)), ((), ())), preferred_element_type=jnp.float32
    ) * scale


def merge(pieces, m_old, l_old, acc_old):
    top = m_old
    for s, _ in pieces:
        row_max = s.max(axis=1, keepdims=True)
        top = row_max if top is None else jnp.maximum(top, row_max)
    total = None
    summed = None
    for s, v in pieces:
        p = jnp.exp(s - top)
        part_total = p.sum(axis=1, keepdims=True)
        part = jnp.dot(p.astype(jnp.bfloat16), v, preferred_element_type=jnp.float32)
        total = part_total if total is None else total + part_total
        summed = part if summed is None else summed + part
    if m_old is not None:
        alpha = jnp.exp(m_old - top)
        total = total + l_old * alpha
        summed = summed + acc_old * alpha
    return top, total, summed


def pack_stats(m, l, width):
    lane = lax.broadcasted_iota(jnp.int32, (m.shape[0], width), 1)
    return jnp.where(lane == 0, m, jnp.where(lane == 1, l, 0.0))


TILE = 256


class HeadView:
    def __init__(self, ref, head, width=None):
        self.ref, self.head, self.width = ref, head, width

    def _index(self, idx):
        if idx is Ellipsis:
            idx = (slice(None), slice(None))
        if self.width is None:
            return (self.head,) + tuple(idx)
        return (idx[0], pl.ds(self.head * self.width, self.width))

    @property
    def dtype(self):
        return self.ref.dtype

    def __getitem__(self, idx):
        return self.ref[self._index(idx)]

    def __setitem__(self, idx, value):
        self.ref[self._index(idx)] = value


def per_head(body, n_prefetch, n_head_major, n_rows_out, width, heads_per_step):
    def kernel(*refs):
        pre = refs[:n_prefetch]
        rest = refs[n_prefetch:]
        n_major = len(rest) - n_rows_out
        for hh in range(heads_per_step):
            views = [HeadView(r, hh) for r in rest[:n_major]]
            outs = [HeadView(r, hh, width) for r in rest[n_major:]]
            body(*pre, *views, *outs)

    return kernel


def own_kernel(per_dev, width, scale, q_ref, k_ref, v_ref, acc_ref, st_ref):
    neg = jnp.float32(-jnp.inf)
    rows = per_dev * BLOCK
    for lo in range(0, rows, TILE):
        q = q_ref[lo:lo + TILE, :]
        n_own = lo + TILE
        s_o = block_scores(q, k_ref[:n_own, :], scale)
        r_ids = lax.broadcasted_iota(jnp.int32, (TILE, n_own), 0)
        c_ids = lax.broadcasted_iota(jnp.int32, (TILE, n_own), 1)
        s_o = jnp.where(c_ids <= r_ids + lo, s_o, neg)
        m, l, acc = merge([(s_o, v_ref[:n_own, :])], None, None, None)
        acc_ref[lo:lo + TILE, :] = acc
        st_ref[lo:lo + TILE, :] = pack_stats(m, l, width)


def column_map(n_cols, values):
    seg = lax.broadcasted_iota(jnp.int32, (1, n_cols), 1) // BLOCK
    out = jnp.zeros((1, n_cols), jnp.int32)
    for j, value in enumerate(values):
        out = jnp.where(seg == j, value, out)
    return out


def prev_kernel(per_dev, width, scale, meta_ref, used_ref, q_ref, kp_ref, vp_ref, acc_ref, st_ref,
                acc_out, st_out, odd_ref):
    prev_ok = meta_ref[0] > 0
    neg = jnp.float32(-jnp.inf)
    rows = per_dev * BLOCK
    per_tile = TILE // BLOCK
    for lo in range(0, rows, TILE):
        q = q_ref[lo:lo + TILE, :]
        n_prev = rows - lo
        s_p = block_scores(q, kp_ref[lo:, :], scale)
        r_ids = lax.broadcasted_iota(jnp.int32, (TILE, n_prev), 0)
        c_ids = lax.broadcasted_iota(jnp.int32, (TILE, n_prev), 1)
        s_p = jnp.where((c_ids > r_ids) & prev_ok, s_p, neg)
        blocks = range(lo // BLOCK, lo // BLOCK + per_tile)
        starts = [pl.multiple_of(meta_ref[1 + i] * BLOCK, BLOCK) for i in blocks]
        k0 = jnp.concatenate([kp_ref[pl.ds(st, BLOCK), :] for st in starts], axis=0)
        v0 = jnp.concatenate([vp_ref[pl.ds(st, BLOCK), :] for st in starts], axis=0)
        s_f = block_scores(q, k0, scale)
        flags = column_map(TILE, [used_ref[i * NOFF] for i in blocks])
        r_blk = lax.broadcasted_iota(jnp.int32, (TILE, TILE), 0) // BLOCK
        c_blk = lax.broadcasted_iota(jnp.int32, (TILE, TILE), 1) // BLOCK
        s_f = jnp.where((r_blk == c_blk) & (flags > 0), s_f, neg)
        st = st_ref[lo:lo + TILE, :]
        m, l, acc = merge(
            [(s_p, vp_ref[lo:, :]), (s_f, v0)], st[:, 0:1], st[:, 1:2], acc_ref[lo:lo + TILE, :]
        )
        for b, i in enumerate(blocks):
            sl = slice(b * BLOCK, (b + 1) * BLOCK)
            half = (i // 2) * BLOCK
            if i % 2:
                odd_ref[half:half + BLOCK, :] = (acc[sl] / l[sl]).astype(odd_ref.dtype)
            else:
                acc_out[half:half + BLOCK, :] = acc[sl]
                st_out[half:half + BLOCK, :] = pack_stats(m[sl], l[sl], width)


def far_kernel(levels, per_dev, width, scale, meta_ref, used_ref, q_ref, acc_ref, st_ref, *rest):
    far_refs = rest[:-1]
    even_ref = rest[-1]
    neg = jnp.float32(-jnp.inf)
    n_even = per_dev // 2
    q = q_ref[...].reshape(n_even * BLOCK, -1)
    keys, vals, targets, flags = [], [], [], []
    pos = 0
    for level in levels:
        offset = 2**level
        n_src = 2 if level == 1 else 1
        refs = far_refs[pos:pos + 2 * n_src]
        pos += 2 * n_src
        k_lvl = refs[0][...]
        v_lvl = refs[1][...]
        if n_src == 2:
            odd = meta_ref[1 + per_dev] > 0
            k_lvl = jnp.where(odd, refs[2][...], k_lvl)
            v_lvl = jnp.where(odd, refs[3][...], v_lvl)
        keys.append(k_lvl)
        vals.append(v_lvl)
        for k in range(k_lvl.shape[0] // BLOCK):
            qblock = k * offset
            targets.append(qblock // 2)
            flags.append(used_ref[qblock * NOFF + level])
    k_far = jnp.concatenate(keys, axis=0)
    v_far = jnp.concatenate(vals, axis=0)
    n_keys = k_far.shape[0]
    s_f = block_scores(q, k_far, scale)
    col_target = column_map(n_keys, targets)
    col_flag = column_map(n_keys, flags)
    r_blk = lax.broadcasted_iota(jnp.int32, (n_even * BLOCK, n_keys), 0) // BLOCK
    s_f = jnp.where((r_blk == col_target) & (col_flag > 0), s_f, neg)
    st = st_ref[...]
    m, l, acc = merge([(s_f, v_far)], st[:, 0:1], st[:, 1:2], acc_ref[...])
    even_ref[...] = (acc / l).astype(even_ref.dtype)


def matmul_kernel(sel_ref, a_ref, w_ref, o_ref):
    o_ref[...] = jnp.dot(a_ref[...], w_ref[...], preferred_element_type=jnp.float32).astype(
        o_ref.dtype
    )


def project_half(attended, weight, half, tn=512, part=0, parts=1):
    rows, depth = attended.shape
    cw = weight.shape[1] // 2
    total_steps = cw // tn
    steps = total_steps // parts
    first = part * steps
    cw = steps * tn
    return pl.pallas_call(
        matmul_kernel,
        out_shape=jax.ShapeDtypeStruct((rows, cw), jnp.bfloat16),
        grid_spec=pltpu.PrefetchScalarGridSpec(
            num_scalar_prefetch=1,
            grid=(steps,),
            in_specs=[
                pl.BlockSpec((rows, depth), lambda j, sel: (0, 0)),
                pl.BlockSpec((depth, tn), lambda j, sel: (0, sel[0] * total_steps + first + j)),
            ],
            out_specs=pl.BlockSpec((rows, tn), lambda j, sel: (0, j)),
        ),
        compiler_params=pltpu.CompilerParams(dimension_semantics=("arbitrary",)),
        cost_estimate=pl.CostEstimate(
            flops=2 * rows * depth * cw,
            transcendentals=0,
            bytes_accessed=2 * (rows * depth + depth * cw + rows * cw),
        ),
    )(jnp.reshape(half, (1,)).astype(jnp.int32), attended, weight)


def pick_blocks(kv, local):
    return jnp.concatenate(
        [lax.dynamic_slice_in_dim(kv, local[b] * BLOCK, BLOCK, axis=2) for b in range(local.shape[0])],
        axis=2,
    )


def per_device(queries, keys, values, far_blocks, out_weight):
    rows, heads, width = queries.shape
    per_dev = rows // BLOCK
    device = lax.axis_index("ctx")
    cycle_size = lax.axis_size("ctx")
    scale = 1.0 / math.sqrt(width)
    q_t = jnp.transpose(queries, (1, 0, 2))
    kv_t = jnp.stack([jnp.transpose(keys, (1, 0, 2)), jnp.transpose(values, (1, 0, 2))])
    prev_kv = from_behind(kv_t, "ctx", 1)
    levels = []
    sends = []
    for level in range(1, NOFF):
        offset = 2**level
        if offset >= cycle_size:
            continue
        target = lax.dynamic_slice_in_dim(far_blocks, (device + offset) * per_dev, per_dev, 0)[
            ::offset, level
        ]
        local = jnp.clip(target - device * per_dev, 0, per_dev - 1)
        if level == 1:
            pairs = [(s, s + 2) for s in range(0, cycle_size - 2, 2)]
            nxt = lax.dynamic_slice_in_dim(far_blocks, (device + 1) * per_dev, per_dev, 0)[::2, 1]
            fwd_local = jnp.clip(nxt - (device - 1) * per_dev, 0, per_dev - 1)
        else:
            pairs = [(s, s + offset) for s in range(0, cycle_size - offset)]
        sends.append((pick_blocks(kv_t, local), pairs))
        levels.append(level)
    q_t, kv_t, *operands = lax.optimization_barrier((q_t, kv_t, *[op for op, _ in sends]))
    far_arrays = []
    for (_, pairs), op, level in zip(sends, operands, levels):
        if level == 1:
            far_arrays.append((op, pairs))
        else:
            far_arrays.append((lax.ppermute(op, "ctx", pairs),))

    own = lax.dynamic_slice_in_dim(far_blocks, device * per_dev, per_dev, 0)
    query_index = device * per_dev + jnp.arange(per_dev, dtype=jnp.int32)
    used = (own <= (query_index - WINDOW // BLOCK - 1)[:, None]).astype(jnp.int32).reshape(-1)
    pick = jnp.clip(own[:, 0] - (device - 1) * per_dev, 0, per_dev - 1)
    meta = jnp.concatenate(
        [(device > 0).astype(jnp.int32)[None], pick.astype(jnp.int32), (device % 2)[None]]
    )

    hb = math.gcd(heads, HEADS_PER_STEP)
    row_spec = lambda n: pl.BlockSpec((hb, n, width), lambda h, *_: (h, 0, 0))
    out_spec = lambda n: pl.BlockSpec((n, hb * width), lambda h, *_: (0, h))
    k_spec = lambda n: pl.BlockSpec((None, hb, n, width), lambda h, *_: (0, h, 0, 0))
    v_spec = lambda n: pl.BlockSpec((None, hb, n, width), lambda h, *_: (1, h, 0, 0))
    half_rows = rows // 2
    q_pairs = q_t.reshape(heads, per_dev // 2, 2, BLOCK, width)
    even_q_spec = pl.BlockSpec((hb, per_dev // 2, None, BLOCK, width), lambda h, *_: (h, 0, 0, 0, 0))
    f32 = jnp.float32
    params = pltpu.CompilerParams(dimension_semantics=("arbitrary",))
    state = lambda n: jax.ShapeDtypeStruct((heads, n, width), f32)

    def cost(keys_per_row, n_rows, extra_bytes):
        return pl.CostEstimate(
            flops=4 * n_rows * heads * width * keys_per_row,
            transcendentals=n_rows * heads * keys_per_row,
            bytes_accessed=extra_bytes,
        )

    acc0, st0 = pl.pallas_call(
        per_head(functools.partial(own_kernel, per_dev, width, scale), 0, 5, 0, width, hb),
        out_shape=(state(rows), state(rows)),
        grid=(heads // hb,),
        in_specs=[row_spec(rows), k_spec(rows), v_spec(rows)],
        out_specs=(row_spec(rows), row_spec(rows)),
        compiler_params=params,
        cost_estimate=cost(WINDOW // 2, rows, 2 * heads * rows * width * (3 * 2 + 2 * 4)),
    )(q_t, kv_t, kv_t)

    if levels and levels[0] == 1:
        direct_op, direct_pairs = far_arrays[0]
        prev_kv, acc0, st0, direct_op = lax.optimization_barrier((prev_kv, acc0, st0, direct_op))
        direct = lax.ppermute(direct_op, "ctx", direct_pairs)
        forwarded = lax.ppermute(
            pick_blocks(prev_kv, fwd_local), "ctx",
            [(s, s + 1) for s in range(0, cycle_size - 1, 2)],
        )
        far_arrays[0] = (direct, forwarded)
    else:
        prev_kv, acc0, st0 = lax.optimization_barrier((prev_kv, acc0, st0))
    far_specs, far_operands = [], []
    for group in far_arrays:
        for a in group:
            far_specs += [k_spec(a.shape[2]), v_spec(a.shape[2])]
            far_operands += [a, a]
    acc1, st1, att_odd = pl.pallas_call(
        per_head(functools.partial(prev_kernel, per_dev, width, scale), 2, 7, 1, width, hb),
        out_shape=(
            state(half_rows),
            state(half_rows),
            jax.ShapeDtypeStruct((half_rows, heads * width), queries.dtype),
        ),
        grid_spec=pltpu.PrefetchScalarGridSpec(
            num_scalar_prefetch=2,
            grid=(heads // hb,),
            in_specs=[row_spec(rows), k_spec(rows), v_spec(rows), row_spec(rows), row_spec(rows)],
            out_specs=(row_spec(half_rows), row_spec(half_rows), out_spec(half_rows)),
        ),
        compiler_params=params,
        cost_estimate=cost(WINDOW // 2 + BLOCK, rows, heads * rows * width * (3 * 2 + 2 * 4 + 8)),
    )(meta, used, q_t, prev_kv, prev_kv, acc0, st0)

    n_head = lax.axis_size("head")
    if n_head != 2:
        att_even = pl.pallas_call(
            per_head(functools.partial(far_kernel, levels, per_dev, width, scale), 2, 0, 1, width, hb),
            out_shape=jax.ShapeDtypeStruct((half_rows, heads * width), queries.dtype),
            grid_spec=pltpu.PrefetchScalarGridSpec(
                num_scalar_prefetch=2,
                grid=(heads // hb,),
                in_specs=[even_q_spec, row_spec(half_rows), row_spec(half_rows)] + far_specs,
                out_specs=out_spec(half_rows),
            ),
            compiler_params=params,
            cost_estimate=cost(2 * BLOCK, half_rows, heads * width * (2 * rows + 8 * half_rows + 2 * sum(a.shape[2] for a in far_operands))),
        )(meta, used, q_pairs, acc1, st1, *far_operands)

        parts = []
        for att in (att_even, att_odd):
            partial_value = jnp.dot(att, out_weight, preferred_element_type=jnp.float32)
            parts.append(lax.psum_scatter(
                partial_value.astype(jnp.bfloat16), "head", scatter_dimension=1, tiled=True
            ))
    else:
        hidx = lax.axis_index("head")
        swap = [(0, 1), (1, 0)]
        received_odd = lax.ppermute(project_half(att_odd, out_weight, 1 - hidx), "head", swap)
        own_odd = project_half(att_odd, out_weight, hidx)
        acc1, st1, own_odd = lax.optimization_barrier((acc1, st1, own_odd))
        att_even = pl.pallas_call(
            per_head(functools.partial(far_kernel, levels, per_dev, width, scale), 2, 0, 1, width, hb),
            out_shape=jax.ShapeDtypeStruct((half_rows, heads * width), queries.dtype),
            grid_spec=pltpu.PrefetchScalarGridSpec(
                num_scalar_prefetch=2,
                grid=(heads // hb,),
                in_specs=[even_q_spec, row_spec(half_rows), row_spec(half_rows)] + far_specs,
                out_specs=out_spec(half_rows),
            ),
            compiler_params=params,
            cost_estimate=cost(2 * BLOCK, half_rows, heads * width * (2 * rows + 8 * half_rows + 2 * sum(a.shape[2] for a in far_operands))),
        )(meta, used, q_pairs, acc1, st1, *far_operands)

        received_even = jnp.concatenate(
            [
                lax.ppermute(project_half(att_even, out_weight, 1 - hidx, part=p, parts=2), "head", swap)
                for p in range(2)
            ],
            axis=1,
        )
        own_even = project_half(att_even, out_weight, hidx)
        parts = [
            (own.astype(jnp.float32) + got.astype(jnp.float32)).astype(jnp.bfloat16)
            for own, got in ((own_even, received_even), (own_odd, received_odd))
        ]
    even, odd = (p.reshape(per_dev // 2, BLOCK, -1) for p in parts)
    return jnp.stack([even, odd], axis=1).reshape(rows, -1)


def solution(mesh):
    placed = (
        P("ctx", "head", None),
        P("ctx", "head", None),
        P("ctx", "head", None),
        P(),
        P("head", None),
    )
    return jax.shard_map(
        per_device, mesh=mesh, in_specs=placed, out_specs=P("ctx", "head"), check_vma=False
    )
```

```python
import functools
import math

import jax
import jax.numpy as jnp
from jax import lax
from jax.experimental import pallas as pl
from jax.experimental.pallas import tpu as pltpu
from jax.sharding import PartitionSpec as P

BLOCK = 64
WINDOW = 512
NOFF = 5
HEADS_PER_STEP = 4


def from_behind(value, axis, steps):
    count = lax.axis_size(axis)
    initial, last = (max(0, -steps), min(count, count - steps))
    return lax.ppermute(value, axis, [(source, source + steps) for source in range(initial, last)])


def block_scores(q, keys, scale):
    return lax.dot_general(
        q, keys, (((1,), (1,)), ((), ())), preferred_element_type=jnp.float32
    ) * scale


def merge(pieces, m_old, l_old, acc_old):
    top = m_old
    for s, _ in pieces:
        row_max = s.max(axis=1, keepdims=True)
        top = row_max if top is None else jnp.maximum(top, row_max)
    total = None
    summed = None
    for s, v in pieces:
        p = jnp.exp(s - top)
        part_total = p.sum(axis=1, keepdims=True)
        part = jnp.dot(p.astype(jnp.bfloat16), v, preferred_element_type=jnp.float32)
        total = part_total if total is None else total + part_total
        summed = part if summed is None else summed + part
    if m_old is not None:
        alpha = jnp.exp(m_old - top)
        total = total + l_old * alpha
        summed = summed + acc_old * alpha
    return top, total, summed


def pack_stats(m, l, width):
    lane = lax.broadcasted_iota(jnp.int32, (m.shape[0], width), 1)
    return jnp.where(lane == 0, m, jnp.where(lane == 1, l, 0.0))


TILE = 256


class HeadView:
    def __init__(self, ref, head, width=None):
        self.ref, self.head, self.width = ref, head, width

    def _index(self, idx):
        if idx is Ellipsis:
            idx = (slice(None), slice(None))
        if self.width is None:
            return (self.head,) + tuple(idx)
        return (idx[0], pl.ds(self.head * self.width, self.width))

    @property
    def dtype(self):
        return self.ref.dtype

    def __getitem__(self, idx):
        return self.ref[self._index(idx)]

    def __setitem__(self, idx, value):
        self.ref[self._index(idx)] = value


def per_head(body, n_prefetch, n_head_major, n_rows_out, width, heads_per_step):
    def kernel(*refs):
        pre = refs[:n_prefetch]
        rest = refs[n_prefetch:]
        n_major = len(rest) - n_rows_out
        for hh in range(heads_per_step):
            views = [HeadView(r, hh) for r in rest[:n_major]]
            outs = [HeadView(r, hh, width) for r in rest[n_major:]]
            body(*pre, *views, *outs)

    return kernel


def own_kernel(per_dev, width, scale, q_ref, k_ref, v_ref, acc_ref, st_ref):
    neg = jnp.float32(-jnp.inf)
    rows = per_dev * BLOCK
    for lo in range(0, rows, TILE):
        q = q_ref[lo:lo + TILE, :]
        n_own = lo + TILE
        s_o = block_scores(q, k_ref[:n_own, :], scale)
        r_ids = lax.broadcasted_iota(jnp.int32, (TILE, n_own), 0)
        c_ids = lax.broadcasted_iota(jnp.int32, (TILE, n_own), 1)
        s_o = jnp.where(c_ids <= r_ids + lo, s_o, neg)
        m, l, acc = merge([(s_o, v_ref[:n_own, :])], None, None, None)
        acc_ref[lo:lo + TILE, :] = acc
        st_ref[lo:lo + TILE, :] = pack_stats(m, l, width)


def column_map(n_cols, values):
    seg = lax.broadcasted_iota(jnp.int32, (1, n_cols), 1) // BLOCK
    out = jnp.zeros((1, n_cols), jnp.int32)
    for j, value in enumerate(values):
        out = jnp.where(seg == j, value, out)
    return out


def prev_kernel(per_dev, width, scale, meta_ref, used_ref, q_ref, kp_ref, vp_ref, acc_ref, st_ref,
                acc_out, st_out, odd_ref):
    prev_ok = meta_ref[0] > 0
    neg = jnp.float32(-jnp.inf)
    rows = per_dev * BLOCK
    per_tile = TILE // BLOCK
    for lo in range(0, rows, TILE):
        q = q_ref[lo:lo + TILE, :]
        n_prev = rows - lo
        s_p = block_scores(q, kp_ref[lo:, :], scale)
        r_ids = lax.broadcasted_iota(jnp.int32, (TILE, n_prev), 0)
        c_ids = lax.broadcasted_iota(jnp.int32, (TILE, n_prev), 1)
        s_p = jnp.where((c_ids > r_ids) & prev_ok, s_p, neg)
        blocks = range(lo // BLOCK, lo // BLOCK + per_tile)
        starts = [pl.multiple_of(meta_ref[1 + i] * BLOCK, BLOCK) for i in blocks]
        k0 = jnp.concatenate([kp_ref[pl.ds(st, BLOCK), :] for st in starts], axis=0)
        v0 = jnp.concatenate([vp_ref[pl.ds(st, BLOCK), :] for st in starts], axis=0)
        s_f = block_scores(q, k0, scale)
        flags = column_map(TILE, [used_ref[i * NOFF] for i in blocks])
        r_blk = lax.broadcasted_iota(jnp.int32, (TILE, TILE), 0) // BLOCK
        c_blk = lax.broadcasted_iota(jnp.int32, (TILE, TILE), 1) // BLOCK
        s_f = jnp.where((r_blk == c_blk) & (flags > 0), s_f, neg)
        st = st_ref[lo:lo + TILE, :]
        m, l, acc = merge(
            [(s_p, vp_ref[lo:, :]), (s_f, v0)], st[:, 0:1], st[:, 1:2], acc_ref[lo:lo + TILE, :]
        )
        for b, i in enumerate(blocks):
            sl = slice(b * BLOCK, (b + 1) * BLOCK)
            half = (i // 2) * BLOCK
            if i % 2:
                odd_ref[half:half + BLOCK, :] = (acc[sl] / l[sl]).astype(odd_ref.dtype)
            else:
                acc_out[half:half + BLOCK, :] = acc[sl]
                st_out[half:half + BLOCK, :] = pack_stats(m[sl], l[sl], width)


def far_kernel(levels, per_dev, width, scale, meta_ref, used_ref, q_ref, acc_ref, st_ref, *rest):
    far_refs = rest[:-1]
    even_ref = rest[-1]
    neg = jnp.float32(-jnp.inf)
    n_even = per_dev // 2
    q = q_ref[...].reshape(n_even * BLOCK, -1)
    keys, vals, targets, flags = [], [], [], []
    pos = 0
    for level in levels:
        offset = 2**level
        n_src = 2 if level == 1 else 1
        refs = far_refs[pos:pos + 2 * n_src]
        pos += 2 * n_src
        k_lvl = refs[0][...]
        v_lvl = refs[1][...]
        if n_src == 2:
            odd = meta_ref[1 + per_dev] > 0
            k_lvl = jnp.where(odd, refs[2][...], k_lvl)
            v_lvl = jnp.where(odd, refs[3][...], v_lvl)
        keys.append(k_lvl)
        vals.append(v_lvl)
        for k in range(k_lvl.shape[0] // BLOCK):
            qblock = k * offset
            targets.append(qblock // 2)
            flags.append(used_ref[qblock * NOFF + level])
    k_far = jnp.concatenate(keys, axis=0)
    v_far = jnp.concatenate(vals, axis=0)
    n_keys = k_far.shape[0]
    s_f = block_scores(q, k_far, scale)
    col_target = column_map(n_keys, targets)
    col_flag = column_map(n_keys, flags)
    r_blk = lax.broadcasted_iota(jnp.int32, (n_even * BLOCK, n_keys), 0) // BLOCK
    s_f = jnp.where((r_blk == col_target) & (col_flag > 0), s_f, neg)
    st = st_ref[...]
    m, l, acc = merge([(s_f, v_far)], st[:, 0:1], st[:, 1:2], acc_ref[...])
    even_ref[...] = (acc / l).astype(even_ref.dtype)


def matmul_kernel(sel_ref, a_ref, w_ref, o_ref):
    o_ref[...] = jnp.dot(a_ref[...], w_ref[...], preferred_element_type=jnp.float32).astype(
        o_ref.dtype
    )


def project_half(attended, weight, half, tn=512, part=0, parts=1):
    rows, depth = attended.shape
    cw = weight.shape[1] // 2
    total_steps = cw // tn
    steps = total_steps // parts
    first = part * steps
    cw = steps * tn
    return pl.pallas_call(
        matmul_kernel,
        out_shape=jax.ShapeDtypeStruct((rows, cw), jnp.bfloat16),
        grid_spec=pltpu.PrefetchScalarGridSpec(
            num_scalar_prefetch=1,
            grid=(steps,),
            in_specs=[
                pl.BlockSpec((rows, depth), lambda j, sel: (0, 0)),
                pl.BlockSpec((depth, tn), lambda j, sel: (0, sel[0] * total_steps + first + j)),
            ],
            out_specs=pl.BlockSpec((rows, tn), lambda j, sel: (0, j)),
        ),
        compiler_params=pltpu.CompilerParams(dimension_semantics=("arbitrary",)),
        cost_estimate=pl.CostEstimate(
            flops=2 * rows * depth * cw,
            transcendentals=0,
            bytes_accessed=2 * (rows * depth + depth * cw + rows * cw),
        ),
    )(jnp.reshape(half, (1,)).astype(jnp.int32), attended, weight)


def pick_blocks(kv, local):
    return jnp.concatenate(
        [lax.dynamic_slice_in_dim(kv, local[b] * BLOCK, BLOCK, axis=2) for b in range(local.shape[0])],
        axis=2,
    )


def per_device(queries, keys, values, far_blocks, out_weight):
    rows, heads, width = queries.shape
    per_dev = rows // BLOCK
    device = lax.axis_index("ctx")
    cycle_size = lax.axis_size("ctx")
    scale = 1.0 / math.sqrt(width)
    q_t = jnp.transpose(queries, (1, 0, 2))
    kv_t = jnp.stack([jnp.transpose(keys, (1, 0, 2)), jnp.transpose(values, (1, 0, 2))])
    prev_kv = from_behind(kv_t, "ctx", 1)
    levels = []
    sends = []
    for level in range(1, NOFF):
        offset = 2**level
        if offset >= cycle_size:
            continue
        target = lax.dynamic_slice_in_dim(far_blocks, (device + offset) * per_dev, per_dev, 0)[
            ::offset, level
        ]
        local = jnp.clip(target - device * per_dev, 0, per_dev - 1)
        if level == 1:
            pairs = [(s, s + 2) for s in range(0, cycle_size - 2, 2)]
            nxt = lax.dynamic_slice_in_dim(far_blocks, (device + 1) * per_dev, per_dev, 0)[::2, 1]
            fwd_local = jnp.clip(nxt - (device - 1) * per_dev, 0, per_dev - 1)
        else:
            pairs = [(s, s + offset) for s in range(0, cycle_size - offset)]
        sends.append((pick_blocks(kv_t, local), pairs))
        levels.append(level)
    q_t, kv_t, *operands = lax.optimization_barrier((q_t, kv_t, *[op for op, _ in sends]))
    far_arrays = []
    for (_, pairs), op, level in zip(sends, operands, levels):
        if level == 1:
            far_arrays.append((op, pairs))
        else:
            far_arrays.append((lax.ppermute(op, "ctx", pairs),))

    own = lax.dynamic_slice_in_dim(far_blocks, device * per_dev, per_dev, 0)
    query_index = device * per_dev + jnp.arange(per_dev, dtype=jnp.int32)
    used = (own <= (query_index - WINDOW // BLOCK - 1)[:, None]).astype(jnp.int32).reshape(-1)
    pick = jnp.clip(own[:, 0] - (device - 1) * per_dev, 0, per_dev - 1)
    meta = jnp.concatenate(
        [(device > 0).astype(jnp.int32)[None], pick.astype(jnp.int32), (device % 2)[None]]
    )

    hb = math.gcd(heads, HEADS_PER_STEP)
    row_spec = lambda n: pl.BlockSpec((hb, n, width), lambda h, *_: (h, 0, 0))
    out_spec = lambda n: pl.BlockSpec((n, hb * width), lambda h, *_: (0, h))
    k_spec = lambda n: pl.BlockSpec((None, hb, n, width), lambda h, *_: (0, h, 0, 0))
    v_spec = lambda n: pl.BlockSpec((None, hb, n, width), lambda h, *_: (1, h, 0, 0))
    half_rows = rows // 2
    q_pairs = q_t.reshape(heads, per_dev // 2, 2, BLOCK, width)
    hc = math.gcd(heads, 2)
    even_q_spec = pl.BlockSpec((hc, per_dev // 2, None, BLOCK, width), lambda h, *_: (h, 0, 0, 0, 0))
    c_row = lambda n: pl.BlockSpec((hc, n, width), lambda h, *_: (h, 0, 0))
    c_out = lambda n: pl.BlockSpec((n, hc * width), lambda h, *_: (0, h))
    c_k = lambda n: pl.BlockSpec((None, hc, n, width), lambda h, *_: (0, h, 0, 0))
    c_v = lambda n: pl.BlockSpec((None, hc, n, width), lambda h, *_: (1, h, 0, 0))
    f32 = jnp.float32
    params = pltpu.CompilerParams(dimension_semantics=("arbitrary",))
    state = lambda n: jax.ShapeDtypeStruct((heads, n, width), f32)

    def cost(keys_per_row, n_rows, extra_bytes):
        return pl.CostEstimate(
            flops=4 * n_rows * heads * width * keys_per_row,
            transcendentals=n_rows * heads * keys_per_row,
            bytes_accessed=extra_bytes,
        )

    acc0, st0 = pl.pallas_call(
        per_head(functools.partial(own_kernel, per_dev, width, scale), 0, 5, 0, width, hb),
        out_shape=(state(rows), state(rows)),
        grid=(heads // hb,),
        in_specs=[row_spec(rows), k_spec(rows), v_spec(rows)],
        out_specs=(row_spec(rows), row_spec(rows)),
        compiler_params=params,
        cost_estimate=cost(WINDOW // 2, rows, 2 * heads * rows * width * (3 * 2 + 2 * 4)),
    )(q_t, kv_t, kv_t)

    if levels and levels[0] == 1:
        direct_op, direct_pairs = far_arrays[0]
        prev_kv, acc0, st0, direct_op = lax.optimization_barrier((prev_kv, acc0, st0, direct_op))
        direct = lax.ppermute(direct_op, "ctx", direct_pairs)
        forwarded = lax.ppermute(
            pick_blocks(prev_kv, fwd_local), "ctx",
            [(s, s + 1) for s in range(0, cycle_size - 1, 2)],
        )
        far_arrays[0] = (direct, forwarded)
    else:
        prev_kv, acc0, st0 = lax.optimization_barrier((prev_kv, acc0, st0))
    far_specs, far_operands = [], []
    for group in far_arrays:
        for a in group:
            far_specs += [c_k(a.shape[2]), c_v(a.shape[2])]
            far_operands += [a, a]
    acc1, st1, att_odd = pl.pallas_call(
        per_head(functools.partial(prev_kernel, per_dev, width, scale), 2, 7, 1, width, hb),
        out_shape=(
            state(half_rows),
            state(half_rows),
            jax.ShapeDtypeStruct((half_rows, heads * width), queries.dtype),
        ),
        grid_spec=pltpu.PrefetchScalarGridSpec(
            num_scalar_prefetch=2,
            grid=(heads // hb,),
            in_specs=[row_spec(rows), k_spec(rows), v_spec(rows), row_spec(rows), row_spec(rows)],
            out_specs=(row_spec(half_rows), row_spec(half_rows), out_spec(half_rows)),
        ),
        compiler_params=params,
        cost_estimate=cost(WINDOW // 2 + BLOCK, rows, heads * rows * width * (3 * 2 + 2 * 4 + 8)),
    )(meta, used, q_t, prev_kv, prev_kv, acc0, st0)

    n_head = lax.axis_size("head")
    if n_head != 2:
        att_even = pl.pallas_call(
            per_head(functools.partial(far_kernel, levels, per_dev, width, scale), 2, 0, 1, width, hc),
            out_shape=jax.ShapeDtypeStruct((half_rows, heads * width), queries.dtype),
            grid_spec=pltpu.PrefetchScalarGridSpec(
                num_scalar_prefetch=2,
                grid=(heads // hc,),
                in_specs=[even_q_spec, c_row(half_rows), c_row(half_rows)] + far_specs,
                out_specs=c_out(half_rows),
            ),
            compiler_params=params,
            cost_estimate=cost(2 * BLOCK, half_rows, heads * width * (2 * rows + 8 * half_rows + 2 * sum(a.shape[2] for a in far_operands))),
        )(meta, used, q_pairs, acc1, st1, *far_operands)

        parts = []
        for att in (att_even, att_odd):
            partial_value = jnp.dot(att, out_weight, preferred_element_type=jnp.float32)
            parts.append(lax.psum_scatter(
                partial_value.astype(jnp.bfloat16), "head", scatter_dimension=1, tiled=True
            ))
    else:
        hidx = lax.axis_index("head")
        swap = [(0, 1), (1, 0)]
        received_odd = lax.ppermute(project_half(att_odd, out_weight, 1 - hidx), "head", swap)
        own_odd = project_half(att_odd, out_weight, hidx)
        acc1, st1, own_odd = lax.optimization_barrier((acc1, st1, own_odd))
        att_even = pl.pallas_call(
            per_head(functools.partial(far_kernel, levels, per_dev, width, scale), 2, 0, 1, width, hc),
            out_shape=jax.ShapeDtypeStruct((half_rows, heads * width), queries.dtype),
            grid_spec=pltpu.PrefetchScalarGridSpec(
                num_scalar_prefetch=2,
                grid=(heads // hc,),
                in_specs=[even_q_spec, c_row(half_rows), c_row(half_rows)] + far_specs,
                out_specs=c_out(half_rows),
            ),
            compiler_params=params,
            cost_estimate=cost(2 * BLOCK, half_rows, heads * width * (2 * rows + 8 * half_rows + 2 * sum(a.shape[2] for a in far_operands))),
        )(meta, used, q_pairs, acc1, st1, *far_operands)

        received_even = jnp.concatenate(
            [
                lax.ppermute(project_half(att_even, out_weight, 1 - hidx, part=p, parts=2), "head", swap)
                for p in range(2)
            ],
            axis=1,
        )
        own_even = project_half(att_even, out_weight, hidx)
        parts = [
            (own.astype(jnp.float32) + got.astype(jnp.float32)).astype(jnp.bfloat16)
            for own, got in ((own_even, received_even), (own_odd, received_odd))
        ]
    even, odd = (p.reshape(per_dev // 2, BLOCK, -1) for p in parts)
    return jnp.stack([even, odd], axis=1).reshape(rows, -1)


def solution(mesh):
    placed = (
        P("ctx", "head", None),
        P("ctx", "head", None),
        P("ctx", "head", None),
        P(),
        P("head", None),
    )
    return jax.shard_map(
        per_device, mesh=mesh, in_specs=placed, out_specs=P("ctx", "head"), check_vma=False
    )
```

```python
import functools
import math

import jax
import jax.numpy as jnp
from jax import lax
from jax.experimental import pallas as pl
from jax.experimental.pallas import tpu as pltpu
from jax.sharding import PartitionSpec as P

BLOCK = 64
WINDOW = 512
NOFF = 5
HEADS_PER_STEP = 4


def from_behind(value, axis, steps):
    count = lax.axis_size(axis)
    initial, last = (max(0, -steps), min(count, count - steps))
    return lax.ppermute(value, axis, [(source, source + steps) for source in range(initial, last)])


def block_scores(q, keys, scale):
    return lax.dot_general(
        q, keys, (((1,), (1,)), ((), ())), preferred_element_type=jnp.float32
    ) * scale


def merge(pieces, m_old, l_old, acc_old):
    top = m_old
    for s, _ in pieces:
        row_max = s.max(axis=1, keepdims=True)
        top = row_max if top is None else jnp.maximum(top, row_max)
    total = None
    summed = None
    for s, v in pieces:
        p = jnp.exp(s - top)
        part_total = p.sum(axis=1, keepdims=True)
        part = jnp.dot(p.astype(jnp.bfloat16), v, preferred_element_type=jnp.float32)
        total = part_total if total is None else total + part_total
        summed = part if summed is None else summed + part
    if m_old is not None:
        alpha = jnp.exp(m_old - top)
        total = total + l_old * alpha
        summed = summed + acc_old * alpha
    return top, total, summed


def pack_stats(m, l, width):
    lane = lax.broadcasted_iota(jnp.int32, (m.shape[0], width), 1)
    return jnp.where(lane == 0, m, jnp.where(lane == 1, l, 0.0))


TILE = 256


class HeadView:
    def __init__(self, ref, head, width=None):
        self.ref, self.head, self.width = ref, head, width

    def _index(self, idx):
        if idx is Ellipsis:
            idx = (slice(None), slice(None))
        if self.width is None:
            return (self.head,) + tuple(idx)
        return (idx[0], pl.ds(self.head * self.width, self.width))

    @property
    def dtype(self):
        return self.ref.dtype

    def __getitem__(self, idx):
        return self.ref[self._index(idx)]

    def __setitem__(self, idx, value):
        self.ref[self._index(idx)] = value


def per_head(body, n_prefetch, n_head_major, n_rows_out, width, heads_per_step):
    def kernel(*refs):
        pre = refs[:n_prefetch]
        rest = refs[n_prefetch:]
        n_major = len(rest) - n_rows_out
        for hh in range(heads_per_step):
            views = [HeadView(r, hh) for r in rest[:n_major]]
            outs = [HeadView(r, hh, width) for r in rest[n_major:]]
            body(*pre, *views, *outs)

    return kernel


def own_kernel(per_dev, width, scale, q_ref, k_ref, v_ref, acc_ref, st_ref):
    neg = jnp.float32(-jnp.inf)
    rows = per_dev * BLOCK
    for lo in range(0, rows, TILE):
        q = q_ref[lo:lo + TILE, :]
        n_own = lo + TILE
        s_o = block_scores(q, k_ref[:n_own, :], scale)
        r_ids = lax.broadcasted_iota(jnp.int32, (TILE, n_own), 0)
        c_ids = lax.broadcasted_iota(jnp.int32, (TILE, n_own), 1)
        s_o = jnp.where(c_ids <= r_ids + lo, s_o, neg)
        m, l, acc = merge([(s_o, v_ref[:n_own, :])], None, None, None)
        acc_ref[lo:lo + TILE, :] = acc
        st_ref[lo:lo + TILE, :] = pack_stats(m, l, width)


def column_map(n_cols, values):
    seg = lax.broadcasted_iota(jnp.int32, (1, n_cols), 1) // BLOCK
    out = jnp.zeros((1, n_cols), jnp.int32)
    for j, value in enumerate(values):
        out = jnp.where(seg == j, value, out)
    return out


def prev_kernel(per_dev, width, scale, meta_ref, used_ref, q_ref, kp_ref, vp_ref, acc_ref, st_ref,
                acc_out, st_out, odd_ref):
    prev_ok = meta_ref[0] > 0
    neg = jnp.float32(-jnp.inf)
    rows = per_dev * BLOCK
    per_tile = TILE // BLOCK
    for lo in range(0, rows, TILE):
        q = q_ref[lo:lo + TILE, :]
        n_prev = rows - lo
        s_p = block_scores(q, kp_ref[lo:, :], scale)
        r_ids = lax.broadcasted_iota(jnp.int32, (TILE, n_prev), 0)
        c_ids = lax.broadcasted_iota(jnp.int32, (TILE, n_prev), 1)
        s_p = jnp.where((c_ids > r_ids) & prev_ok, s_p, neg)
        blocks = range(lo // BLOCK, lo // BLOCK + per_tile)
        starts = [pl.multiple_of(meta_ref[1 + i] * BLOCK, BLOCK) for i in blocks]
        k0 = jnp.concatenate([kp_ref[pl.ds(st, BLOCK), :] for st in starts], axis=0)
        v0 = jnp.concatenate([vp_ref[pl.ds(st, BLOCK), :] for st in starts], axis=0)
        s_f = block_scores(q, k0, scale)
        flags = column_map(TILE, [used_ref[i * NOFF] for i in blocks])
        r_blk = lax.broadcasted_iota(jnp.int32, (TILE, TILE), 0) // BLOCK
        c_blk = lax.broadcasted_iota(jnp.int32, (TILE, TILE), 1) // BLOCK
        s_f = jnp.where((r_blk == c_blk) & (flags > 0), s_f, neg)
        st = st_ref[lo:lo + TILE, :]
        m, l, acc = merge(
            [(s_p, vp_ref[lo:, :]), (s_f, v0)], st[:, 0:1], st[:, 1:2], acc_ref[lo:lo + TILE, :]
        )
        for b, i in enumerate(blocks):
            sl = slice(b * BLOCK, (b + 1) * BLOCK)
            half = (i // 2) * BLOCK
            if i % 2:
                odd_ref[half:half + BLOCK, :] = (acc[sl] / l[sl]).astype(odd_ref.dtype)
            else:
                acc_out[half:half + BLOCK, :] = acc[sl]
                st_out[half:half + BLOCK, :] = pack_stats(m[sl], l[sl], width)


def far_kernel(levels, per_dev, width, scale, meta_ref, used_ref, q_ref, acc_ref, st_ref, *rest):
    far_refs = rest[:-1]
    even_ref = rest[-1]
    neg = jnp.float32(-jnp.inf)
    n_even = per_dev // 2
    q = jnp.concatenate([q_ref[2 * e * BLOCK:(2 * e + 1) * BLOCK, :] for e in range(n_even)], axis=0)
    keys, vals, targets, flags = [], [], [], []
    pos = 0
    for level in levels:
        offset = 2**level
        n_src = 2 if level == 1 else 1
        refs = far_refs[pos:pos + 2 * n_src]
        pos += 2 * n_src
        k_lvl = refs[0][...]
        v_lvl = refs[1][...]
        if n_src == 2:
            odd = meta_ref[1 + per_dev] > 0
            k_lvl = jnp.where(odd, refs[2][...], k_lvl)
            v_lvl = jnp.where(odd, refs[3][...], v_lvl)
        keys.append(k_lvl)
        vals.append(v_lvl)
        for k in range(k_lvl.shape[0] // BLOCK):
            qblock = k * offset
            targets.append(qblock // 2)
            flags.append(used_ref[qblock * NOFF + level])
    k_far = jnp.concatenate(keys, axis=0)
    v_far = jnp.concatenate(vals, axis=0)
    n_keys = k_far.shape[0]
    s_f = block_scores(q, k_far, scale)
    col_target = column_map(n_keys, targets)
    col_flag = column_map(n_keys, flags)
    r_blk = lax.broadcasted_iota(jnp.int32, (n_even * BLOCK, n_keys), 0) // BLOCK
    s_f = jnp.where((r_blk == col_target) & (col_flag > 0), s_f, neg)
    st = st_ref[...]
    m, l, acc = merge([(s_f, v_far)], st[:, 0:1], st[:, 1:2], acc_ref[...])
    even_ref[...] = (acc / l).astype(even_ref.dtype)


def matmul_kernel(sel_ref, a_ref, w_ref, o_ref):
    o_ref[...] = jnp.dot(a_ref[...], w_ref[...], preferred_element_type=jnp.float32).astype(
        o_ref.dtype
    )


def project_half(attended, weight, half, tn=512, part=0, parts=1, span=None):
    rows, depth = attended.shape
    cw = weight.shape[1] // 2
    total_steps = cw // tn
    steps = total_steps // parts
    first = part * steps
    if span is not None:
        first, steps = span
    cw = steps * tn
    return pl.pallas_call(
        matmul_kernel,
        out_shape=jax.ShapeDtypeStruct((rows, cw), jnp.bfloat16),
        grid_spec=pltpu.PrefetchScalarGridSpec(
            num_scalar_prefetch=1,
            grid=(steps,),
            in_specs=[
                pl.BlockSpec((rows, depth), lambda j, sel: (0, 0)),
                pl.BlockSpec((depth, tn), lambda j, sel: (0, sel[0] * total_steps + first + j)),
            ],
            out_specs=pl.BlockSpec((rows, tn), lambda j, sel: (0, j)),
        ),
        compiler_params=pltpu.CompilerParams(dimension_semantics=("arbitrary",)),
        cost_estimate=pl.CostEstimate(
            flops=2 * rows * depth * cw,
            transcendentals=0,
            bytes_accessed=2 * (rows * depth + depth * cw + rows * cw),
        ),
    )(jnp.reshape(half, (1,)).astype(jnp.int32), attended, weight)


def pick_blocks(kv, local):
    return jnp.concatenate(
        [lax.dynamic_slice_in_dim(kv, local[b] * BLOCK, BLOCK, axis=2) for b in range(local.shape[0])],
        axis=2,
    )


def per_device(queries, keys, values, far_blocks, out_weight):
    rows, heads, width = queries.shape
    per_dev = rows // BLOCK
    device = lax.axis_index("ctx")
    cycle_size = lax.axis_size("ctx")
    scale = 1.0 / math.sqrt(width)
    q_t = jnp.transpose(queries, (1, 0, 2))
    kv_t = jnp.stack([jnp.transpose(keys, (1, 0, 2)), jnp.transpose(values, (1, 0, 2))])
    prev_kv = from_behind(kv_t, "ctx", 1)
    levels = []
    sends = []
    for level in range(1, NOFF):
        offset = 2**level
        if offset >= cycle_size:
            continue
        target = lax.dynamic_slice_in_dim(far_blocks, (device + offset) * per_dev, per_dev, 0)[
            ::offset, level
        ]
        local = jnp.clip(target - device * per_dev, 0, per_dev - 1)
        if level == 1:
            pairs = [(s, s + 2) for s in range(0, cycle_size - 2, 2)]
            nxt = lax.dynamic_slice_in_dim(far_blocks, (device + 1) * per_dev, per_dev, 0)[::2, 1]
            fwd_local = jnp.clip(nxt - (device - 1) * per_dev, 0, per_dev - 1)
        else:
            pairs = [(s, s + offset) for s in range(0, cycle_size - offset)]
        sends.append((pick_blocks(kv_t, local), pairs))
        levels.append(level)
    q_t, kv_t, *operands = lax.optimization_barrier((q_t, kv_t, *[op for op, _ in sends]))
    far_arrays = []
    for (_, pairs), op, level in zip(sends, operands, levels):
        if level == 1:
            far_arrays.append((op, pairs))
        else:
            far_arrays.append((lax.ppermute(op, "ctx", pairs),))

    own = lax.dynamic_slice_in_dim(far_blocks, device * per_dev, per_dev, 0)
    query_index = device * per_dev + jnp.arange(per_dev, dtype=jnp.int32)
    used = (own <= (query_index - WINDOW // BLOCK - 1)[:, None]).astype(jnp.int32).reshape(-1)
    pick = jnp.clip(own[:, 0] - (device - 1) * per_dev, 0, per_dev - 1)
    meta = jnp.concatenate(
        [(device > 0).astype(jnp.int32)[None], pick.astype(jnp.int32), (device % 2)[None]]
    )

    hb = math.gcd(heads, HEADS_PER_STEP)
    row_spec = lambda n: pl.BlockSpec((hb, n, width), lambda h, *_: (h, 0, 0))
    out_spec = lambda n: pl.BlockSpec((n, hb * width), lambda h, *_: (0, h))
    k_spec = lambda n: pl.BlockSpec((None, hb, n, width), lambda h, *_: (0, h, 0, 0))
    v_spec = lambda n: pl.BlockSpec((None, hb, n, width), lambda h, *_: (1, h, 0, 0))
    half_rows = rows // 2
    f32 = jnp.float32
    params = pltpu.CompilerParams(dimension_semantics=("arbitrary",))
    state = lambda n: jax.ShapeDtypeStruct((heads, n, width), f32)

    def cost(keys_per_row, n_rows, extra_bytes):
        return pl.CostEstimate(
            flops=4 * n_rows * heads * width * keys_per_row,
            transcendentals=n_rows * heads * keys_per_row,
            bytes_accessed=extra_bytes,
        )

    acc0, st0 = pl.pallas_call(
        per_head(functools.partial(own_kernel, per_dev, width, scale), 0, 5, 0, width, hb),
        out_shape=(state(rows), state(rows)),
        grid=(heads // hb,),
        in_specs=[row_spec(rows), k_spec(rows), v_spec(rows)],
        out_specs=(row_spec(rows), row_spec(rows)),
        compiler_params=params,
        cost_estimate=cost(WINDOW // 2, rows, 2 * heads * rows * width * (3 * 2 + 2 * 4)),
    )(q_t, kv_t, kv_t)

    if levels and levels[0] == 1:
        direct_op, direct_pairs = far_arrays[0]
        prev_kv, acc0, st0, direct_op = lax.optimization_barrier((prev_kv, acc0, st0, direct_op))
        direct = lax.ppermute(direct_op, "ctx", direct_pairs)
        forwarded = lax.ppermute(
            pick_blocks(prev_kv, fwd_local), "ctx",
            [(s, s + 1) for s in range(0, cycle_size - 1, 2)],
        )
        far_arrays[0] = (direct, forwarded)
    else:
        prev_kv, acc0, st0 = lax.optimization_barrier((prev_kv, acc0, st0))
    far_specs, far_operands = [], []
    for group in far_arrays:
        for a in group:
            far_specs += [k_spec(a.shape[2]), v_spec(a.shape[2])]
            far_operands += [a, a]
    acc1, st1, att_odd = pl.pallas_call(
        per_head(functools.partial(prev_kernel, per_dev, width, scale), 2, 7, 1, width, hb),
        out_shape=(
            state(half_rows),
            state(half_rows),
            jax.ShapeDtypeStruct((half_rows, heads * width), queries.dtype),
        ),
        grid_spec=pltpu.PrefetchScalarGridSpec(
            num_scalar_prefetch=2,
            grid=(heads // hb,),
            in_specs=[row_spec(rows), k_spec(rows), v_spec(rows), row_spec(rows), row_spec(rows)],
            out_specs=(row_spec(half_rows), row_spec(half_rows), out_spec(half_rows)),
        ),
        compiler_params=params,
        cost_estimate=cost(WINDOW // 2 + BLOCK, rows, heads * rows * width * (3 * 2 + 2 * 4 + 8)),
    )(meta, used, q_t, prev_kv, prev_kv, acc0, st0)

    n_head = lax.axis_size("head")
    if n_head != 2:
        att_even = pl.pallas_call(
            per_head(functools.partial(far_kernel, levels, per_dev, width, scale), 2, 0, 1, width, hb),
            out_shape=jax.ShapeDtypeStruct((half_rows, heads * width), queries.dtype),
            grid_spec=pltpu.PrefetchScalarGridSpec(
                num_scalar_prefetch=2,
                grid=(heads // hb,),
                in_specs=[row_spec(rows), row_spec(half_rows), row_spec(half_rows)] + far_specs,
                out_specs=out_spec(half_rows),
            ),
            compiler_params=params,
            cost_estimate=cost(2 * BLOCK, half_rows, heads * width * (2 * rows + 8 * half_rows + 2 * sum(a.shape[2] for a in far_operands))),
        )(meta, used, q_t, acc1, st1, *far_operands)

        parts = []
        for att in (att_even, att_odd):
            partial_value = jnp.dot(att, out_weight, preferred_element_type=jnp.float32)
            parts.append(lax.psum_scatter(
                partial_value.astype(jnp.bfloat16), "head", scatter_dimension=1, tiled=True
            ))
    else:
        hidx = lax.axis_index("head")
        swap = [(0, 1), (1, 0)]
        received_odd = lax.ppermute(project_half(att_odd, out_weight, 1 - hidx), "head", swap)
        own_odd = project_half(att_odd, out_weight, hidx)
        acc1, st1, own_odd = lax.optimization_barrier((acc1, st1, own_odd))
        att_even = pl.pallas_call(
            per_head(functools.partial(far_kernel, levels, per_dev, width, scale), 2, 0, 1, width, hb),
            out_shape=jax.ShapeDtypeStruct((half_rows, heads * width), queries.dtype),
            grid_spec=pltpu.PrefetchScalarGridSpec(
                num_scalar_prefetch=2,
                grid=(heads // hb,),
                in_specs=[row_spec(rows), row_spec(half_rows), row_spec(half_rows)] + far_specs,
                out_specs=out_spec(half_rows),
            ),
            compiler_params=params,
            cost_estimate=cost(2 * BLOCK, half_rows, heads * width * (2 * rows + 8 * half_rows + 2 * sum(a.shape[2] for a in far_operands))),
        )(meta, used, q_t, acc1, st1, *far_operands)

        received_even = jnp.concatenate(
            [
                lax.ppermute(project_half(att_even, out_weight, 1 - hidx, span=span), "head", swap)
                for span in ((0, 1), (1, out_weight.shape[1] // 2 // 512 - 1))
            ],
            axis=1,
        )
        own_even = project_half(att_even, out_weight, hidx)
        parts = [
            (own.astype(jnp.float32) + got.astype(jnp.float32)).astype(jnp.bfloat16)
            for own, got in ((own_even, received_even), (own_odd, received_odd))
        ]
    even, odd = (p.reshape(per_dev // 2, BLOCK, -1) for p in parts)
    return jnp.stack([even, odd], axis=1).reshape(rows, -1)


def solution(mesh):
    placed = (
        P("ctx", "head", None),
        P("ctx", "head", None),
        P("ctx", "head", None),
        P(),
        P("head", None),
    )
    return jax.shard_map(
        per_device, mesh=mesh, in_specs=placed, out_specs=P("ctx", "head"), check_vma=False
    )
```
